32 devices in a mesh: groups: 2 (over y), dp: 4 (over z), tensor: 4 (over x, core).
Axes of the slice: x: 2, y: 2, z: 4, core: 2. Of those that a mesh axis runs over, the one named last changes fastest.
Arguments:
- kv_cache: bfloat16 [256, 128, 2048], P(('groups', 'dp'), None, 'tensor'), parts along dimension 0
- lengths: int32 [256], P(('groups', 'dp')), parts along dimension 0, may hold values from 1 to 128, as said below
- source: int32 [256], P(('groups', 'dp')), parts along dimension 0, may hold values from 0 to 127, as said below
- queries: bfloat16 [256, 16, 2048], P(('groups', 'dp'), None, 'tensor'), parts along dimension 0, may hold values from -6 to 6
- fresh_kv: bfloat16 [256, 16, 2048], P(('groups', 'dp'), None, 'tensor'), parts along dimension 0, may hold values from -6 to 6
- out_weight: bfloat16 [2048, 4608], P('tensor')
- norm_gain: float32 [4608], P('tensor'), may hold values from 0.5 to 1.5
Outputs:
- normed: bfloat16 [256, 16, 4608], P(('groups', 'dp'), None, 'tensor'), parts along dimension 0
The draws below stay inside these ranges and needn't reach their ends.
There are 2 independent parts, one for each index of `groups`. The reference program is written for one: setup_inputs(seed, part) draws one part's arguments, and reference() takes and returns one part's arrays. A program takes and returns all parts, laid end to end along the dimension named above; an argument that names none is the same for every part. Nothing has to cross between parts.
Inputs may be any that keep to these rules, and one draw needn't show every extreme that they name: `source`: A permutation of the slots. A session may stay on its device or move to another; at most 8 sessions go from one device to any one device, and some device sends 8 to one device. Every device receives 32 sessions, one from each old slot number. `lengths`: some session has 128 cached tokens.
All inputs are finite; a program needn't handle non-finite values.
Results may differ from the reference program's by a relative error of at most 0.018.
Values may be sent and summed in bfloat16 or wider, within the bound.
No kernel may reach another device: no remote copies, remote signals or barrier semaphores. Data moves between devices by JAX's collectives and lax.ppermute only.
A program may use at most 64 MiB of HBM per device.

```python
import jax
import jax.numpy as jnp
from jax import lax

D = 4608
HEAD = 128
QHEADS = 16
KVHEADS = 8
S_DEV = 32
CACHE_LEN = 128
BLOCK_ROWS = 16
SESSIONS = 128
N_TENSOR = 4


def draw_source(key, part):
    dp_count = SESSIONS // S_DEV
    key_place, key_offset, key_slots = jax.random.split(jax.random.fold_in(key, 11), 3)
    placing = jax.random.permutation(key_place, dp_count).astype(jnp.int32)
    offsets = jax.random.permutation(key_offset, dp_count).astype(jnp.int32)[jnp.arange(S_DEV) % dp_count]
    new_home = (placing[:, None] + offsets[None, :]) % dp_count
    orders = jax.vmap(lambda sub_key: jax.random.permutation(sub_key, S_DEV))(jax.random.split(key_slots, dp_count)).astype(jnp.int32)
    slot_ids = jnp.arange(S_DEV, dtype=jnp.int32)
    new_slot = orders[new_home, slot_ids[None, :]]
    new_global = (new_home * S_DEV + new_slot).reshape(-1)
    old_global = jnp.arange(SESSIONS, dtype=jnp.int32)
    return jnp.zeros((SESSIONS,), jnp.int32).at[new_global].set(old_global)


def draw_lengths(key, part):
    dp_count = SESSIONS // S_DEV
    key_heavy, key_value, key_spot = jax.random.split(jax.random.fold_in(key, 23), 3)
    heavy_dev = jax.random.randint(key_heavy, (dp_count, 1), 0, 2)
    lowest = jnp.where(heavy_dev == 1, CACHE_LEN // 2, 1)
    highest = jnp.where(heavy_dev == 1, CACHE_LEN, max(CACHE_LEN // 4, 1))
    spread = jax.random.randint(key_value, (dp_count, S_DEV), 0, 1 << 20)
    drawn = (lowest + spread % (highest - lowest + 1)).reshape(-1)
    full_spot = jax.random.randint(key_spot, (), 0, SESSIONS)
    return jnp.where(jnp.arange(SESSIONS) == full_spot, CACHE_LEN, drawn).astype(jnp.int32)


def base_values(key, shape):
    return jax.random.truncated_normal(key, -6.0, 6.0, shape, jnp.float32)


def draw_out_weight(key, part):
    row_total = QHEADS * HEAD
    row_block = row_total // 8
    col_block = D // 8
    key_base, key_grid, key_cols = jax.random.split(jax.random.fold_in(key, 37), 3)
    base = base_values(key_base, (row_total, D))
    grid_log = jax.random.uniform(key_grid, (8, 8), jnp.float32, -1.2, 1.2)
    column_log = jax.random.uniform(key_cols, (1, 8), jnp.float32, -0.7, 0.7)
    block_scale = jnp.exp(grid_log + column_log)
    block_scale = jnp.repeat(jnp.repeat(block_scale, row_block, axis=0), col_block, axis=1)
    return (base * block_scale * (0.57 * row_total ** (-0.5))).astype(jnp.bfloat16)


def draw_kv_cache(key, part):
    key_base, key_scale = jax.random.split(jax.random.fold_in(key, 41), 2)
    base = base_values(key_base, (SESSIONS, CACHE_LEN, KVHEADS, 2, HEAD))
    value_log = jax.random.uniform(key_scale, (SESSIONS, 1, KVHEADS, 1, 1), jnp.float32, -1.2, 1.2)
    key_part = jnp.ones((SESSIONS, 1, KVHEADS, 1, 1), jnp.float32)
    half_scale = jnp.concatenate([key_part, jnp.exp(value_log)], axis=3)
    scaled = base * half_scale
    return scaled.reshape(SESSIONS, CACHE_LEN, KVHEADS * 2 * HEAD).astype(jnp.bfloat16)


def levels(stream_key, dims, pieces, least, high):
    def one(axis_at, parts):
        heights = jax.random.uniform(jax.random.fold_in(jax.random.fold_in(stream_key, 6), axis_at), (parts,), jnp.float32, least / len(pieces), high / len(pieces))
        return jnp.repeat(jnp.exp(heights), dims[axis_at] // parts).reshape((-1,) + (1,) * (len(dims) - axis_at - 1))

    loudness = one(*pieces[0])
    for cut in pieces[1:]:
        loudness = loudness * one(*cut)
    return loudness


def noise(own_key, dims, width, most, cuts=(), held_as=jnp.bfloat16):
    entries = width * jax.random.normal(own_key, dims, jnp.float32)
    if cuts:
        entries = entries * levels(own_key, dims, cuts, -0.22, 0.18)
    return jnp.clip(entries, -most, most).astype(held_as)


def setup_inputs(seed: int = 0, part: int = 0) -> dict:
    arg_keys = jax.random.split(jax.random.key(seed), 8)
    own_keys = jax.random.split(jax.random.fold_in(arg_keys[7], part), 8)
    kv_cache = draw_kv_cache(jax.random.fold_in(jax.random.fold_in(arg_keys[7], part), 71), part)
    lengths = draw_lengths(jax.random.fold_in(jax.random.fold_in(arg_keys[7], part), 71), part)
    source = draw_source(jax.random.fold_in(jax.random.fold_in(arg_keys[7], part), 71), part)
    queries = noise(own_keys[3], (SESSIONS, BLOCK_ROWS, QHEADS * HEAD), 1.0, 6.0, ((0, 4), (2, 4)))
    fresh_kv = noise(own_keys[4], (SESSIONS, BLOCK_ROWS, KVHEADS * 2 * HEAD), 1.0, 6.0, ((0, 4), (2, 4)))
    out_weight = draw_out_weight(jax.random.fold_in(arg_keys[7], 71), part)
    norm_gain = jnp.clip(1.0 + 0.1 * jax.random.normal(arg_keys[6], (D,), jnp.float32), 0.5, 1.5)
    return {"kv_cache": kv_cache, "lengths": lengths, "source": source, "queries": queries, "fresh_kv": fresh_kv, "out_weight": out_weight, "norm_gain": norm_gain}


score_scale = 144.0 ** (-0.5)
soft_cap = 50.0
norm_eps = 1e-06

def rounded_copy(values):
    return lax.optimization_barrier(values.astype(jnp.bfloat16)).astype(jnp.float32)

def attend_slot(queries, cached, length, fresh_kv):
    cache_length = cached.shape[0]
    row_count = queries.shape[0]
    group_size = QHEADS // KVHEADS
    key_values = jnp.concatenate([cached, fresh_kv], axis=0).astype(jnp.float32)
    key_values = key_values.reshape(cache_length + row_count, KVHEADS, 2, HEAD)
    key_rows = key_values[:, :, 0]
    value_rows = key_values[:, :, 1]
    grouped = queries.astype(jnp.float32).reshape(row_count, KVHEADS, group_size, HEAD)
    scores = jnp.einsum('rkgh,jkh->kgrj', grouped, key_rows) * score_scale
    capped = soft_cap * jnp.tanh(scores / soft_cap)
    position = jnp.arange(cache_length + row_count, dtype=jnp.int32)
    row_position = jnp.arange(row_count, dtype=jnp.int32)
    in_cache = position[None, :] < length
    in_block = (position[None, :] >= cache_length) & (position[None, :] - cache_length <= row_position[:, None])
    visible = in_cache | in_block
    weights = jnp.where(visible[None, None], jnp.exp(capped), 0.0)
    soft_weights = rounded_copy(weights / lax.optimization_barrier(jnp.sum(weights, axis=-1, keepdims=True)))
    attended = jnp.einsum('kgrj,jkh->rkgh', soft_weights, value_rows)
    return attended.reshape(row_count, QHEADS * HEAD).astype(jnp.bfloat16)

def reference(kv_cache, lengths, source, queries, fresh_kv, out_weight, norm_gain):

    def per_slot(session_index):
        anchor = source[session_index]
        return attend_slot(queries[session_index], kv_cache[anchor], lengths[anchor], fresh_kv[session_index])
    attended = lax.map(per_slot, jnp.arange(SESSIONS, dtype=jnp.int32))
    flat_rows = attended.reshape(SESSIONS * BLOCK_ROWS, QHEADS * HEAD)
    head_cols = QHEADS * HEAD // N_TENSOR
    branch = jnp.zeros((flat_rows.shape[0], D), jnp.float32)
    for shard_index in range(N_TENSOR):
        partial_value = jnp.dot(flat_rows[:, shard_index * head_cols:(shard_index + 1) * head_cols], out_weight[shard_index * head_cols:(shard_index + 1) * head_cols], preferred_element_type=jnp.float32)
        branch = branch + rounded_copy(partial_value)
    mean_square = lax.optimization_barrier(jnp.mean(branch * branch, axis=-1, keepdims=True))
    normed = branch * lax.rsqrt(mean_square + norm_eps) * norm_gain
    return normed.astype(jnp.bfloat16).reshape(SESSIONS, BLOCK_ROWS, D)
```

```python
import jax
import jax.numpy as jnp
from jax import lax
from jax.sharding import PartitionSpec as P

HEAD = 128
QHEADS = 16
KVHEADS = 8
TAG_WIDTH = 128


score_scale = 144.0 ** (-0.5)
soft_cap = 50.0
norm_eps = 1e-06


def attend(queries, cached, lengths, fresh_kv):
    slot_count, row_count, query_width = queries.shape
    cache_length = cached.shape[1]
    group_size = QHEADS // KVHEADS
    kv_heads = cached.shape[2] // (2 * HEAD)
    key_values = jnp.concatenate([cached, fresh_kv], axis=1)
    key_values = key_values.reshape(slot_count, cache_length + row_count, kv_heads, 2, HEAD)
    key_rows = key_values[:, :, :, 0]
    value_rows = key_values[:, :, :, 1]
    grouped = queries.reshape(slot_count, row_count, kv_heads, group_size, HEAD)
    scores = (
        jnp.einsum("srkgh,sjkh->skgrj", grouped, key_rows, preferred_element_type=jnp.float32)
        * score_scale
    )
    capped = soft_cap * jnp.tanh(scores / soft_cap)
    position = jnp.arange(cache_length + row_count, dtype=jnp.int32)
    row_position = jnp.arange(row_count, dtype=jnp.int32)
    in_cache = position[None, None, :] < lengths[:, None, None]
    in_block = (position[None, :] >= cache_length) & (
        position[None, :] - cache_length <= row_position[:, None]
    )
    visible = in_cache | in_block[None]
    weights = jnp.where(visible[:, None, None], jnp.exp(capped), 0.0)
    soft_weights = (weights / jnp.sum(weights, axis=-1, keepdims=True)).astype(jnp.bfloat16)
    attended = jnp.einsum(
        "skgrj,sjkh->srkgh", soft_weights, value_rows, preferred_element_type=jnp.float32
    )
    return attended.reshape(slot_count, row_count, query_width).astype(jnp.bfloat16)


def pack_lanes(payload, slot_lanes, lane_count):
    lane_ids = jnp.arange(lane_count, dtype=jnp.int32)
    slot_ids = jnp.arange(payload.shape[0], dtype=jnp.int32)
    lane_hits = slot_lanes[None, :] == lane_ids[:, None]
    filled = jnp.any(lane_hits, axis=1)
    chosen = jnp.sum(jnp.where(lane_hits, slot_ids[None, :], 0), axis=1)
    picked = jnp.take(payload, chosen, axis=0)
    return jnp.where(filled[:, None, None], picked, jnp.zeros((), payload.dtype))


def shards(kv_cache, lengths, source, queries, fresh_kv, out_weight, norm_gain):
    dp_count = lax.axis_size("dp")
    slot_count, row_count, query_width = queries.shape
    kv_width = fresh_kv.shape[2]
    pair_cap = max(1, slot_count // dp_count)
    lane_count = dp_count * pair_cap
    slot_ids = jnp.arange(slot_count, dtype=jnp.int32)
    lane_ids = jnp.arange(lane_count, dtype=jnp.int32)

    old_home = source // slot_count
    old_slot = source % slot_count
    earlier = slot_ids[None, :] < slot_ids[:, None]
    same_home = old_home[:, None] == old_home[None, :]
    rank = jnp.sum(same_home & earlier, axis=1)
    out_lane = old_home * pair_cap + rank
    tag = jnp.broadcast_to(
        (old_slot + 1).astype(jnp.bfloat16)[:, None, None], (slot_count, row_count, TAG_WIDTH)
    )
    payload = jnp.concatenate([queries, fresh_kv, tag], axis=2)
    sending = pack_lanes(payload, out_lane, lane_count)
    arrived = lax.all_to_all(sending, "dp", 0, 0, tiled=True)

    lane_slot = arrived[:, 0, query_width + kv_width].astype(jnp.int32) - 1
    hits = lane_slot[None, :] == slot_ids[:, None]
    slot_lane = jnp.sum(jnp.where(hits, lane_ids[None, :], 0), axis=1)
    gathered = jnp.take(arrived, slot_lane, axis=0)
    local_q = gathered[:, :, :query_width]
    local_fresh = gathered[:, :, query_width:query_width + kv_width]
    attended = attend(local_q, kv_cache, lengths, local_fresh)

    filled = lane_slot >= 0
    back = jnp.take(attended, jnp.maximum(lane_slot, 0), axis=0)
    back = jnp.where(filled[:, None, None], back, jnp.zeros((), back.dtype))
    returned = lax.all_to_all(back, "dp", 0, 0, tiled=True)
    attended_here = jnp.take(returned, out_lane, axis=0)

    row_total = slot_count * row_count
    flat_rows = attended_here.reshape(row_total, query_width)
    partial_value = jnp.dot(flat_rows, out_weight, preferred_element_type=jnp.float32)
    model_width = out_weight.shape[1]
    own_part = lax.psum_scatter(
        partial_value.astype(jnp.bfloat16), "tensor", scatter_dimension=1, tiled=True
    ).astype(jnp.float32)
    square_sum = lax.psum(jnp.sum(own_part * own_part, axis=-1, keepdims=True), "tensor")
    mean_square = square_sum / model_width
    normed = own_part * lax.rsqrt(mean_square + norm_eps) * norm_gain
    return normed.astype(jnp.bfloat16).reshape(slot_count, row_count, own_part.shape[1])


def solution(mesh):
    placed = (
        P(("groups", "dp"), None, "tensor"),
        P(("groups", "dp")),
        P(("groups", "dp")),
        P(("groups", "dp"), None, "tensor"),
        P(("groups", "dp"), None, "tensor"),
        P("tensor", None),
        P("tensor"),
    )
    return jax.shard_map(
        shards,
        mesh=mesh,
        in_specs=placed,
        out_specs=P(("groups", "dp"), None, "tensor"),
        check_vma=False,
    )
```

```python
import functools

import jax
import jax.numpy as jnp
from jax import lax
from jax.experimental import pallas as pl
from jax.sharding import PartitionSpec as P

HEAD = 128
QHEADS = 16
KVHEADS = 8
TAG_WIDTH = 128


score_scale = 144.0 ** (-0.5)
soft_cap = 50.0
norm_eps = 1e-06


def attention_kernel(length_ref, pay_ref, cache_ref, out_ref, *, q_width):
    sessions, cache_length, _ = cache_ref.shape
    row_count = pay_ref.shape[1]
    kv_heads = cache_ref.shape[2] // (2 * HEAD)
    group_size = QHEADS // KVHEADS
    lengths = length_ref[...]
    cache_pos = lax.broadcasted_iota(jnp.int32, (sessions, group_size * row_count, cache_length), 2)
    cache_seen = cache_pos < lengths
    fresh_pos = lax.broadcasted_iota(jnp.int32, (sessions, group_size * row_count, row_count), 2)
    query_row = lax.broadcasted_iota(jnp.int32, (sessions, group_size * row_count, row_count), 1) % row_count
    fresh_seen = fresh_pos <= query_row
    for k in range(kv_heads):
        key_col = 2 * HEAD * k
        grouped = jnp.concatenate(
            [pay_ref[:, :, (group_size * k + g) * HEAD:(group_size * k + g + 1) * HEAD] for g in range(group_size)],
            axis=1,
        )
        cache_keys = cache_ref[:, :, key_col:key_col + HEAD]
        cache_values = cache_ref[:, :, key_col + HEAD:key_col + 2 * HEAD]
        fresh_keys = pay_ref[:, :, q_width + key_col:q_width + key_col + HEAD]
        fresh_values = pay_ref[:, :, q_width + key_col + HEAD:q_width + key_col + 2 * HEAD]
        cache_scores = jnp.einsum("bqd,bkd->bqk", grouped, cache_keys, preferred_element_type=jnp.float32) * score_scale
        fresh_scores = jnp.einsum("bqd,bkd->bqk", grouped, fresh_keys, preferred_element_type=jnp.float32) * score_scale
        cache_w = jnp.where(cache_seen, jnp.exp(soft_cap * jnp.tanh(cache_scores / soft_cap)), 0.0)
        fresh_w = jnp.where(fresh_seen, jnp.exp(soft_cap * jnp.tanh(fresh_scores / soft_cap)), 0.0)
        total = jnp.sum(cache_w, axis=-1, keepdims=True) + jnp.sum(fresh_w, axis=-1, keepdims=True)
        cache_p = (cache_w / total).astype(jnp.bfloat16)
        fresh_p = (fresh_w / total).astype(jnp.bfloat16)
        mixed = jnp.einsum("bqk,bkd->bqd", cache_p, cache_values, preferred_element_type=jnp.float32)
        mixed = mixed + jnp.einsum("bqk,bkd->bqd", fresh_p, fresh_values, preferred_element_type=jnp.float32)
        mixed = mixed.astype(out_ref.dtype)
        for g in range(group_size):
            col = (group_size * k + g) * HEAD
            out_ref[:, :, col:col + HEAD] = mixed[:, g * row_count:(g + 1) * row_count]


def attend_kernel(payload, cached, lengths, q_width, block=8):
    slot_count, row_count, _ = payload.shape
    cache_length, kv_width = cached.shape[1], cached.shape[2]
    block = min(block, slot_count)
    length_col = lengths.reshape(slot_count, 1, 1)
    return pl.pallas_call(
        functools.partial(attention_kernel, q_width=q_width),
        out_shape=jax.ShapeDtypeStruct((slot_count, row_count, q_width), jnp.bfloat16),
        grid=(slot_count // block,),
        in_specs=[
            pl.BlockSpec((block, 1, 1), lambda b: (b, 0, 0)),
            pl.BlockSpec((block, row_count, payload.shape[2]), lambda b: (b, 0, 0)),
            pl.BlockSpec((block, cache_length, kv_width), lambda b: (b, 0, 0)),
        ],
        out_specs=pl.BlockSpec((block, row_count, q_width), lambda b: (b, 0, 0)),
        cost_estimate=pl.CostEstimate(
            flops=4 * slot_count * (q_width // HEAD) * row_count * (cache_length + row_count) * HEAD,
            transcendentals=2 * slot_count * (q_width // HEAD) * row_count * (cache_length + row_count),
            bytes_accessed=int(cached.size * 2 + payload.size * 2 + slot_count * row_count * q_width * 2),
        ),
    )(length_col, payload, cached)


def pack_lanes(payload, slot_lanes, lane_count):
    lane_ids = jnp.arange(lane_count, dtype=jnp.int32)
    slot_ids = jnp.arange(payload.shape[0], dtype=jnp.int32)
    lane_hits = slot_lanes[None, :] == lane_ids[:, None]
    filled = jnp.any(lane_hits, axis=1)
    chosen = jnp.sum(jnp.where(lane_hits, slot_ids[None, :], 0), axis=1)
    picked = jnp.take(payload, chosen, axis=0)
    return jnp.where(filled[:, None, None], picked, jnp.zeros((), payload.dtype))


def shards(kv_cache, lengths, source, queries, fresh_kv, out_weight, norm_gain):
    dp_count = lax.axis_size("dp")
    slot_count, row_count, query_width = queries.shape
    kv_width = fresh_kv.shape[2]
    pair_cap = max(1, slot_count // dp_count)
    lane_count = dp_count * pair_cap
    slot_ids = jnp.arange(slot_count, dtype=jnp.int32)
    lane_ids = jnp.arange(lane_count, dtype=jnp.int32)

    old_home = source // slot_count
    old_slot = source % slot_count
    earlier = slot_ids[None, :] < slot_ids[:, None]
    same_home = old_home[:, None] == old_home[None, :]
    rank = jnp.sum(same_home & earlier, axis=1)
    out_lane = old_home * pair_cap + rank
    tag = jnp.broadcast_to(
        (old_slot + 1).astype(jnp.bfloat16)[:, None, None], (slot_count, row_count, TAG_WIDTH)
    )
    payload = jnp.concatenate([queries, fresh_kv, tag], axis=2)
    sending = pack_lanes(payload, out_lane, lane_count)
    arrived = lax.all_to_all(sending, "dp", 0, 0, tiled=True)

    lane_slot = arrived[:, 0, query_width + kv_width].astype(jnp.int32) - 1
    hits = lane_slot[None, :] == slot_ids[:, None]
    slot_lane = jnp.sum(jnp.where(hits, lane_ids[None, :], 0), axis=1)
    gathered = jnp.take(arrived, slot_lane, axis=0)
    attended = attend_kernel(gathered, kv_cache, lengths, query_width)

    filled = lane_slot >= 0
    back = jnp.take(attended, jnp.maximum(lane_slot, 0), axis=0)
    back = jnp.where(filled[:, None, None], back, jnp.zeros((), back.dtype))
    returned = lax.all_to_all(back, "dp", 0, 0, tiled=True)
    attended_here = jnp.take(returned, out_lane, axis=0)

    row_total = slot_count * row_count
    flat_rows = attended_here.reshape(row_total, query_width)
    partial_value = jnp.dot(flat_rows, out_weight, preferred_element_type=jnp.float32)
    model_width = out_weight.shape[1]
    own_part = lax.psum_scatter(
        partial_value.astype(jnp.bfloat16), "tensor", scatter_dimension=1, tiled=True
    ).astype(jnp.float32)
    square_sum = lax.psum(jnp.sum(own_part * own_part, axis=-1, keepdims=True), "tensor")
    mean_square = square_sum / model_width
    normed = own_part * lax.rsqrt(mean_square + norm_eps) * norm_gain
    return normed.astype(jnp.bfloat16).reshape(slot_count, row_count, own_part.shape[1])


def solution(mesh):
    placed = (
        P(("groups", "dp"), None, "tensor"),
        P(("groups", "dp")),
        P(("groups", "dp")),
        P(("groups", "dp"), None, "tensor"),
        P(("groups", "dp"), None, "tensor"),
        P("tensor", None),
        P("tensor"),
    )
    return jax.shard_map(
        shards,
        mesh=mesh,
        in_specs=placed,
        out_specs=P(("groups", "dp"), None, "tensor"),
        check_vma=False,
    )
```

```python
import functools

import jax
import jax.numpy as jnp
from jax import lax
from jax.experimental import pallas as pl
from jax.sharding import PartitionSpec as P

HEAD = 128
QHEADS = 16
KVHEADS = 8
TAG_WIDTH = 128


score_scale = 144.0 ** (-0.5)
soft_cap = 50.0
norm_eps = 1e-06


def attention_kernel(length_ref, pay_ref, cache_ref, out_ref, *, q_width):
    sessions, cache_length, _ = cache_ref.shape
    row_count = pay_ref.shape[1]
    kv_heads = cache_ref.shape[2] // (2 * HEAD)
    group_size = QHEADS // KVHEADS
    lengths = length_ref[...]
    cache_pos = lax.broadcasted_iota(jnp.int32, (sessions, group_size * row_count, cache_length), 2)
    cache_seen = cache_pos < lengths
    fresh_pos = lax.broadcasted_iota(jnp.int32, (sessions, group_size * row_count, row_count), 2)
    query_row = lax.broadcasted_iota(jnp.int32, (sessions, group_size * row_count, row_count), 1) % row_count
    fresh_seen = fresh_pos <= query_row
    for k in range(kv_heads):
        key_col = 2 * HEAD * k
        grouped = jnp.concatenate(
            [pay_ref[:, :, (group_size * k + g) * HEAD:(group_size * k + g + 1) * HEAD] for g in range(group_size)],
            axis=1,
        )
        cache_keys = cache_ref[:, :, key_col:key_col + HEAD]
        cache_values = cache_ref[:, :, key_col + HEAD:key_col + 2 * HEAD]
        fresh_keys = pay_ref[:, :, q_width + key_col:q_width + key_col + HEAD]
        fresh_values = pay_ref[:, :, q_width + key_col + HEAD:q_width + key_col + 2 * HEAD]
        cache_scores = jnp.einsum("bqd,bkd->bqk", grouped, cache_keys, preferred_element_type=jnp.float32) * score_scale
        fresh_scores = jnp.einsum("bqd,bkd->bqk", grouped, fresh_keys, preferred_element_type=jnp.float32) * score_scale
        cache_w = jnp.where(cache_seen, jnp.exp(soft_cap * jnp.tanh(cache_scores / soft_cap)), 0.0)
        fresh_w = jnp.where(fresh_seen, jnp.exp(soft_cap * jnp.tanh(fresh_scores / soft_cap)), 0.0)
        total = jnp.sum(cache_w, axis=-1, keepdims=True) + jnp.sum(fresh_w, axis=-1, keepdims=True)
        cache_p = (cache_w / total).astype(jnp.bfloat16)
        fresh_p = (fresh_w / total).astype(jnp.bfloat16)
        mixed = jnp.einsum("bqk,bkd->bqd", cache_p, cache_values, preferred_element_type=jnp.float32)
        mixed = mixed + jnp.einsum("bqk,bkd->bqd", fresh_p, fresh_values, preferred_element_type=jnp.float32)
        mixed = mixed.astype(out_ref.dtype)
        for g in range(group_size):
            col = (group_size * k + g) * HEAD
            out_ref[:, :, col:col + HEAD] = mixed[:, g * row_count:(g + 1) * row_count]


def attend_kernel(payload, cached, lengths, q_width, block=8):
    slot_count, row_count, _ = payload.shape
    cache_length, kv_width = cached.shape[1], cached.shape[2]
    block = min(block, slot_count)
    length_col = lengths.reshape(slot_count, 1, 1)
    return pl.pallas_call(
        functools.partial(attention_kernel, q_width=q_width),
        out_shape=jax.ShapeDtypeStruct((slot_count, row_count, q_width), jnp.bfloat16),
        grid=(slot_count // block,),
        in_specs=[
            pl.BlockSpec((block, 1, 1), lambda b: (b, 0, 0)),
            pl.BlockSpec((block, row_count, payload.shape[2]), lambda b: (b, 0, 0)),
            pl.BlockSpec((block, cache_length, kv_width), lambda b: (b, 0, 0)),
        ],
        out_specs=pl.BlockSpec((block, row_count, q_width), lambda b: (b, 0, 0)),
        cost_estimate=pl.CostEstimate(
            flops=4 * slot_count * (q_width // HEAD) * row_count * (cache_length + row_count) * HEAD,
            transcendentals=2 * slot_count * (q_width // HEAD) * row_count * (cache_length + row_count),
            bytes_accessed=int(cached.size * 2 + payload.size * 2 + slot_count * row_count * q_width * 2),
        ),
    )(length_col, payload, cached)


def pack_lanes(payload, slot_lanes, lane_count):
    lane_ids = jnp.arange(lane_count, dtype=jnp.int32)
    slot_ids = jnp.arange(payload.shape[0], dtype=jnp.int32)
    lane_hits = slot_lanes[None, :] == lane_ids[:, None]
    filled = jnp.any(lane_hits, axis=1)
    chosen = jnp.sum(jnp.where(lane_hits, slot_ids[None, :], 0), axis=1)
    picked = jnp.take(payload, chosen, axis=0)
    return jnp.where(filled[:, None, None], picked, jnp.zeros((), payload.dtype))


def halving_stages(axis):
    count = lax.axis_size(axis)
    stages = count.bit_length() - 1
    return count, stages if (1 << stages) == count else None


def scatter_sum(partial, axis):
    count, stages = halving_stages(axis)
    rows, width = partial.shape
    if stages is None:
        return lax.psum_scatter(partial, axis, scatter_dimension=1, tiled=True).astype(jnp.float32)
    me = lax.axis_index(axis)
    held = partial.reshape((rows,) + (2,) * stages + (width // count,))
    for s in range(stages):
        bit = (me >> s) & 1
        dim = stages - s
        keep = lax.dynamic_index_in_dim(held, bit, axis=dim, keepdims=False)
        send = lax.dynamic_index_in_dim(held, 1 - bit, axis=dim, keepdims=False)
        got = lax.ppermute(
            send.astype(jnp.bfloat16), axis, perm=[(i, i ^ (1 << s)) for i in range(count)]
        )
        held = keep.astype(jnp.float32) + got.astype(jnp.float32)
    return held


def butterfly_sum(values, axis):
    count, stages = halving_stages(axis)
    if stages is None:
        return lax.psum(values, axis)
    shape = values.shape
    lanes = 128 if values.size % 128 == 0 else values.size
    values = values.reshape(values.size // lanes, lanes)
    for s in range(stages):
        values = values + lax.ppermute(values, axis, perm=[(i, i ^ (1 << s)) for i in range(count)])
    return values.reshape(shape)


def shards(kv_cache, lengths, source, queries, fresh_kv, out_weight, norm_gain):
    dp_count = lax.axis_size("dp")
    slot_count, row_count, query_width = queries.shape
    kv_width = fresh_kv.shape[2]
    pair_cap = max(1, slot_count // dp_count)
    lane_count = dp_count * pair_cap
    slot_ids = jnp.arange(slot_count, dtype=jnp.int32)
    lane_ids = jnp.arange(lane_count, dtype=jnp.int32)

    old_home = source // slot_count
    old_slot = source % slot_count
    earlier = slot_ids[None, :] < slot_ids[:, None]
    same_home = old_home[:, None] == old_home[None, :]
    rank = jnp.sum(same_home & earlier, axis=1)
    out_lane = old_home * pair_cap + rank
    tag = jnp.broadcast_to(
        (old_slot + 1).astype(jnp.bfloat16)[:, None, None], (slot_count, row_count, TAG_WIDTH)
    )
    payload = jnp.concatenate([queries, fresh_kv, tag], axis=2)
    sending = pack_lanes(payload, out_lane, lane_count)
    arrived = lax.all_to_all(sending, "dp", 0, 0, tiled=True)

    lane_slot = arrived[:, 0, query_width + kv_width].astype(jnp.int32) - 1
    hits = lane_slot[None, :] == slot_ids[:, None]
    slot_lane = jnp.sum(jnp.where(hits, lane_ids[None, :], 0), axis=1)
    gathered = jnp.take(arrived, slot_lane, axis=0)
    attended = attend_kernel(gathered, kv_cache, lengths, query_width)

    filled = lane_slot >= 0
    back = jnp.take(attended, jnp.maximum(lane_slot, 0), axis=0)
    back = jnp.where(filled[:, None, None], back, jnp.zeros((), back.dtype))
    returned = lax.all_to_all(back, "dp", 0, 0, tiled=True)
    attended_here = jnp.take(returned, out_lane, axis=0)

    row_total = slot_count * row_count
    flat_rows = attended_here.reshape(row_total, query_width)
    partial_value = jnp.dot(flat_rows, out_weight, preferred_element_type=jnp.float32)
    model_width = out_weight.shape[1]
    own_part = scatter_sum(partial_value.astype(jnp.bfloat16), "tensor")
    square_sum = jnp.sum(own_part * own_part, axis=-1)
    square_sum = butterfly_sum(square_sum, "tensor").reshape(row_total, 1)
    mean_square = square_sum / model_width
    normed = own_part * lax.rsqrt(mean_square + norm_eps) * norm_gain
    return normed.astype(jnp.bfloat16).reshape(slot_count, row_count, own_part.shape[1])


def solution(mesh):
    placed = (
        P(("groups", "dp"), None, "tensor"),
        P(("groups", "dp")),
        P(("groups", "dp")),
        P(("groups", "dp"), None, "tensor"),
        P(("groups", "dp"), None, "tensor"),
        P("tensor", None),
        P("tensor"),
    )
    return jax.shard_map(
        shards,
        mesh=mesh,
        in_specs=placed,
        out_specs=P(("groups", "dp"), None, "tensor"),
        check_vma=False,
    )
```

```python
import functools

import jax
import jax.numpy as jnp
from jax import lax
from jax.experimental import pallas as pl
from jax.experimental.pallas import tpu as pltpu
from jax.sharding import PartitionSpec as P

HEAD = 128
QHEADS = 16
KVHEADS = 8
TAG_WIDTH = 128


score_scale = 144.0 ** (-0.5)
soft_cap = 50.0
norm_eps = 1e-06


def attention_kernel(length_ref, pay_ref, cache_ref, out_ref, *, q_width):
    sessions, cache_length, _ = cache_ref.shape
    row_count = pay_ref.shape[1]
    kv_heads = cache_ref.shape[2] // (2 * HEAD)
    group_size = QHEADS // KVHEADS
    lengths = length_ref[...]
    cache_pos = lax.broadcasted_iota(jnp.int32, (sessions, group_size * row_count, cache_length), 2)
    cache_seen = cache_pos < lengths
    fresh_pos = lax.broadcasted_iota(jnp.int32, (sessions, group_size * row_count, row_count), 2)
    query_row = lax.broadcasted_iota(jnp.int32, (sessions, group_size * row_count, row_count), 1) % row_count
    fresh_seen = fresh_pos <= query_row
    for k in range(kv_heads):
        key_col = 2 * HEAD * k
        grouped = jnp.concatenate(
            [pay_ref[:, :, (group_size * k + g) * HEAD:(group_size * k + g + 1) * HEAD] for g in range(group_size)],
            axis=1,
        )
        cache_keys = cache_ref[:, :, key_col:key_col + HEAD]
        cache_values = cache_ref[:, :, key_col + HEAD:key_col + 2 * HEAD]
        fresh_keys = pay_ref[:, :, q_width + key_col:q_width + key_col + HEAD]
        fresh_values = pay_ref[:, :, q_width + key_col + HEAD:q_width + key_col + 2 * HEAD]
        cache_scores = jnp.einsum("bqd,bkd->bqk", grouped, cache_keys, preferred_element_type=jnp.float32) * score_scale
        fresh_scores = jnp.einsum("bqd,bkd->bqk", grouped, fresh_keys, preferred_element_type=jnp.float32) * score_scale
        cache_w = jnp.where(cache_seen, jnp.exp(soft_cap * jnp.tanh(cache_scores / soft_cap)), 0.0)
        fresh_w = jnp.where(fresh_seen, jnp.exp(soft_cap * jnp.tanh(fresh_scores / soft_cap)), 0.0)
        total = jnp.sum(cache_w, axis=-1, keepdims=True) + jnp.sum(fresh_w, axis=-1, keepdims=True)
        cache_p = (cache_w / total).astype(jnp.bfloat16)
        fresh_p = (fresh_w / total).astype(jnp.bfloat16)
        mixed = jnp.einsum("bqk,bkd->bqd", cache_p, cache_values, preferred_element_type=jnp.float32)
        mixed = mixed + jnp.einsum("bqk,bkd->bqd", fresh_p, fresh_values, preferred_element_type=jnp.float32)
        mixed = mixed.astype(out_ref.dtype)
        for g in range(group_size):
            col = (group_size * k + g) * HEAD
            out_ref[:, :, col:col + HEAD] = mixed[:, g * row_count:(g + 1) * row_count]


def attend_kernel(payload, cached, lengths, q_width, block=8):
    slot_count, row_count, _ = payload.shape
    cache_length, kv_width = cached.shape[1], cached.shape[2]
    block = min(block, slot_count)
    length_col = lengths.reshape(slot_count, 1, 1)
    return pl.pallas_call(
        functools.partial(attention_kernel, q_width=q_width),
        out_shape=jax.ShapeDtypeStruct((slot_count, row_count, q_width), jnp.bfloat16),
        grid=(slot_count // block,),
        in_specs=[
            pl.BlockSpec((block, 1, 1), lambda b: (b, 0, 0)),
            pl.BlockSpec((block, row_count, payload.shape[2]), lambda b: (b, 0, 0)),
            pl.BlockSpec((block, cache_length, kv_width), lambda b: (b, 0, 0)),
        ],
        out_specs=pl.BlockSpec((block, row_count, q_width), lambda b: (b, 0, 0)),
        cost_estimate=pl.CostEstimate(
            flops=4 * slot_count * (q_width // HEAD) * row_count * (cache_length + row_count) * HEAD,
            transcendentals=2 * slot_count * (q_width // HEAD) * row_count * (cache_length + row_count),
            bytes_accessed=int(cached.size * 2 + payload.size * 2 + slot_count * row_count * q_width * 2),
        ),
    )(length_col, payload, cached)


def pack_lanes(payload, slot_lanes, lane_count):
    lane_ids = jnp.arange(lane_count, dtype=jnp.int32)
    slot_ids = jnp.arange(payload.shape[0], dtype=jnp.int32)
    lane_hits = slot_lanes[None, :] == lane_ids[:, None]
    filled = jnp.any(lane_hits, axis=1)
    chosen = jnp.sum(jnp.where(lane_hits, slot_ids[None, :], 0), axis=1)
    picked = jnp.take(payload, chosen, axis=0)
    return jnp.where(filled[:, None, None], picked, jnp.zeros((), payload.dtype))


def halving_stages(axis):
    count = lax.axis_size(axis)
    stages = count.bit_length() - 1
    return count, stages if (1 << stages) == count else None


def scatter_sum(partial, axis):
    count, stages = halving_stages(axis)
    rows, width = partial.shape
    if stages is None:
        return lax.psum_scatter(partial, axis, scatter_dimension=1, tiled=True).astype(jnp.float32)
    me = lax.axis_index(axis)
    held = partial.reshape((rows,) + (2,) * stages + (width // count,))
    for s in range(stages):
        bit = (me >> s) & 1
        dim = stages - s
        keep = lax.dynamic_index_in_dim(held, bit, axis=dim, keepdims=False)
        send = lax.dynamic_index_in_dim(held, 1 - bit, axis=dim, keepdims=False)
        got = lax.ppermute(
            send.astype(jnp.bfloat16), axis, perm=[(i, i ^ (1 << s)) for i in range(count)]
        )
        held = keep.astype(jnp.float32) + got.astype(jnp.float32)
    return held


def projection_kernel(block_ref, rows_ref, weight_ref, out_ref):
    out_ref[0] = jnp.dot(rows_ref[...], weight_ref[...], preferred_element_type=jnp.float32).astype(out_ref.dtype)


def project_blocks(rows, weight, blocks):
    row_total, inner = rows.shape
    width = weight.shape[1] // lax.axis_size("tensor")
    count = blocks.shape[0]
    return pl.pallas_call(
        projection_kernel,
        out_shape=jax.ShapeDtypeStruct((count, row_total, width), jnp.bfloat16),
        grid_spec=pltpu.PrefetchScalarGridSpec(
            num_scalar_prefetch=1,
            grid=(count,),
            in_specs=[
                pl.BlockSpec((row_total, inner), lambda j, blk: (0, 0)),
                pl.BlockSpec((inner, width), lambda j, blk: (0, blk[j])),
            ],
            out_specs=pl.BlockSpec((1, row_total, width), lambda j, blk: (j, 0, 0)),
        ),
        cost_estimate=pl.CostEstimate(
            flops=2 * count * row_total * inner * width,
            transcendentals=0,
            bytes_accessed=int(rows.size * 2 + count * (inner * width + row_total * width) * 2),
        ),
    )(blocks, rows, weight)


def bit_reversed(value, bits):
    out = 0
    for b in range(bits):
        out |= ((value >> b) & 1) << (bits - 1 - b)
    return out


def project_and_scatter(rows, weight, axis):
    count = lax.axis_size(axis)
    stages = count.bit_length() - 1
    if (1 << stages) != count or (weight.shape[1] // count) % 128:
        products = jnp.dot(rows, weight, preferred_element_type=jnp.float32).astype(jnp.bfloat16)
        return scatter_sum(products, axis)
    me = lax.axis_index(axis)
    order = jnp.array([bit_reversed(j, stages) for j in range(count)], jnp.int32)
    blocks = jnp.bitwise_xor(me, order)
    half = count // 2
    sent = project_blocks(rows, weight, blocks[half:])
    kept = project_blocks(rows, weight, blocks[:half])
    got = lax.ppermute(sent, axis, perm=[(i, i ^ 1) for i in range(count)])
    held = kept.astype(jnp.float32) + got.astype(jnp.float32)
    for s in range(1, stages):
        half = held.shape[0] // 2
        got = lax.ppermute(
            held[half:].astype(jnp.bfloat16), axis, perm=[(i, i ^ (1 << s)) for i in range(count)]
        )
        held = held[:half] + got.astype(jnp.float32)
    return held[0]


def butterfly_sum(values, axis):
    count, stages = halving_stages(axis)
    if stages is None:
        return lax.psum(values, axis)
    shape = values.shape
    lanes = 128 if values.size % 128 == 0 else values.size
    values = values.reshape(values.size // lanes, lanes)
    for s in range(stages):
        values = values + lax.ppermute(values, axis, perm=[(i, i ^ (1 << s)) for i in range(count)])
    return values.reshape(shape)


def shards(kv_cache, lengths, source, queries, fresh_kv, out_weight, norm_gain):
    dp_count = lax.axis_size("dp")
    slot_count, row_count, query_width = queries.shape
    kv_width = fresh_kv.shape[2]
    pair_cap = max(1, slot_count // dp_count)
    lane_count = dp_count * pair_cap
    slot_ids = jnp.arange(slot_count, dtype=jnp.int32)
    lane_ids = jnp.arange(lane_count, dtype=jnp.int32)

    old_home = source // slot_count
    old_slot = source % slot_count
    earlier = slot_ids[None, :] < slot_ids[:, None]
    same_home = old_home[:, None] == old_home[None, :]
    rank = jnp.sum(same_home & earlier, axis=1)
    out_lane = old_home * pair_cap + rank
    tag = jnp.broadcast_to(
        (old_slot + 1).astype(jnp.bfloat16)[:, None, None], (slot_count, row_count, TAG_WIDTH)
    )
    payload = jnp.concatenate([queries, fresh_kv, tag], axis=2)
    sending = pack_lanes(payload, out_lane, lane_count)
    arrived = lax.all_to_all(sending, "dp", 0, 0, tiled=True)

    lane_slot = arrived[:, 0, query_width + kv_width].astype(jnp.int32) - 1
    hits = lane_slot[None, :] == slot_ids[:, None]
    slot_lane = jnp.sum(jnp.where(hits, lane_ids[None, :], 0), axis=1)
    gathered = jnp.take(arrived, slot_lane, axis=0)
    attended = attend_kernel(gathered, kv_cache, lengths, query_width)

    filled = lane_slot >= 0
    back = jnp.take(attended, jnp.maximum(lane_slot, 0), axis=0)
    back = jnp.where(filled[:, None, None], back, jnp.zeros((), back.dtype))
    returned = lax.all_to_all(back, "dp", 0, 0, tiled=True)
    attended_here = jnp.take(returned, out_lane, axis=0)

    row_total = slot_count * row_count
    flat_rows = attended_here.reshape(row_total, query_width)
    model_width = out_weight.shape[1]
    own_part = project_and_scatter(flat_rows, out_weight, "tensor")
    square_sum = jnp.sum(own_part * own_part, axis=-1)
    square_sum = butterfly_sum(square_sum, "tensor").reshape(row_total, 1)
    mean_square = square_sum / model_width
    normed = own_part * lax.rsqrt(mean_square + norm_eps) * norm_gain
    return normed.astype(jnp.bfloat16).reshape(slot_count, row_count, own_part.shape[1])


def solution(mesh):
    placed = (
        P(("groups", "dp"), None, "tensor"),
        P(("groups", "dp")),
        P(("groups", "dp")),
        P(("groups", "dp"), None, "tensor"),
        P(("groups", "dp"), None, "tensor"),
        P("tensor", None),
        P("tensor"),
    )
    return jax.shard_map(
        shards,
        mesh=mesh,
        in_specs=placed,
        out_specs=P(("groups", "dp"), None, "tensor"),
        check_vma=False,
    )
```

```python
import functools

import jax
import jax.numpy as jnp
from jax import lax
from jax.experimental import pallas as pl
from jax.experimental.pallas import tpu as pltpu
from jax.sharding import PartitionSpec as P

HEAD = 128
QHEADS = 16
KVHEADS = 8
TAG_WIDTH = 128


score_scale = 144.0 ** (-0.5)
soft_cap = 50.0
norm_eps = 1e-06


def attention_kernel(slot_ref, length_ref, pay_ref, cache_hbm, out_ref, cache_buf, cache_sem, *, q_width):
    step = pl.program_id(0)
    steps = pl.num_programs(0)
    sessions, row_count, _ = pay_ref.shape
    cache_length = cache_buf.shape[2]
    kv_heads = cache_buf.shape[3] // (2 * HEAD)
    group_size = QHEADS // KVHEADS

    def cache_copies(block, slot):
        return [
            pltpu.make_async_copy(
                cache_hbm.at[slot_ref[block * sessions + i]], cache_buf.at[slot, i], cache_sem.at[slot, i]
            )
            for i in range(sessions)
        ]

    @pl.when(step == 0)
    def _():
        for copy in cache_copies(0, 0):
            copy.start()

    @pl.when(step + 1 < steps)
    def _():
        for copy in cache_copies(step + 1, (step + 1) % 2):
            copy.start()

    current = step % 2
    for copy in cache_copies(step, current):
        copy.wait()
    cache_ref = cache_buf.at[current]

    lengths = length_ref[...]
    cache_pos = lax.broadcasted_iota(jnp.int32, (sessions, group_size * row_count, cache_length), 2)
    cache_seen = cache_pos < lengths
    fresh_pos = lax.broadcasted_iota(jnp.int32, (sessions, group_size * row_count, row_count), 2)
    query_row = lax.broadcasted_iota(jnp.int32, (sessions, group_size * row_count, row_count), 1) % row_count
    fresh_seen = fresh_pos <= query_row
    for k in range(kv_heads):
        key_col = 2 * HEAD * k
        grouped = jnp.concatenate(
            [pay_ref[:, :, (group_size * k + g) * HEAD:(group_size * k + g + 1) * HEAD] for g in range(group_size)],
            axis=1,
        )
        cache_keys = cache_ref[:, :, key_col:key_col + HEAD]
        cache_values = cache_ref[:, :, key_col + HEAD:key_col + 2 * HEAD]
        fresh_keys = pay_ref[:, :, q_width + key_col:q_width + key_col + HEAD]
        fresh_values = pay_ref[:, :, q_width + key_col + HEAD:q_width + key_col + 2 * HEAD]
        cache_scores = jnp.einsum("bqd,bkd->bqk", grouped, cache_keys, preferred_element_type=jnp.float32) * score_scale
        fresh_scores = jnp.einsum("bqd,bkd->bqk", grouped, fresh_keys, preferred_element_type=jnp.float32) * score_scale
        cache_w = jnp.where(cache_seen, jnp.exp(soft_cap * jnp.tanh(cache_scores / soft_cap)), 0.0)
        fresh_w = jnp.where(fresh_seen, jnp.exp(soft_cap * jnp.tanh(fresh_scores / soft_cap)), 0.0)
        total = jnp.sum(cache_w, axis=-1, keepdims=True) + jnp.sum(fresh_w, axis=-1, keepdims=True)
        cache_p = (cache_w / total).astype(jnp.bfloat16)
        fresh_p = (fresh_w / total).astype(jnp.bfloat16)
        mixed = jnp.einsum("bqk,bkd->bqd", cache_p, cache_values, preferred_element_type=jnp.float32)
        mixed = mixed + jnp.einsum("bqk,bkd->bqd", fresh_p, fresh_values, preferred_element_type=jnp.float32)
        mixed = mixed.astype(out_ref.dtype)
        for g in range(group_size):
            col = (group_size * k + g) * HEAD
            out_ref[:, :, col:col + HEAD] = mixed[:, g * row_count:(g + 1) * row_count]


def attend_lanes(payload, cached, lane_slot, lane_length, q_width, block=8):
    lane_count, row_count, pay_width = payload.shape
    cache_length, kv_width = cached.shape[1], cached.shape[2]
    block = block if lane_count % block == 0 else lane_count
    return pl.pallas_call(
        functools.partial(attention_kernel, q_width=q_width),
        out_shape=jax.ShapeDtypeStruct((lane_count, row_count, q_width), jnp.bfloat16),
        grid_spec=pltpu.PrefetchScalarGridSpec(
            num_scalar_prefetch=1,
            grid=(lane_count // block,),
            in_specs=[
                pl.BlockSpec((block, 1, 1), lambda b, slots: (b, 0, 0)),
                pl.BlockSpec((block, row_count, pay_width), lambda b, slots: (b, 0, 0)),
                pl.BlockSpec(memory_space=pl.ANY),
            ],
            out_specs=pl.BlockSpec((block, row_count, q_width), lambda b, slots: (b, 0, 0)),
            scratch_shapes=[
                pltpu.VMEM((2, block, cache_length, kv_width), cached.dtype),
                pltpu.SemaphoreType.DMA((2, block)),
            ],
        ),
        cost_estimate=pl.CostEstimate(
            flops=4 * lane_count * (q_width // HEAD) * row_count * (cache_length + row_count) * HEAD,
            transcendentals=2 * lane_count * (q_width // HEAD) * row_count * (cache_length + row_count),
            bytes_accessed=int(lane_count * (cache_length * kv_width + row_count * (pay_width + q_width)) * 2),
        ),
    )(lane_slot, lane_length.reshape(lane_count, 1, 1), payload, cached)


def pack_lanes(payload, slot_lanes, lane_count):
    lane_ids = jnp.arange(lane_count, dtype=jnp.int32)
    slot_ids = jnp.arange(payload.shape[0], dtype=jnp.int32)
    lane_hits = slot_lanes[None, :] == lane_ids[:, None]
    filled = jnp.any(lane_hits, axis=1)
    chosen = jnp.sum(jnp.where(lane_hits, slot_ids[None, :], 0), axis=1)
    picked = jnp.take(payload, chosen, axis=0)
    return jnp.where(filled[:, None, None], picked, jnp.zeros((), payload.dtype))


def halving_stages(axis):
    count = lax.axis_size(axis)
    stages = count.bit_length() - 1
    return count, stages if (1 << stages) == count else None


def scatter_sum(partial, axis):
    count, stages = halving_stages(axis)
    rows, width = partial.shape
    if stages is None:
        return lax.psum_scatter(partial, axis, scatter_dimension=1, tiled=True).astype(jnp.float32)
    me = lax.axis_index(axis)
    held = partial.reshape((rows,) + (2,) * stages + (width // count,))
    for s in range(stages):
        bit = (me >> s) & 1
        dim = stages - s
        keep = lax.dynamic_index_in_dim(held, bit, axis=dim, keepdims=False)
        send = lax.dynamic_index_in_dim(held, 1 - bit, axis=dim, keepdims=False)
        got = lax.ppermute(
            send.astype(jnp.bfloat16), axis, perm=[(i, i ^ (1 << s)) for i in range(count)]
        )
        held = keep.astype(jnp.float32) + got.astype(jnp.float32)
    return held


def projection_kernel(block_ref, rows_ref, weight_ref, out_ref):
    out_ref[0] = jnp.dot(rows_ref[...], weight_ref[...], preferred_element_type=jnp.float32).astype(out_ref.dtype)


def project_blocks(rows, weight, blocks):
    row_total, inner = rows.shape
    width = weight.shape[1] // lax.axis_size("tensor")
    count = blocks.shape[0]
    return pl.pallas_call(
        projection_kernel,
        out_shape=jax.ShapeDtypeStruct((count, row_total, width), jnp.bfloat16),
        grid_spec=pltpu.PrefetchScalarGridSpec(
            num_scalar_prefetch=1,
            grid=(count,),
            in_specs=[
                pl.BlockSpec((row_total, inner), lambda j, blk: (0, 0)),
                pl.BlockSpec((inner, width), lambda j, blk: (0, blk[j])),
            ],
            out_specs=pl.BlockSpec((1, row_total, width), lambda j, blk: (j, 0, 0)),
        ),
        cost_estimate=pl.CostEstimate(
            flops=2 * count * row_total * inner * width,
            transcendentals=0,
            bytes_accessed=int(rows.size * 2 + count * (inner * width + row_total * width) * 2),
        ),
    )(blocks, rows, weight)


def bit_reversed(value, bits):
    out = 0
    for b in range(bits):
        out |= ((value >> b) & 1) << (bits - 1 - b)
    return out


def project_and_scatter(rows, weight, axis):
    count = lax.axis_size(axis)
    stages = count.bit_length() - 1
    if (1 << stages) != count or (weight.shape[1] // count) % 128:
        products = jnp.dot(rows, weight, preferred_element_type=jnp.float32).astype(jnp.bfloat16)
        return scatter_sum(products, axis)
    me = lax.axis_index(axis)
    order = jnp.array([bit_reversed(j, stages) for j in range(count)], jnp.int32)
    blocks = jnp.bitwise_xor(me, order)
    half = count // 2
    sent = project_blocks(rows, weight, blocks[half:])
    kept = project_blocks(rows, weight, blocks[:half])
    got = lax.ppermute(sent, axis, perm=[(i, i ^ 1) for i in range(count)])
    held = kept.astype(jnp.float32) + got.astype(jnp.float32)
    for s in range(1, stages):
        half = held.shape[0] // 2
        got = lax.ppermute(
            held[half:].astype(jnp.bfloat16), axis, perm=[(i, i ^ (1 << s)) for i in range(count)]
        )
        held = held[:half] + got.astype(jnp.float32)
    return held[0]


def butterfly_sum(values, axis):
    count, stages = halving_stages(axis)
    if stages is None:
        return lax.psum(values, axis)
    shape = values.shape
    lanes = 128 if values.size % 128 == 0 else values.size
    values = values.reshape(values.size // lanes, lanes)
    for s in range(stages):
        values = values + lax.ppermute(values, axis, perm=[(i, i ^ (1 << s)) for i in range(count)])
    return values.reshape(shape)


def shards(kv_cache, lengths, source, queries, fresh_kv, out_weight, norm_gain):
    dp_count = lax.axis_size("dp")
    slot_count, row_count, query_width = queries.shape
    kv_width = fresh_kv.shape[2]
    pair_cap = max(1, slot_count // dp_count)
    chunks = 2 if pair_cap % 2 == 0 else 1
    chunk_cap = pair_cap // chunks
    chunk_lanes = dp_count * chunk_cap
    slot_ids = jnp.arange(slot_count, dtype=jnp.int32)
    model_width = out_weight.shape[1]

    old_home = source // slot_count
    old_slot = source % slot_count
    earlier = slot_ids[None, :] < slot_ids[:, None]
    same_home = old_home[:, None] == old_home[None, :]
    rank = jnp.sum(same_home & earlier, axis=1)
    chunk_of = rank // chunk_cap
    lane_of = old_home * chunk_cap + rank % chunk_cap
    tag = jnp.broadcast_to(
        (old_slot + 1).astype(jnp.bfloat16)[:, None, None], (slot_count, row_count, TAG_WIDTH)
    )
    payload = jnp.concatenate([queries, fresh_kv, tag], axis=2)

    normed_parts = []
    for c in range(chunks):
        sending = pack_lanes(payload, jnp.where(chunk_of == c, lane_of, -1), chunk_lanes)
        arrived = lax.all_to_all(sending, "dp", 0, 0, tiled=True)
        lane_slot = jnp.clip(arrived[:, 0, query_width + kv_width].astype(jnp.int32) - 1, 0, slot_count - 1)
        attended = attend_lanes(arrived, kv_cache, lane_slot, lengths[lane_slot], query_width)
        returned = lax.all_to_all(attended, "dp", 0, 0, tiled=True)
        flat_rows = returned.reshape(chunk_lanes * row_count, query_width)
        own_part = project_and_scatter(flat_rows, out_weight, "tensor")
        square_sum = jnp.sum(own_part * own_part, axis=-1)
        square_sum = butterfly_sum(square_sum, "tensor").reshape(-1, 1)
        mean_square = square_sum / model_width
        normed = own_part * lax.rsqrt(mean_square + norm_eps) * norm_gain
        normed_parts.append(normed.astype(jnp.bfloat16).reshape(chunk_lanes, row_count, -1))
    normed_lanes = jnp.concatenate(normed_parts, axis=0)
    return jnp.take(normed_lanes, chunk_of * chunk_lanes + lane_of, axis=0)


def solution(mesh):
    placed = (
        P(("groups", "dp"), None, "tensor"),
        P(("groups", "dp")),
        P(("groups", "dp")),
        P(("groups", "dp"), None, "tensor"),
        P(("groups", "dp"), None, "tensor"),
        P("tensor", None),
        P("tensor"),
    )
    return jax.shard_map(
        shards,
        mesh=mesh,
        in_specs=placed,
        out_specs=P(("groups", "dp"), None, "tensor"),
        check_vma=False,
    )
```

```python
import functools

import jax
import jax.numpy as jnp
from jax import lax
from jax.experimental import pallas as pl
from jax.experimental.pallas import tpu as pltpu
from jax.sharding import PartitionSpec as P

HEAD = 128
QHEADS = 16
KVHEADS = 8
TAG_WIDTH = 128


score_scale = 144.0 ** (-0.5)
soft_cap = 50.0
norm_eps = 1e-06


def attention_kernel(slot_ref, length_ref, pay_ref, cache_hbm, out_ref, cache_buf, cache_sem, *, q_width):
    step = pl.program_id(0)
    steps = pl.num_programs(0)
    sessions, row_count, _ = pay_ref.shape
    cache_length = cache_buf.shape[2]
    kv_heads = cache_buf.shape[3] // (2 * HEAD)
    group_size = QHEADS // KVHEADS

    def cache_copies(block, slot):
        return [
            pltpu.make_async_copy(
                cache_hbm.at[slot_ref[block * sessions + i]], cache_buf.at[slot, i], cache_sem.at[slot, i]
            )
            for i in range(sessions)
        ]

    @pl.when(step == 0)
    def _():
        for copy in cache_copies(0, 0):
            copy.start()

    @pl.when(step + 1 < steps)
    def _():
        for copy in cache_copies(step + 1, (step + 1) % 2):
            copy.start()

    current = step % 2
    for copy in cache_copies(step, current):
        copy.wait()
    cache_ref = cache_buf.at[current]

    lengths = length_ref[...]
    cache_pos = lax.broadcasted_iota(jnp.int32, (sessions, group_size * row_count, cache_length), 2)
    cache_seen = cache_pos < lengths
    fresh_pos = lax.broadcasted_iota(jnp.int32, (sessions, group_size * row_count, row_count), 2)
    query_row = lax.broadcasted_iota(jnp.int32, (sessions, group_size * row_count, row_count), 1) % row_count
    fresh_seen = fresh_pos <= query_row
    for k in range(kv_heads):
        key_col = 2 * HEAD * k
        grouped = jnp.concatenate(
            [pay_ref[:, :, (group_size * k + g) * HEAD:(group_size * k + g + 1) * HEAD] for g in range(group_size)],
            axis=1,
        )
        cache_keys = cache_ref[:, :, key_col:key_col + HEAD]
        cache_values = cache_ref[:, :, key_col + HEAD:key_col + 2 * HEAD]
        fresh_keys = pay_ref[:, :, q_width + key_col:q_width + key_col + HEAD]
        fresh_values = pay_ref[:, :, q_width + key_col + HEAD:q_width + key_col + 2 * HEAD]
        cache_scores = jnp.einsum("bqd,bkd->bqk", grouped, cache_keys, preferred_element_type=jnp.float32) * score_scale
        fresh_scores = jnp.einsum("bqd,bkd->bqk", grouped, fresh_keys, preferred_element_type=jnp.float32) * score_scale
        cache_w = jnp.where(cache_seen, jnp.exp(soft_cap * jnp.tanh(cache_scores / soft_cap)), 0.0)
        fresh_w = jnp.where(fresh_seen, jnp.exp(soft_cap * jnp.tanh(fresh_scores / soft_cap)), 0.0)
        total = jnp.sum(cache_w, axis=-1, keepdims=True) + jnp.sum(fresh_w, axis=-1, keepdims=True)
        cache_p = (cache_w / total).astype(jnp.bfloat16)
        fresh_p = (fresh_w / total).astype(jnp.bfloat16)
        mixed = jnp.einsum("bqk,bkd->bqd", cache_p, cache_values, preferred_element_type=jnp.float32)
        mixed = mixed + jnp.einsum("bqk,bkd->bqd", fresh_p, fresh_values, preferred_element_type=jnp.float32)
        mixed = mixed.astype(out_ref.dtype)
        for g in range(group_size):
            col = (group_size * k + g) * HEAD
            out_ref[:, :, col:col + HEAD] = mixed[:, g * row_count:(g + 1) * row_count]


def attend_lanes(payload, cached, lane_slot, lane_length, q_width, block, chunks):
    lane_count, row_count, pay_width = payload.shape
    cache_length, kv_width = cached.shape[1], cached.shape[2]
    return pl.pallas_call(
        functools.partial(attention_kernel, q_width=q_width),
        out_shape=jax.ShapeDtypeStruct((chunks, lane_count // chunks, row_count, q_width), jnp.bfloat16),
        grid_spec=pltpu.PrefetchScalarGridSpec(
            num_scalar_prefetch=1,
            grid=(lane_count // block,),
            in_specs=[
                pl.BlockSpec((block, 1, 1), lambda b, slots: (b, 0, 0)),
                pl.BlockSpec((block, row_count, pay_width), lambda b, slots: (b, 0, 0)),
                pl.BlockSpec(memory_space=pl.ANY),
            ],
            out_specs=pl.BlockSpec((None, block, row_count, q_width), lambda b, slots: (b % chunks, b // chunks, 0, 0)),
            scratch_shapes=[
                pltpu.VMEM((2, block, cache_length, kv_width), cached.dtype),
                pltpu.SemaphoreType.DMA((2, block)),
            ],
        ),
        cost_estimate=pl.CostEstimate(
            flops=4 * lane_count * (q_width // HEAD) * row_count * (cache_length + row_count) * HEAD,
            transcendentals=2 * lane_count * (q_width // HEAD) * row_count * (cache_length + row_count),
            bytes_accessed=int(lane_count * (cache_length * kv_width + row_count * (pay_width + q_width)) * 2),
        ),
    )(lane_slot, lane_length.reshape(lane_count, 1, 1), payload, cached)


def pack_lanes(payload, slot_lanes, lane_count):
    lane_ids = jnp.arange(lane_count, dtype=jnp.int32)
    slot_ids = jnp.arange(payload.shape[0], dtype=jnp.int32)
    lane_hits = slot_lanes[None, :] == lane_ids[:, None]
    filled = jnp.any(lane_hits, axis=1)
    chosen = jnp.sum(jnp.where(lane_hits, slot_ids[None, :], 0), axis=1)
    picked = jnp.take(payload, chosen, axis=0)
    return jnp.where(filled[:, None, None], picked, jnp.zeros((), payload.dtype))


def halving_stages(axis):
    count = lax.axis_size(axis)
    stages = count.bit_length() - 1
    return count, stages if (1 << stages) == count else None


def scatter_sum(partial, axis):
    count, stages = halving_stages(axis)
    rows, width = partial.shape
    if stages is None:
        return lax.psum_scatter(partial, axis, scatter_dimension=1, tiled=True).astype(jnp.float32)
    me = lax.axis_index(axis)
    held = partial.reshape((rows,) + (2,) * stages + (width // count,))
    for s in range(stages):
        bit = (me >> s) & 1
        dim = stages - s
        keep = lax.dynamic_index_in_dim(held, bit, axis=dim, keepdims=False)
        send = lax.dynamic_index_in_dim(held, 1 - bit, axis=dim, keepdims=False)
        got = lax.ppermute(
            send.astype(jnp.bfloat16), axis, perm=[(i, i ^ (1 << s)) for i in range(count)]
        )
        held = keep.astype(jnp.float32) + got.astype(jnp.float32)
    return held


def projection_kernel(block_ref, rows_ref, weight_ref, out_ref):
    out_ref[0] = jnp.dot(rows_ref[...], weight_ref[...], preferred_element_type=jnp.float32).astype(out_ref.dtype)


def project_blocks(rows, weight, blocks):
    row_total, inner = rows.shape
    width = weight.shape[1] // lax.axis_size("tensor")
    count = blocks.shape[0]
    return pl.pallas_call(
        projection_kernel,
        out_shape=jax.ShapeDtypeStruct((count, row_total, width), jnp.bfloat16),
        grid_spec=pltpu.PrefetchScalarGridSpec(
            num_scalar_prefetch=1,
            grid=(count,),
            in_specs=[
                pl.BlockSpec((row_total, inner), lambda j, blk: (0, 0)),
                pl.BlockSpec((inner, width), lambda j, blk: (0, blk[j])),
            ],
            out_specs=pl.BlockSpec((1, row_total, width), lambda j, blk: (j, 0, 0)),
        ),
        cost_estimate=pl.CostEstimate(
            flops=2 * count * row_total * inner * width,
            transcendentals=0,
            bytes_accessed=int(rows.size * 2 + count * (inner * width + row_total * width) * 2),
        ),
    )(blocks, rows, weight)


def bit_reversed(value, bits):
    out = 0
    for b in range(bits):
        out |= ((value >> b) & 1) << (bits - 1 - b)
    return out


def project_and_scatter(rows, weight, axis):
    count = lax.axis_size(axis)
    stages = count.bit_length() - 1
    if (1 << stages) != count or (weight.shape[1] // count) % 128:
        products = jnp.dot(rows, weight, preferred_element_type=jnp.float32).astype(jnp.bfloat16)
        return scatter_sum(products, axis), None
    me = lax.axis_index(axis)
    order = jnp.array([bit_reversed(j, stages) for j in range(count)], jnp.int32)
    blocks = jnp.bitwise_xor(me, order)
    half = count // 2
    sent = project_blocks(rows, weight, blocks[half:])
    kept = project_blocks(rows, weight, blocks[:half])
    got = lax.ppermute(sent, axis, perm=[(i, i ^ 1) for i in range(count)])
    held = kept.astype(jnp.float32) + got.astype(jnp.float32)
    for s in range(1, stages):
        half = held.shape[0] // 2
        sent = held[half:].astype(jnp.bfloat16)
        got = lax.ppermute(sent, axis, perm=[(i, i ^ (1 << s)) for i in range(count)])
        held = held[:half] + got.astype(jnp.float32)
    return held[0], sent


def butterfly_sum(values, axis):
    count, stages = halving_stages(axis)
    if stages is None:
        return lax.psum(values, axis)
    shape = values.shape
    lanes = 128 if values.size % 128 == 0 else values.size
    values = values.reshape(values.size // lanes, lanes)
    for s in range(stages):
        values = values + lax.ppermute(values, axis, perm=[(i, i ^ (1 << s)) for i in range(count)])
    return values.reshape(shape)


def shards(kv_cache, lengths, source, queries, fresh_kv, out_weight, norm_gain):
    dp_count = lax.axis_size("dp")
    slot_count, row_count, query_width = queries.shape
    kv_width = fresh_kv.shape[2]
    pair_cap = max(1, slot_count // dp_count)
    lane_count = dp_count * pair_cap
    chunks = 2 if pair_cap % 2 == 0 else 1
    chunk_cap = pair_cap // chunks
    chunk_lanes = dp_count * chunk_cap
    slot_ids = jnp.arange(slot_count, dtype=jnp.int32)
    model_width = out_weight.shape[1]

    old_home = source // slot_count
    old_slot = source % slot_count
    earlier = slot_ids[None, :] < slot_ids[:, None]
    same_home = old_home[:, None] == old_home[None, :]
    rank = jnp.sum(same_home & earlier, axis=1)
    out_lane = old_home * pair_cap + rank
    tag = jnp.broadcast_to(
        (old_slot + 1).astype(jnp.bfloat16)[:, None, None], (slot_count, row_count, TAG_WIDTH)
    )
    payload = jnp.concatenate([queries, fresh_kv, tag], axis=2)
    sending = pack_lanes(payload, out_lane, lane_count)
    arrived = lax.all_to_all(sending, "dp", 0, 0, tiled=True)

    lane_slot = jnp.clip(arrived[:, 0, query_width + kv_width].astype(jnp.int32) - 1, 0, slot_count - 1)
    attended = attend_lanes(arrived, kv_cache, lane_slot, lengths[lane_slot], query_width, chunk_cap, chunks)

    normed_parts = []
    gate = None
    for c in range(chunks):
        returned = lax.all_to_all(attended[c], "dp", 0, 0, tiled=True)
        flat_rows = returned.reshape(chunk_lanes * row_count, query_width)
        if gate is not None:
            flat_rows = lax.optimization_barrier((flat_rows, gate))[0]
        own_part, gate = project_and_scatter(flat_rows, out_weight, "tensor")
        square_sum = jnp.sum(own_part * own_part, axis=-1)
        square_sum = butterfly_sum(square_sum, "tensor").reshape(-1, 1)
        mean_square = square_sum / model_width
        normed = own_part * lax.rsqrt(mean_square + norm_eps) * norm_gain
        normed_parts.append(normed.astype(jnp.bfloat16).reshape(chunk_lanes, row_count, -1))
    normed_lanes = jnp.concatenate(normed_parts, axis=0)
    chunk_of = rank // chunk_cap
    lane_of = old_home * chunk_cap + rank % chunk_cap
    return jnp.take(normed_lanes, chunk_of * chunk_lanes + lane_of, axis=0)


def solution(mesh):
    placed = (
        P(("groups", "dp"), None, "tensor"),
        P(("groups", "dp")),
        P(("groups", "dp")),
        P(("groups", "dp"), None, "tensor"),
        P(("groups", "dp"), None, "tensor"),
        P("tensor", None),
        P("tensor"),
    )
    return jax.shard_map(
        shards,
        mesh=mesh,
        in_specs=placed,
        out_specs=P(("groups", "dp"), None, "tensor"),
        check_vma=False,
    )
```

```python
import functools

import jax
import jax.numpy as jnp
from jax import lax
from jax.experimental import pallas as pl
from jax.experimental.pallas import tpu as pltpu
from jax.sharding import PartitionSpec as P

HEAD = 128
QHEADS = 16
KVHEADS = 8
TAG_WIDTH = 128


score_scale = 144.0 ** (-0.5)
soft_cap = 50.0
norm_eps = 1e-06


def attention_kernel(length_ref, pay_ref, cache_ref, out_ref, *, q_width):
    sessions, cache_length, _ = cache_ref.shape
    row_count = pay_ref.shape[1]
    kv_heads = cache_ref.shape[2] // (2 * HEAD)
    group_size = QHEADS // KVHEADS
    lengths = length_ref[...]
    cache_pos = lax.broadcasted_iota(jnp.int32, (sessions, group_size * row_count, cache_length), 2)
    cache_seen = cache_pos < lengths
    lane = lax.broadcasted_iota(jnp.int32, (sessions, row_count, TAG_WIDTH), 2)
    sums = jnp.zeros((sessions, row_count, TAG_WIDTH), jnp.float32)
    for k in range(kv_heads):
        key_col = 2 * HEAD * k
        grouped = jnp.concatenate(
            [pay_ref[:, :, (group_size * k + g) * HEAD:(group_size * k + g + 1) * HEAD] for g in range(group_size)],
            axis=1,
        )
        cache_keys = cache_ref[:, :, key_col:key_col + HEAD]
        cache_values = cache_ref[:, :, key_col + HEAD:key_col + 2 * HEAD]
        cache_scores = jnp.einsum("bqd,bkd->bqk", grouped, cache_keys, preferred_element_type=jnp.float32) * score_scale
        cache_w = jnp.where(cache_seen, jnp.exp(soft_cap * jnp.tanh(cache_scores / soft_cap)), 0.0)
        total = jnp.sum(cache_w, axis=-1, keepdims=True)
        mixed = jnp.einsum("bqk,bkd->bqd", cache_w.astype(jnp.bfloat16), cache_values, preferred_element_type=jnp.float32)
        mixed = (mixed / total).astype(out_ref.dtype)
        high = total.astype(jnp.bfloat16).astype(jnp.float32)
        low = total - high
        for g in range(group_size):
            head = group_size * k + g
            col = head * HEAD
            out_ref[:, :, col:col + HEAD] = mixed[:, g * row_count:(g + 1) * row_count]
            sums = jnp.where(lane == head, high[:, g * row_count:(g + 1) * row_count], sums)
            sums = jnp.where(lane == TAG_WIDTH // 2 + head, low[:, g * row_count:(g + 1) * row_count], sums)
    out_ref[:, :, q_width:q_width + TAG_WIDTH] = sums.astype(out_ref.dtype)


def attend_cache(payload, cached, lengths, q_width, block=8):
    slot_count, row_count, _ = payload.shape
    cache_length, kv_width = cached.shape[1], cached.shape[2]
    block = min(block, slot_count)
    length_col = lengths.reshape(slot_count, 1, 1)
    return pl.pallas_call(
        functools.partial(attention_kernel, q_width=q_width),
        out_shape=jax.ShapeDtypeStruct((slot_count, row_count, q_width + TAG_WIDTH), jnp.bfloat16),
        grid=(slot_count // block,),
        in_specs=[
            pl.BlockSpec((block, 1, 1), lambda b: (b, 0, 0)),
            pl.BlockSpec((block, row_count, payload.shape[2]), lambda b: (b, 0, 0)),
            pl.BlockSpec((block, cache_length, kv_width), lambda b: (b, 0, 0)),
        ],
        out_specs=pl.BlockSpec((block, row_count, q_width + TAG_WIDTH), lambda b: (b, 0, 0)),
        cost_estimate=pl.CostEstimate(
            flops=4 * slot_count * (q_width // HEAD) * row_count * cache_length * HEAD,
            transcendentals=2 * slot_count * (q_width // HEAD) * row_count * cache_length,
            bytes_accessed=int(cached.size * 2 + payload.size * 2 + slot_count * row_count * (q_width + TAG_WIDTH) * 2),
        ),
    )(length_col, payload, cached)


def fresh_kernel(q_ref, fresh_ref, mix_ref, sum_ref):
    sessions, row_count, _ = q_ref.shape
    kv_heads = fresh_ref.shape[2] // (2 * HEAD)
    group_size = QHEADS // KVHEADS
    fresh_pos = lax.broadcasted_iota(jnp.int32, (sessions, group_size * row_count, row_count), 2)
    query_row = lax.broadcasted_iota(jnp.int32, (sessions, group_size * row_count, row_count), 1) % row_count
    fresh_seen = fresh_pos <= query_row
    lane = lax.broadcasted_iota(jnp.int32, (sessions, row_count, TAG_WIDTH), 2)
    sums = jnp.zeros((sessions, row_count, TAG_WIDTH), jnp.float32)
    for k in range(kv_heads):
        key_col = 2 * HEAD * k
        grouped = jnp.concatenate(
            [q_ref[:, :, (group_size * k + g) * HEAD:(group_size * k + g + 1) * HEAD] for g in range(group_size)],
            axis=1,
        )
        fresh_keys = fresh_ref[:, :, key_col:key_col + HEAD]
        fresh_values = fresh_ref[:, :, key_col + HEAD:key_col + 2 * HEAD]
        fresh_scores = jnp.einsum("bqd,bkd->bqk", grouped, fresh_keys, preferred_element_type=jnp.float32) * score_scale
        fresh_w = jnp.where(fresh_seen, jnp.exp(soft_cap * jnp.tanh(fresh_scores / soft_cap)), 0.0)
        total = jnp.sum(fresh_w, axis=-1, keepdims=True)
        mixed = jnp.einsum("bqk,bkd->bqd", fresh_w.astype(jnp.bfloat16), fresh_values, preferred_element_type=jnp.float32)
        for g in range(group_size):
            head = group_size * k + g
            col = head * HEAD
            mix_ref[:, :, col:col + HEAD] = mixed[:, g * row_count:(g + 1) * row_count]
            sums = jnp.where(lane == head, total[:, g * row_count:(g + 1) * row_count], sums)
    sum_ref[...] = sums


def attend_fresh(queries, fresh_kv, block=8):
    slot_count, row_count, q_width = queries.shape
    kv_width = fresh_kv.shape[2]
    block = min(block, slot_count)
    return pl.pallas_call(
        fresh_kernel,
        out_shape=(
            jax.ShapeDtypeStruct((slot_count, row_count, q_width), jnp.float32),
            jax.ShapeDtypeStruct((slot_count, row_count, TAG_WIDTH), jnp.float32),
        ),
        grid=(slot_count // block,),
        in_specs=[
            pl.BlockSpec((block, row_count, q_width), lambda b: (b, 0, 0)),
            pl.BlockSpec((block, row_count, kv_width), lambda b: (b, 0, 0)),
        ],
        out_specs=(
            pl.BlockSpec((block, row_count, q_width), lambda b: (b, 0, 0)),
            pl.BlockSpec((block, row_count, TAG_WIDTH), lambda b: (b, 0, 0)),
        ),
        cost_estimate=pl.CostEstimate(
            flops=4 * slot_count * (q_width // HEAD) * row_count * row_count * HEAD,
            transcendentals=2 * slot_count * (q_width // HEAD) * row_count * row_count,
            bytes_accessed=int((queries.size + fresh_kv.size) * 2 + slot_count * row_count * (q_width + TAG_WIDTH) * 4),
        ),
    )(queries, fresh_kv)


def pack_lanes(payload, slot_lanes, lane_count):
    lane_ids = jnp.arange(lane_count, dtype=jnp.int32)
    slot_ids = jnp.arange(payload.shape[0], dtype=jnp.int32)
    lane_hits = slot_lanes[None, :] == lane_ids[:, None]
    filled = jnp.any(lane_hits, axis=1)
    chosen = jnp.sum(jnp.where(lane_hits, slot_ids[None, :], 0), axis=1)
    picked = jnp.take(payload, chosen, axis=0)
    return jnp.where(filled[:, None, None], picked, jnp.zeros((), payload.dtype))


def halving_stages(axis):
    count = lax.axis_size(axis)
    stages = count.bit_length() - 1
    return count, stages if (1 << stages) == count else None


def scatter_sum(partial, axis):
    count, stages = halving_stages(axis)
    rows, width = partial.shape
    if stages is None:
        return lax.psum_scatter(partial, axis, scatter_dimension=1, tiled=True).astype(jnp.float32)
    me = lax.axis_index(axis)
    held = partial.reshape((rows,) + (2,) * stages + (width // count,))
    for s in range(stages):
        bit = (me >> s) & 1
        dim = stages - s
        keep = lax.dynamic_index_in_dim(held, bit, axis=dim, keepdims=False)
        send = lax.dynamic_index_in_dim(held, 1 - bit, axis=dim, keepdims=False)
        got = lax.ppermute(
            send.astype(jnp.bfloat16), axis, perm=[(i, i ^ (1 << s)) for i in range(count)]
        )
        held = keep.astype(jnp.float32) + got.astype(jnp.float32)
    return held


def projection_kernel(block_ref, rows_ref, weight_ref, out_ref):
    out_ref[0] = jnp.dot(rows_ref[...], weight_ref[...], preferred_element_type=jnp.float32).astype(out_ref.dtype)


def project_blocks(rows, weight, blocks):
    row_total, inner = rows.shape
    width = weight.shape[1] // lax.axis_size("tensor")
    count = blocks.shape[0]
    return pl.pallas_call(
        projection_kernel,
        out_shape=jax.ShapeDtypeStruct((count, row_total, width), jnp.bfloat16),
        grid_spec=pltpu.PrefetchScalarGridSpec(
            num_scalar_prefetch=1,
            grid=(count,),
            in_specs=[
                pl.BlockSpec((row_total, inner), lambda j, blk: (0, 0)),
                pl.BlockSpec((inner, width), lambda j, blk: (0, blk[j])),
            ],
            out_specs=pl.BlockSpec((1, row_total, width), lambda j, blk: (j, 0, 0)),
        ),
        cost_estimate=pl.CostEstimate(
            flops=2 * count * row_total * inner * width,
            transcendentals=0,
            bytes_accessed=int(rows.size * 2 + count * (inner * width + row_total * width) * 2),
        ),
    )(blocks, rows, weight)


def bit_reversed(value, bits):
    out = 0
    for b in range(bits):
        out |= ((value >> b) & 1) << (bits - 1 - b)
    return out


def project_and_scatter(rows, weight, axis):
    count = lax.axis_size(axis)
    stages = count.bit_length() - 1
    if (1 << stages) != count or (weight.shape[1] // count) % 128:
        products = jnp.dot(rows, weight, preferred_element_type=jnp.float32).astype(jnp.bfloat16)
        return scatter_sum(products, axis)
    me = lax.axis_index(axis)
    order = jnp.array([bit_reversed(j, stages) for j in range(count)], jnp.int32)
    blocks = jnp.bitwise_xor(me, order)
    half = count // 2
    sent = project_blocks(rows, weight, blocks[half:])
    kept = project_blocks(rows, weight, blocks[:half])
    got = lax.ppermute(sent, axis, perm=[(i, i ^ 1) for i in range(count)])
    held = kept.astype(jnp.float32) + got.astype(jnp.float32)
    for s in range(1, stages):
        half = held.shape[0] // 2
        got = lax.ppermute(
            held[half:].astype(jnp.bfloat16), axis, perm=[(i, i ^ (1 << s)) for i in range(count)]
        )
        held = held[:half] + got.astype(jnp.float32)
    return held[0]


def butterfly_sum(values, axis):
    count, stages = halving_stages(axis)
    if stages is None:
        return lax.psum(values, axis)
    shape = values.shape
    lanes = 128 if values.size % 128 == 0 else values.size
    values = values.reshape(values.size // lanes, lanes)
    for s in range(stages):
        values = values + lax.ppermute(values, axis, perm=[(i, i ^ (1 << s)) for i in range(count)])
    return values.reshape(shape)


def shards(kv_cache, lengths, source, queries, fresh_kv, out_weight, norm_gain):
    dp_count = lax.axis_size("dp")
    slot_count, row_count, query_width = queries.shape
    kv_width = fresh_kv.shape[2]
    pair_cap = max(1, slot_count // dp_count)
    lane_count = dp_count * pair_cap
    slot_ids = jnp.arange(slot_count, dtype=jnp.int32)
    lane_ids = jnp.arange(lane_count, dtype=jnp.int32)

    old_home = source // slot_count
    old_slot = source % slot_count
    earlier = slot_ids[None, :] < slot_ids[:, None]
    same_home = old_home[:, None] == old_home[None, :]
    rank = jnp.sum(same_home & earlier, axis=1)
    out_lane = old_home * pair_cap + rank
    tag = jnp.broadcast_to(
        (old_slot + 1).astype(jnp.bfloat16)[:, None, None], (slot_count, row_count, TAG_WIDTH)
    )
    payload = jnp.concatenate([queries, tag], axis=2)
    sending = pack_lanes(payload, out_lane, lane_count)
    arrived = lax.all_to_all(sending, "dp", 0, 0, tiled=True)
    fresh_mix, fresh_sum = attend_fresh(queries, fresh_kv)

    lane_slot = arrived[:, 0, query_width].astype(jnp.int32) - 1
    hits = lane_slot[None, :] == slot_ids[:, None]
    slot_lane = jnp.sum(jnp.where(hits, lane_ids[None, :], 0), axis=1)
    gathered = jnp.take(arrived, slot_lane, axis=0)
    cache_part = attend_cache(gathered, kv_cache, lengths, query_width)

    filled = lane_slot >= 0
    back = jnp.take(cache_part, jnp.maximum(lane_slot, 0), axis=0)
    back = jnp.where(filled[:, None, None], back, jnp.zeros((), back.dtype))
    returned = lax.all_to_all(back, "dp", 0, 0, tiled=True)
    cache_here = jnp.take(returned, out_lane, axis=0)

    heads = query_width // HEAD
    sums = cache_here[:, :, query_width:].astype(jnp.float32)
    cache_sum = sums[:, :, :heads] + sums[:, :, TAG_WIDTH // 2:TAG_WIDTH // 2 + heads]
    total = cache_sum + fresh_sum[:, :, :heads]
    cache_mix = cache_here[:, :, :query_width].astype(jnp.float32).reshape(slot_count, row_count, heads, HEAD)
    joined = cache_mix * cache_sum[..., None] + fresh_mix.reshape(slot_count, row_count, heads, HEAD)
    attended_here = (joined / total[..., None]).astype(jnp.bfloat16).reshape(slot_count, row_count, query_width)

    row_total = slot_count * row_count
    flat_rows = attended_here.reshape(row_total, query_width)
    model_width = out_weight.shape[1]
    own_part = project_and_scatter(flat_rows, out_weight, "tensor")
    square_sum = jnp.sum(own_part * own_part, axis=-1)
    square_sum = butterfly_sum(square_sum, "tensor").reshape(row_total, 1)
    mean_square = square_sum / model_width
    normed = own_part * lax.rsqrt(mean_square + norm_eps) * norm_gain
    return normed.astype(jnp.bfloat16).reshape(slot_count, row_count, own_part.shape[1])


def solution(mesh):
    placed = (
        P(("groups", "dp"), None, "tensor"),
        P(("groups", "dp")),
        P(("groups", "dp")),
        P(("groups", "dp"), None, "tensor"),
        P(("groups", "dp"), None, "tensor"),
        P("tensor", None),
        P("tensor"),
    )
    return jax.shard_map(
        shards,
        mesh=mesh,
        in_specs=placed,
        out_specs=P(("groups", "dp"), None, "tensor"),
        check_vma=False,
    )
```

```python
import functools

import jax
import jax.numpy as jnp
from jax import lax
from jax.experimental import pallas as pl
from jax.experimental.pallas import tpu as pltpu
from jax.sharding import PartitionSpec as P

HEAD = 128
QHEADS = 16
KVHEADS = 8
TAG_WIDTH = 128


score_scale = 144.0 ** (-0.5)
soft_cap = 50.0
norm_eps = 1e-06


def attention_kernel(length_ref, pay_ref, cache_ref, out_ref, *, q_width):
    sessions, cache_length, _ = cache_ref.shape
    row_count = pay_ref.shape[1]
    kv_heads = cache_ref.shape[2] // (2 * HEAD)
    group_size = QHEADS // KVHEADS
    lengths = length_ref[...]
    cache_pos = lax.broadcasted_iota(jnp.int32, (sessions, group_size * row_count, cache_length), 2)
    cache_seen = cache_pos < lengths
    lane = lax.broadcasted_iota(jnp.int32, (sessions, row_count, TAG_WIDTH), 2)
    sums = jnp.zeros((sessions, row_count, TAG_WIDTH), jnp.float32)
    for k in range(kv_heads):
        key_col = 2 * HEAD * k
        grouped = jnp.concatenate(
            [pay_ref[:, :, (group_size * k + g) * HEAD:(group_size * k + g + 1) * HEAD] for g in range(group_size)],
            axis=1,
        )
        cache_keys = cache_ref[:, :, key_col:key_col + HEAD]
        cache_values = cache_ref[:, :, key_col + HEAD:key_col + 2 * HEAD]
        cache_scores = jnp.einsum("bqd,bkd->bqk", grouped, cache_keys, preferred_element_type=jnp.float32) * score_scale
        cache_w = jnp.where(cache_seen, jnp.exp(soft_cap * jnp.tanh(cache_scores / soft_cap)), 0.0)
        total = jnp.sum(cache_w, axis=-1, keepdims=True)
        mixed = jnp.einsum("bqk,bkd->bqd", cache_w.astype(jnp.bfloat16), cache_values, preferred_element_type=jnp.float32)
        mixed = (mixed / total).astype(out_ref.dtype)
        high = total.astype(jnp.bfloat16).astype(jnp.float32)
        low = total - high
        for g in range(group_size):
            head = group_size * k + g
            col = head * HEAD
            out_ref[:, :, col:col + HEAD] = mixed[:, g * row_count:(g + 1) * row_count]
            sums = jnp.where(lane == head, high[:, g * row_count:(g + 1) * row_count], sums)
            sums = jnp.where(lane == TAG_WIDTH // 2 + head, low[:, g * row_count:(g + 1) * row_count], sums)
    out_ref[:, :, q_width:q_width + TAG_WIDTH] = sums.astype(out_ref.dtype)


def attend_cache(payload, cached, lengths, q_width, block=8):
    slot_count, row_count, _ = payload.shape
    cache_length, kv_width = cached.shape[1], cached.shape[2]
    block = min(block, slot_count)
    length_col = lengths.reshape(slot_count, 1, 1)
    return pl.pallas_call(
        functools.partial(attention_kernel, q_width=q_width),
        out_shape=jax.ShapeDtypeStruct((slot_count, row_count, q_width + TAG_WIDTH), jnp.bfloat16),
        grid=(slot_count // block,),
        in_specs=[
            pl.BlockSpec((block, 1, 1), lambda b: (b, 0, 0)),
            pl.BlockSpec((block, row_count, payload.shape[2]), lambda b: (b, 0, 0)),
            pl.BlockSpec((block, cache_length, kv_width), lambda b: (b, 0, 0)),
        ],
        out_specs=pl.BlockSpec((block, row_count, q_width + TAG_WIDTH), lambda b: (b, 0, 0)),
        cost_estimate=pl.CostEstimate(
            flops=4 * slot_count * (q_width // HEAD) * row_count * cache_length * HEAD,
            transcendentals=2 * slot_count * (q_width // HEAD) * row_count * cache_length,
            bytes_accessed=int(cached.size * 2 + payload.size * 2 + slot_count * row_count * (q_width + TAG_WIDTH) * 2),
        ),
    )(length_col, payload, cached)


def fresh_kernel(q_ref, fresh_ref, mix_ref, sum_ref):
    sessions, row_count, _ = q_ref.shape
    kv_heads = fresh_ref.shape[2] // (2 * HEAD)
    group_size = QHEADS // KVHEADS
    fresh_pos = lax.broadcasted_iota(jnp.int32, (sessions, group_size * row_count, row_count), 2)
    query_row = lax.broadcasted_iota(jnp.int32, (sessions, group_size * row_count, row_count), 1) % row_count
    fresh_seen = fresh_pos <= query_row
    lane = lax.broadcasted_iota(jnp.int32, (sessions, row_count, TAG_WIDTH), 2)
    sums = jnp.zeros((sessions, row_count, TAG_WIDTH), jnp.float32)
    for k in range(kv_heads):
        key_col = 2 * HEAD * k
        grouped = jnp.concatenate(
            [q_ref[:, :, (group_size * k + g) * HEAD:(group_size * k + g + 1) * HEAD] for g in range(group_size)],
            axis=1,
        )
        fresh_keys = fresh_ref[:, :, key_col:key_col + HEAD]
        fresh_values = fresh_ref[:, :, key_col + HEAD:key_col + 2 * HEAD]
        fresh_scores = jnp.einsum("bqd,bkd->bqk", grouped, fresh_keys, preferred_element_type=jnp.float32) * score_scale
        fresh_w = jnp.where(fresh_seen, jnp.exp(soft_cap * jnp.tanh(fresh_scores / soft_cap)), 0.0)
        total = jnp.sum(fresh_w, axis=-1, keepdims=True)
        mixed = jnp.einsum("bqk,bkd->bqd", fresh_w.astype(jnp.bfloat16), fresh_values, preferred_element_type=jnp.float32)
        for g in range(group_size):
            head = group_size * k + g
            col = head * HEAD
            mix_ref[:, :, col:col + HEAD] = mixed[:, g * row_count:(g + 1) * row_count]
            sums = jnp.where(lane == head, total[:, g * row_count:(g + 1) * row_count], sums)
    sum_ref[...] = sums


def attend_fresh(queries, fresh_kv, block=8):
    slot_count, row_count, q_width = queries.shape
    kv_width = fresh_kv.shape[2]
    block = min(block, slot_count)
    return pl.pallas_call(
        fresh_kernel,
        out_shape=(
            jax.ShapeDtypeStruct((slot_count, row_count, q_width), jnp.float32),
            jax.ShapeDtypeStruct((slot_count, row_count, TAG_WIDTH), jnp.float32),
        ),
        grid=(slot_count // block,),
        in_specs=[
            pl.BlockSpec((block, row_count, q_width), lambda b: (b, 0, 0)),
            pl.BlockSpec((block, row_count, kv_width), lambda b: (b, 0, 0)),
        ],
        out_specs=(
            pl.BlockSpec((block, row_count, q_width), lambda b: (b, 0, 0)),
            pl.BlockSpec((block, row_count, TAG_WIDTH), lambda b: (b, 0, 0)),
        ),
        cost_estimate=pl.CostEstimate(
            flops=4 * slot_count * (q_width // HEAD) * row_count * row_count * HEAD,
            transcendentals=2 * slot_count * (q_width // HEAD) * row_count * row_count,
            bytes_accessed=int((queries.size + fresh_kv.size) * 2 + slot_count * row_count * (q_width + TAG_WIDTH) * 4),
        ),
    )(queries, fresh_kv)


def pack_lanes(payload, slot_lanes, lane_count):
    lane_ids = jnp.arange(lane_count, dtype=jnp.int32)
    slot_ids = jnp.arange(payload.shape[0], dtype=jnp.int32)
    lane_hits = slot_lanes[None, :] == lane_ids[:, None]
    filled = jnp.any(lane_hits, axis=1)
    chosen = jnp.sum(jnp.where(lane_hits, slot_ids[None, :], 0), axis=1)
    picked = jnp.take(payload, chosen, axis=0)
    return jnp.where(filled[:, None, None], picked, jnp.zeros((), payload.dtype)), chosen


def halving_stages(axis):
    count = lax.axis_size(axis)
    stages = count.bit_length() - 1
    return count, stages if (1 << stages) == count else None


def scatter_sum(partial, axis):
    count, stages = halving_stages(axis)
    rows, width = partial.shape
    if stages is None:
        return lax.psum_scatter(partial, axis, scatter_dimension=1, tiled=True).astype(jnp.float32)
    me = lax.axis_index(axis)
    held = partial.reshape((rows,) + (2,) * stages + (width // count,))
    for s in range(stages):
        bit = (me >> s) & 1
        dim = stages - s
        keep = lax.dynamic_index_in_dim(held, bit, axis=dim, keepdims=False)
        send = lax.dynamic_index_in_dim(held, 1 - bit, axis=dim, keepdims=False)
        got = lax.ppermute(
            send.astype(jnp.bfloat16), axis, perm=[(i, i ^ (1 << s)) for i in range(count)]
        )
        held = keep.astype(jnp.float32) + got.astype(jnp.float32)
    return held


def projection_kernel(block_ref, rows_ref, weight_ref, out_ref):
    out_ref[0] = jnp.dot(rows_ref[...], weight_ref[...], preferred_element_type=jnp.float32).astype(out_ref.dtype)


def project_blocks(rows, weight, blocks):
    row_total, inner = rows.shape
    width = weight.shape[1] // lax.axis_size("tensor")
    count = blocks.shape[0]
    return pl.pallas_call(
        projection_kernel,
        out_shape=jax.ShapeDtypeStruct((count, row_total, width), jnp.bfloat16),
        grid_spec=pltpu.PrefetchScalarGridSpec(
            num_scalar_prefetch=1,
            grid=(count,),
            in_specs=[
                pl.BlockSpec((row_total, inner), lambda j, blk: (0, 0)),
                pl.BlockSpec((inner, width), lambda j, blk: (0, blk[j])),
            ],
            out_specs=pl.BlockSpec((1, row_total, width), lambda j, blk: (j, 0, 0)),
        ),
        cost_estimate=pl.CostEstimate(
            flops=2 * count * row_total * inner * width,
            transcendentals=0,
            bytes_accessed=int(rows.size * 2 + count * (inner * width + row_total * width) * 2),
        ),
    )(blocks, rows, weight)


def bit_reversed(value, bits):
    out = 0
    for b in range(bits):
        out |= ((value >> b) & 1) << (bits - 1 - b)
    return out


def project_and_scatter(rows, weight, axis):
    count = lax.axis_size(axis)
    stages = count.bit_length() - 1
    if (1 << stages) != count or (weight.shape[1] // count) % 128:
        products = jnp.dot(rows, weight, preferred_element_type=jnp.float32).astype(jnp.bfloat16)
        return scatter_sum(products, axis)
    me = lax.axis_index(axis)
    order = jnp.array([bit_reversed(j, stages) for j in range(count)], jnp.int32)
    blocks = jnp.bitwise_xor(me, order)
    half = count // 2
    sent = project_blocks(rows, weight, blocks[half:])
    kept = project_blocks(rows, weight, blocks[:half])
    got = lax.ppermute(sent, axis, perm=[(i, i ^ 1) for i in range(count)])
    held = kept.astype(jnp.float32) + got.astype(jnp.float32)
    for s in range(1, stages):
        half = held.shape[0] // 2
        got = lax.ppermute(
            held[half:].astype(jnp.bfloat16), axis, perm=[(i, i ^ (1 << s)) for i in range(count)]
        )
        held = held[:half] + got.astype(jnp.float32)
    return held[0]


def butterfly_sum(values, axis):
    count, stages = halving_stages(axis)
    if stages is None:
        return lax.psum(values, axis)
    shape = values.shape
    lanes = 128 if values.size % 128 == 0 else values.size
    values = values.reshape(values.size // lanes, lanes)
    for s in range(stages):
        values = values + lax.ppermute(values, axis, perm=[(i, i ^ (1 << s)) for i in range(count)])
    return values.reshape(shape)


def finish_rows(cache_part, fresh_mix, fresh_sum, out_weight, norm_gain, query_width):
    lane_count, row_count, _ = cache_part.shape
    heads = query_width // HEAD
    model_width = out_weight.shape[1]
    sums = cache_part[:, :, query_width:].astype(jnp.float32)
    cache_sum = sums[:, :, :heads] + sums[:, :, TAG_WIDTH // 2:TAG_WIDTH // 2 + heads]
    total = cache_sum + fresh_sum[:, :, :heads]
    cache_mix = cache_part[:, :, :query_width].astype(jnp.float32).reshape(lane_count, row_count, heads, HEAD)
    joined = cache_mix * cache_sum[..., None] + fresh_mix.reshape(lane_count, row_count, heads, HEAD)
    attended = (joined / total[..., None]).astype(jnp.bfloat16).reshape(lane_count * row_count, query_width)
    own_part = project_and_scatter(attended, out_weight, "tensor")
    square_sum = jnp.sum(own_part * own_part, axis=-1)
    square_sum = butterfly_sum(square_sum, "tensor").reshape(-1, 1)
    mean_square = square_sum / model_width
    normed = own_part * lax.rsqrt(mean_square + norm_eps) * norm_gain
    return normed.astype(jnp.bfloat16).reshape(lane_count, row_count, -1)


def shards(kv_cache, lengths, source, queries, fresh_kv, out_weight, norm_gain):
    dp_count = lax.axis_size("dp")
    me = lax.axis_index("dp")
    slot_count, row_count, query_width = queries.shape
    pair_cap = max(1, slot_count // dp_count)
    lane_count = dp_count * pair_cap
    slot_ids = jnp.arange(slot_count, dtype=jnp.int32)
    lane_ids = jnp.arange(lane_count, dtype=jnp.int32)

    old_home = source // slot_count
    old_slot = source % slot_count
    earlier = slot_ids[None, :] < slot_ids[:, None]
    same_home = old_home[:, None] == old_home[None, :]
    rank = jnp.sum(same_home & earlier, axis=1)
    out_lane = old_home * pair_cap + rank
    tag = jnp.broadcast_to(
        (old_slot + 1).astype(jnp.bfloat16)[:, None, None], (slot_count, row_count, TAG_WIDTH)
    )
    payload = jnp.concatenate([queries, tag], axis=2)
    sending, lane_session = pack_lanes(payload, out_lane, lane_count)
    arrived = lax.all_to_all(sending, "dp", 0, 0, tiled=True)
    fresh_mix, fresh_sum = attend_fresh(queries, fresh_kv)

    self_lanes = lax.dynamic_slice_in_dim(sending, me * pair_cap, pair_cap, axis=0)
    self_session = lax.dynamic_slice_in_dim(lane_session, me * pair_cap, pair_cap, axis=0)
    self_slot = old_slot[self_session]
    self_part = attend_cache(self_lanes, jnp.take(kv_cache, self_slot, axis=0), lengths[self_slot], query_width)
    normed_self = finish_rows(
        self_part, fresh_mix[self_session], fresh_sum[self_session], out_weight, norm_gain, query_width
    )

    lane_slot = arrived[:, 0, query_width].astype(jnp.int32) - 1
    hits = lane_slot[None, :] == slot_ids[:, None]
    slot_lane = jnp.sum(jnp.where(hits, lane_ids[None, :], 0), axis=1)
    gathered = jnp.take(arrived, slot_lane, axis=0)
    cache_part = attend_cache(gathered, kv_cache, lengths, query_width)

    filled = lane_slot >= 0
    back = jnp.take(cache_part, jnp.maximum(lane_slot, 0), axis=0)
    back = jnp.where(filled[:, None, None], back, jnp.zeros((), back.dtype))
    returned = lax.all_to_all(back, "dp", 0, 0, tiled=True)

    other_ids = jnp.arange(lane_count - pair_cap, dtype=jnp.int32)
    other_home = other_ids // pair_cap
    other_home = other_home + (other_home >= me).astype(jnp.int32)
    other_lane = other_home * pair_cap + other_ids % pair_cap
    other_session = lane_session[other_lane]
    normed_other = finish_rows(
        jnp.take(returned, other_lane, axis=0),
        fresh_mix[other_session],
        fresh_sum[other_session],
        out_weight,
        norm_gain,
        query_width,
    )

    normed_all = jnp.concatenate([normed_self, normed_other], axis=0)
    shifted_home = old_home - (old_home > me).astype(jnp.int32)
    position = jnp.where(old_home == me, rank, pair_cap + shifted_home * pair_cap + rank)
    return jnp.take(normed_all, position, axis=0)


def solution(mesh):
    placed = (
        P(("groups", "dp"), None, "tensor"),
        P(("groups", "dp")),
        P(("groups", "dp")),
        P(("groups", "dp"), None, "tensor"),
        P(("groups", "dp"), None, "tensor"),
        P("tensor", None),
        P("tensor"),
    )
    return jax.shard_map(
        shards,
        mesh=mesh,
        in_specs=placed,
        out_specs=P(("groups", "dp"), None, "tensor"),
        check_vma=False,
    )
```

```python
import functools

import jax
import jax.numpy as jnp
from jax import lax
from jax.experimental import pallas as pl
from jax.experimental.pallas import tpu as pltpu
from jax.sharding import PartitionSpec as P

HEAD = 128
QHEADS = 16
KVHEADS = 8
TAG_WIDTH = 128


score_scale = 144.0 ** (-0.5)
soft_cap = 50.0
norm_eps = 1e-06


def attention_kernel(length_ref, pay_ref, cache_ref, out_ref, *, q_width):
    sessions, cache_length, _ = cache_ref.shape
    row_count = pay_ref.shape[1]
    kv_heads = cache_ref.shape[2] // (2 * HEAD)
    group_size = QHEADS // KVHEADS
    lengths = length_ref[...]
    cache_pos = lax.broadcasted_iota(jnp.int32, (sessions, group_size * row_count, cache_length), 2)
    cache_seen = cache_pos < lengths
    lane = lax.broadcasted_iota(jnp.int32, (sessions, row_count, TAG_WIDTH), 2)
    sums = jnp.zeros((sessions, row_count, TAG_WIDTH), jnp.float32)
    for k in range(kv_heads):
        key_col = 2 * HEAD * k
        grouped = jnp.concatenate(
            [pay_ref[:, :, (group_size * k + g) * HEAD:(group_size * k + g + 1) * HEAD] for g in range(group_size)],
            axis=1,
        )
        cache_keys = cache_ref[:, :, key_col:key_col + HEAD]
        cache_values = cache_ref[:, :, key_col + HEAD:key_col + 2 * HEAD]
        cache_scores = jnp.einsum("bqd,bkd->bqk", grouped, cache_keys, preferred_element_type=jnp.float32) * score_scale
        cache_w = jnp.where(cache_seen, jnp.exp(soft_cap * jnp.tanh(cache_scores / soft_cap)), 0.0)
        total = jnp.sum(cache_w, axis=-1, keepdims=True)
        mixed = jnp.einsum("bqk,bkd->bqd", cache_w.astype(jnp.bfloat16), cache_values, preferred_element_type=jnp.float32)
        mixed = (mixed / total).astype(out_ref.dtype)
        high = total.astype(jnp.bfloat16).astype(jnp.float32)
        low = total - high
        for g in range(group_size):
            head = group_size * k + g
            col = head * HEAD
            out_ref[:, :, col:col + HEAD] = mixed[:, g * row_count:(g + 1) * row_count]
            sums = jnp.where(lane == head, high[:, g * row_count:(g + 1) * row_count], sums)
            sums = jnp.where(lane == TAG_WIDTH // 2 + head, low[:, g * row_count:(g + 1) * row_count], sums)
    out_ref[:, :, q_width:q_width + TAG_WIDTH] = sums.astype(out_ref.dtype)


def attend_cache(payload, cached, lengths, q_width, block=8):
    slot_count, row_count, _ = payload.shape
    cache_length, kv_width = cached.shape[1], cached.shape[2]
    block = min(block, slot_count)
    length_col = lengths.reshape(slot_count, 1, 1)
    return pl.pallas_call(
        functools.partial(attention_kernel, q_width=q_width),
        out_shape=jax.ShapeDtypeStruct((slot_count, row_count, q_width + TAG_WIDTH), jnp.bfloat16),
        grid=(slot_count // block,),
        in_specs=[
            pl.BlockSpec((block, 1, 1), lambda b: (b, 0, 0)),
            pl.BlockSpec((block, row_count, payload.shape[2]), lambda b: (b, 0, 0)),
            pl.BlockSpec((block, cache_length, kv_width), lambda b: (b, 0, 0)),
        ],
        out_specs=pl.BlockSpec((block, row_count, q_width + TAG_WIDTH), lambda b: (b, 0, 0)),
        cost_estimate=pl.CostEstimate(
            flops=4 * slot_count * (q_width // HEAD) * row_count * cache_length * HEAD,
            transcendentals=2 * slot_count * (q_width // HEAD) * row_count * cache_length,
            bytes_accessed=int(cached.size * 2 + payload.size * 2 + slot_count * row_count * (q_width + TAG_WIDTH) * 2),
        ),
    )(length_col, payload, cached)


def fresh_kernel(q_ref, fresh_ref, mix_ref, sum_ref):
    sessions, row_count, _ = q_ref.shape
    kv_heads = fresh_ref.shape[2] // (2 * HEAD)
    group_size = QHEADS // KVHEADS
    fresh_pos = lax.broadcasted_iota(jnp.int32, (sessions, group_size * row_count, row_count), 2)
    query_row = lax.broadcasted_iota(jnp.int32, (sessions, group_size * row_count, row_count), 1) % row_count
    fresh_seen = fresh_pos <= query_row
    lane = lax.broadcasted_iota(jnp.int32, (sessions, row_count, TAG_WIDTH), 2)
    sums = jnp.zeros((sessions, row_count, TAG_WIDTH), jnp.float32)
    for k in range(kv_heads):
        key_col = 2 * HEAD * k
        grouped = jnp.concatenate(
            [q_ref[:, :, (group_size * k + g) * HEAD:(group_size * k + g + 1) * HEAD] for g in range(group_size)],
            axis=1,
        )
        fresh_keys = fresh_ref[:, :, key_col:key_col + HEAD]
        fresh_values = fresh_ref[:, :, key_col + HEAD:key_col + 2 * HEAD]
        fresh_scores = jnp.einsum("bqd,bkd->bqk", grouped, fresh_keys, preferred_element_type=jnp.float32) * score_scale
        fresh_w = jnp.where(fresh_seen, jnp.exp(soft_cap * jnp.tanh(fresh_scores / soft_cap)), 0.0)
        total = jnp.sum(fresh_w, axis=-1, keepdims=True)
        mixed = jnp.einsum("bqk,bkd->bqd", fresh_w.astype(jnp.bfloat16), fresh_values, preferred_element_type=jnp.float32)
        for g in range(group_size):
            head = group_size * k + g
            col = head * HEAD
            mix_ref[:, :, col:col + HEAD] = mixed[:, g * row_count:(g + 1) * row_count]
            sums = jnp.where(lane == head, total[:, g * row_count:(g + 1) * row_count], sums)
    sum_ref[...] = sums


def attend_fresh(queries, fresh_kv, block=8):
    slot_count, row_count, q_width = queries.shape
    kv_width = fresh_kv.shape[2]
    block = min(block, slot_count)
    return pl.pallas_call(
        fresh_kernel,
        out_shape=(
            jax.ShapeDtypeStruct((slot_count, row_count, q_width), jnp.float32),
            jax.ShapeDtypeStruct((slot_count, row_count, TAG_WIDTH), jnp.float32),
        ),
        grid=(slot_count // block,),
        in_specs=[
            pl.BlockSpec((block, row_count, q_width), lambda b: (b, 0, 0)),
            pl.BlockSpec((block, row_count, kv_width), lambda b: (b, 0, 0)),
        ],
        out_specs=(
            pl.BlockSpec((block, row_count, q_width), lambda b: (b, 0, 0)),
            pl.BlockSpec((block, row_count, TAG_WIDTH), lambda b: (b, 0, 0)),
        ),
        cost_estimate=pl.CostEstimate(
            flops=4 * slot_count * (q_width // HEAD) * row_count * row_count * HEAD,
            transcendentals=2 * slot_count * (q_width // HEAD) * row_count * row_count,
            bytes_accessed=int((queries.size + fresh_kv.size) * 2 + slot_count * row_count * (q_width + TAG_WIDTH) * 4),
        ),
    )(queries, fresh_kv)


def pack_lanes(payload, slot_lanes, lane_count):
    lane_ids = jnp.arange(lane_count, dtype=jnp.int32)
    slot_ids = jnp.arange(payload.shape[0], dtype=jnp.int32)
    lane_hits = slot_lanes[None, :] == lane_ids[:, None]
    chosen = jnp.sum(jnp.where(lane_hits, slot_ids[None, :], 0), axis=1)
    return jnp.take(payload, chosen, axis=0)


def halving_stages(axis):
    count = lax.axis_size(axis)
    stages = count.bit_length() - 1
    return count, stages if (1 << stages) == count else None


def scatter_sum(partial, axis):
    count, stages = halving_stages(axis)
    rows, width = partial.shape
    if stages is None:
        return lax.psum_scatter(partial, axis, scatter_dimension=1, tiled=True).astype(jnp.float32)
    me = lax.axis_index(axis)
    held = partial.reshape((rows,) + (2,) * stages + (width // count,))
    for s in range(stages):
        bit = (me >> s) & 1
        dim = stages - s
        keep = lax.dynamic_index_in_dim(held, bit, axis=dim, keepdims=False)
        send = lax.dynamic_index_in_dim(held, 1 - bit, axis=dim, keepdims=False)
        got = lax.ppermute(
            send.astype(jnp.bfloat16), axis, perm=[(i, i ^ (1 << s)) for i in range(count)]
        )
        held = keep.astype(jnp.float32) + got.astype(jnp.float32)
    return held


def projection_kernel(block_ref, rows_ref, weight_ref, out_ref):
    out_ref[0] = jnp.dot(rows_ref[...], weight_ref[...], preferred_element_type=jnp.float32).astype(out_ref.dtype)


def project_blocks(rows, weight, blocks, row_tile=256):
    row_total, inner = rows.shape
    width = weight.shape[1] // lax.axis_size("tensor")
    count = blocks.shape[0]
    row_tile = row_tile if row_total % row_tile == 0 else row_total
    return pl.pallas_call(
        projection_kernel,
        out_shape=jax.ShapeDtypeStruct((count, row_total, width), jnp.bfloat16),
        grid_spec=pltpu.PrefetchScalarGridSpec(
            num_scalar_prefetch=1,
            grid=(count, row_total // row_tile),
            in_specs=[
                pl.BlockSpec((row_tile, inner), lambda j, i, blk: (i, 0)),
                pl.BlockSpec((inner, width), lambda j, i, blk: (0, blk[j])),
            ],
            out_specs=pl.BlockSpec((1, row_tile, width), lambda j, i, blk: (j, i, 0)),
        ),
        cost_estimate=pl.CostEstimate(
            flops=2 * count * row_total * inner * width,
            transcendentals=0,
            bytes_accessed=int(rows.size * 2 + count * (inner * width + row_total * width) * 2),
        ),
    )(blocks, rows, weight)


def bit_reversed(value, bits):
    out = 0
    for b in range(bits):
        out |= ((value >> b) & 1) << (bits - 1 - b)
    return out


def project_and_scatter(rows, weight, axis):
    count = lax.axis_size(axis)
    stages = count.bit_length() - 1
    if (1 << stages) != count or (weight.shape[1] // count) % 128:
        products = jnp.dot(rows, weight, preferred_element_type=jnp.float32).astype(jnp.bfloat16)
        return scatter_sum(products, axis)
    me = lax.axis_index(axis)
    order = jnp.array([bit_reversed(j, stages) for j in range(count)], jnp.int32)
    blocks = jnp.bitwise_xor(me, order)
    half = count // 2
    sent = project_blocks(rows, weight, blocks[half:])
    kept = project_blocks(rows, weight, blocks[:half])
    got = lax.ppermute(sent, axis, perm=[(i, i ^ 1) for i in range(count)])
    held = kept.astype(jnp.float32) + got.astype(jnp.float32)
    for s in range(1, stages):
        half = held.shape[0] // 2
        got = lax.ppermute(
            held[half:].astype(jnp.bfloat16), axis, perm=[(i, i ^ (1 << s)) for i in range(count)]
        )
        held = held[:half] + got.astype(jnp.float32)
    return held[0]


def butterfly_sum(values, axis):
    count, stages = halving_stages(axis)
    if stages is None:
        return lax.psum(values, axis)
    shape = values.shape
    lanes = 128 if values.size % 128 == 0 else values.size
    values = values.reshape(values.size // lanes, lanes)
    for s in range(stages):
        values = values + lax.ppermute(values, axis, perm=[(i, i ^ (1 << s)) for i in range(count)])
    return values.reshape(shape)


def shards(kv_cache, lengths, source, queries, fresh_kv, out_weight, norm_gain):
    dp_count = lax.axis_size("dp")
    slot_count, row_count, query_width = queries.shape
    kv_width = fresh_kv.shape[2]
    pair_cap = max(1, slot_count // dp_count)
    lane_count = dp_count * pair_cap
    slot_ids = jnp.arange(slot_count, dtype=jnp.int32)
    lane_ids = jnp.arange(lane_count, dtype=jnp.int32)

    old_home = source // slot_count
    old_slot = source % slot_count
    earlier = slot_ids[None, :] < slot_ids[:, None]
    same_home = old_home[:, None] == old_home[None, :]
    rank = jnp.sum(same_home & earlier, axis=1)
    out_lane = old_home * pair_cap + rank
    tag = jnp.broadcast_to(
        (old_slot + 1).astype(jnp.bfloat16)[:, None, None], (slot_count, row_count, TAG_WIDTH)
    )
    payload = jnp.concatenate([queries, tag], axis=2)
    sending = pack_lanes(payload, out_lane, lane_count)
    arrived = lax.all_to_all(sending, "dp", 0, 0, tiled=True)
    fresh_mix, fresh_sum = attend_fresh(queries, fresh_kv)

    lane_slot = arrived[:, 0, query_width].astype(jnp.int32) - 1
    hits = lane_slot[None, :] == slot_ids[:, None]
    slot_lane = jnp.sum(jnp.where(hits, lane_ids[None, :], 0), axis=1)
    gathered = jnp.take(arrived, slot_lane, axis=0)
    cache_part = attend_cache(gathered, kv_cache, lengths, query_width)

    back = jnp.take(cache_part, jnp.clip(lane_slot, 0, slot_count - 1), axis=0)
    returned = lax.all_to_all(back, "dp", 0, 0, tiled=True)
    cache_here = jnp.take(returned, out_lane, axis=0)

    heads = query_width // HEAD
    sums = cache_here[:, :, query_width:].astype(jnp.float32)
    cache_sum = sums[:, :, :heads] + sums[:, :, TAG_WIDTH // 2:TAG_WIDTH // 2 + heads]
    total = cache_sum + fresh_sum[:, :, :heads]
    cache_mix = cache_here[:, :, :query_width].astype(jnp.float32).reshape(slot_count, row_count, heads, HEAD)
    joined = cache_mix * cache_sum[..., None] + fresh_mix.reshape(slot_count, row_count, heads, HEAD)
    attended_here = (joined / total[..., None]).astype(jnp.bfloat16).reshape(slot_count, row_count, query_width)

    row_total = slot_count * row_count
    flat_rows = attended_here.reshape(row_total, query_width)
    model_width = out_weight.shape[1]
    own_part = project_and_scatter(flat_rows, out_weight, "tensor")
    square_sum = jnp.sum(own_part * own_part, axis=-1)
    square_sum = butterfly_sum(square_sum, "tensor").reshape(row_total, 1)
    mean_square = square_sum / model_width
    normed = own_part * lax.rsqrt(mean_square + norm_eps) * norm_gain
    return normed.astype(jnp.bfloat16).reshape(slot_count, row_count, own_part.shape[1])


def solution(mesh):
    placed = (
        P(("groups", "dp"), None, "tensor"),
        P(("groups", "dp")),
        P(("groups", "dp")),
        P(("groups", "dp"), None, "tensor"),
        P(("groups", "dp"), None, "tensor"),
        P("tensor", None),
        P("tensor"),
    )
    return jax.shard_map(
        shards,
        mesh=mesh,
        in_specs=placed,
        out_specs=P(("groups", "dp"), None, "tensor"),
        check_vma=False,
    )
```

```python
import functools

import jax
import jax.numpy as jnp
from jax import lax
from jax.experimental import pallas as pl
from jax.experimental.pallas import tpu as pltpu
from jax.sharding import PartitionSpec as P

HEAD = 128
QHEADS = 16
KVHEADS = 8
TAG_WIDTH = 128


score_scale = 144.0 ** (-0.5)
soft_cap = 50.0
norm_eps = 1e-06


def attention_kernel(length_ref, pay_ref, cache_ref, out_ref, *, q_width):
    sessions, cache_length, _ = cache_ref.shape
    row_count = pay_ref.shape[1]
    kv_heads = cache_ref.shape[2] // (2 * HEAD)
    group_size = QHEADS // KVHEADS
    lengths = length_ref[...]
    cache_pos = lax.broadcasted_iota(jnp.int32, (sessions, group_size * row_count, cache_length), 2)
    cache_seen = cache_pos < lengths
    lane = lax.broadcasted_iota(jnp.int32, (sessions, row_count, TAG_WIDTH), 2)
    sums = jnp.zeros((sessions, row_count, TAG_WIDTH), jnp.float32)
    for k in range(kv_heads):
        key_col = 2 * HEAD * k
        grouped = jnp.concatenate(
            [pay_ref[:, :, (group_size * k + g) * HEAD:(group_size * k + g + 1) * HEAD] for g in range(group_size)],
            axis=1,
        )
        cache_keys = cache_ref[:, :, key_col:key_col + HEAD]
        cache_values = cache_ref[:, :, key_col + HEAD:key_col + 2 * HEAD]
        cache_scores = jnp.einsum("bqd,bkd->bqk", grouped, cache_keys, preferred_element_type=jnp.float32) * score_scale
        cache_w = jnp.where(cache_seen, jnp.exp(soft_cap * jnp.tanh(cache_scores / soft_cap)), 0.0)
        total = jnp.sum(cache_w, axis=-1, keepdims=True)
        mixed = jnp.einsum("bqk,bkd->bqd", cache_w.astype(jnp.bfloat16), cache_values, preferred_element_type=jnp.float32)
        mixed = (mixed / total).astype(out_ref.dtype)
        high = total.astype(jnp.bfloat16).astype(jnp.float32)
        low = total - high
        for g in range(group_size):
            head = group_size * k + g
            col = head * HEAD
            out_ref[:, :, col:col + HEAD] = mixed[:, g * row_count:(g + 1) * row_count]
            sums = jnp.where(lane == head, high[:, g * row_count:(g + 1) * row_count], sums)
            sums = jnp.where(lane == TAG_WIDTH // 2 + head, low[:, g * row_count:(g + 1) * row_count], sums)
    out_ref[:, :, q_width:q_width + TAG_WIDTH] = sums.astype(out_ref.dtype)


def attend_cache(payload, cached, lengths, q_width, block=8):
    slot_count, row_count, _ = payload.shape
    cache_length, kv_width = cached.shape[1], cached.shape[2]
    block = min(block, slot_count)
    length_col = lengths.reshape(slot_count, 1, 1)
    return pl.pallas_call(
        functools.partial(attention_kernel, q_width=q_width),
        out_shape=jax.ShapeDtypeStruct((slot_count, row_count, q_width + TAG_WIDTH), jnp.bfloat16),
        grid=(slot_count // block,),
        in_specs=[
            pl.BlockSpec((block, 1, 1), lambda b: (b, 0, 0)),
            pl.BlockSpec((block, row_count, payload.shape[2]), lambda b: (b, 0, 0)),
            pl.BlockSpec((block, cache_length, kv_width), lambda b: (b, 0, 0)),
        ],
        out_specs=pl.BlockSpec((block, row_count, q_width + TAG_WIDTH), lambda b: (b, 0, 0)),
        cost_estimate=pl.CostEstimate(
            flops=4 * slot_count * (q_width // HEAD) * row_count * cache_length * HEAD,
            transcendentals=2 * slot_count * (q_width // HEAD) * row_count * cache_length,
            bytes_accessed=int(cached.size * 2 + payload.size * 2 + slot_count * row_count * (q_width + TAG_WIDTH) * 2),
        ),
    )(length_col, payload, cached)


def fresh_kernel(q_ref, fresh_ref, mix_ref, sum_ref):
    sessions, row_count, _ = q_ref.shape
    kv_heads = fresh_ref.shape[2] // (2 * HEAD)
    group_size = QHEADS // KVHEADS
    fresh_pos = lax.broadcasted_iota(jnp.int32, (sessions, group_size * row_count, row_count), 2)
    query_row = lax.broadcasted_iota(jnp.int32, (sessions, group_size * row_count, row_count), 1) % row_count
    fresh_seen = fresh_pos <= query_row
    lane = lax.broadcasted_iota(jnp.int32, (sessions, row_count, TAG_WIDTH), 2)
    sums = jnp.zeros((sessions, row_count, TAG_WIDTH), jnp.float32)
    for k in range(kv_heads):
        key_col = 2 * HEAD * k
        grouped = jnp.concatenate(
            [q_ref[:, :, (group_size * k + g) * HEAD:(group_size * k + g + 1) * HEAD] for g in range(group_size)],
            axis=1,
        )
        fresh_keys = fresh_ref[:, :, key_col:key_col + HEAD]
        fresh_values = fresh_ref[:, :, key_col + HEAD:key_col + 2 * HEAD]
        fresh_scores = jnp.einsum("bqd,bkd->bqk", grouped, fresh_keys, preferred_element_type=jnp.float32) * score_scale
        fresh_w = jnp.where(fresh_seen, jnp.exp(soft_cap * jnp.tanh(fresh_scores / soft_cap)), 0.0)
        total = jnp.sum(fresh_w, axis=-1, keepdims=True)
        mixed = jnp.einsum("bqk,bkd->bqd", fresh_w.astype(jnp.bfloat16), fresh_values, preferred_element_type=jnp.float32)
        for g in range(group_size):
            head = group_size * k + g
            col = head * HEAD
            mix_ref[:, :, col:col + HEAD] = mixed[:, g * row_count:(g + 1) * row_count]
            sums = jnp.where(lane == head, total[:, g * row_count:(g + 1) * row_count], sums)
    sum_ref[...] = sums


def attend_fresh(queries, fresh_kv, block=8):
    slot_count, row_count, q_width = queries.shape
    kv_width = fresh_kv.shape[2]
    block = min(block, slot_count)
    return pl.pallas_call(
        fresh_kernel,
        out_shape=(
            jax.ShapeDtypeStruct((slot_count, row_count, q_width), jnp.float32),
            jax.ShapeDtypeStruct((slot_count, row_count, TAG_WIDTH), jnp.float32),
        ),
        grid=(slot_count // block,),
        in_specs=[
            pl.BlockSpec((block, row_count, q_width), lambda b: (b, 0, 0)),
            pl.BlockSpec((block, row_count, kv_width), lambda b: (b, 0, 0)),
        ],
        out_specs=(
            pl.BlockSpec((block, row_count, q_width), lambda b: (b, 0, 0)),
            pl.BlockSpec((block, row_count, TAG_WIDTH), lambda b: (b, 0, 0)),
        ),
        cost_estimate=pl.CostEstimate(
            flops=4 * slot_count * (q_width // HEAD) * row_count * row_count * HEAD,
            transcendentals=2 * slot_count * (q_width // HEAD) * row_count * row_count,
            bytes_accessed=int((queries.size + fresh_kv.size) * 2 + slot_count * row_count * (q_width + TAG_WIDTH) * 4),
        ),
    )(queries, fresh_kv)


def pack_lanes(payload, slot_lanes, lane_count):
    lane_ids = jnp.arange(lane_count, dtype=jnp.int32)
    slot_ids = jnp.arange(payload.shape[0], dtype=jnp.int32)
    lane_hits = slot_lanes[None, :] == lane_ids[:, None]
    filled = jnp.any(lane_hits, axis=1)
    chosen = jnp.sum(jnp.where(lane_hits, slot_ids[None, :], 0), axis=1)
    picked = jnp.take(payload, chosen, axis=0)
    return jnp.where(filled[:, None, None], picked, jnp.zeros((), payload.dtype))


def halving_stages(axis):
    count = lax.axis_size(axis)
    stages = count.bit_length() - 1
    return count, stages if (1 << stages) == count else None


def scatter_sum(partial, axis):
    count, stages = halving_stages(axis)
    rows, width = partial.shape
    if stages is None:
        return lax.psum_scatter(partial, axis, scatter_dimension=1, tiled=True).astype(jnp.float32)
    me = lax.axis_index(axis)
    held = partial.reshape((rows,) + (2,) * stages + (width // count,))
    for s in range(stages):
        bit = (me >> s) & 1
        dim = stages - s
        keep = lax.dynamic_index_in_dim(held, bit, axis=dim, keepdims=False)
        send = lax.dynamic_index_in_dim(held, 1 - bit, axis=dim, keepdims=False)
        got = lax.ppermute(
            send.astype(jnp.bfloat16), axis, perm=[(i, i ^ (1 << s)) for i in range(count)]
        )
        held = keep.astype(jnp.float32) + got.astype(jnp.float32)
    return held


def projection_kernel(block_ref, rows_ref, weight_ref, out_ref):
    out_ref[0] = jnp.dot(rows_ref[...], weight_ref[...], preferred_element_type=jnp.float32).astype(out_ref.dtype)


def project_blocks(rows, weight, blocks):
    row_total, inner = rows.shape
    width = weight.shape[1] // lax.axis_size("tensor")
    count = blocks.shape[0]
    return pl.pallas_call(
        projection_kernel,
        out_shape=jax.ShapeDtypeStruct((count, row_total, width), jnp.bfloat16),
        grid_spec=pltpu.PrefetchScalarGridSpec(
            num_scalar_prefetch=1,
            grid=(count,),
            in_specs=[
                pl.BlockSpec((row_total, inner), lambda j, blk: (0, 0)),
                pl.BlockSpec((inner, width), lambda j, blk: (0, blk[j])),
            ],
            out_specs=pl.BlockSpec((1, row_total, width), lambda j, blk: (j, 0, 0)),
        ),
        cost_estimate=pl.CostEstimate(
            flops=2 * count * row_total * inner * width,
            transcendentals=0,
            bytes_accessed=int(rows.size * 2 + count * (inner * width + row_total * width) * 2),
        ),
    )(blocks, rows, weight)


def bit_reversed(value, bits):
    out = 0
    for b in range(bits):
        out |= ((value >> b) & 1) << (bits - 1 - b)
    return out


def project_and_scatter(rows, weight, axis):
    count = lax.axis_size(axis)
    stages = count.bit_length() - 1
    if (1 << stages) != count or (weight.shape[1] // count) % 128:
        products = jnp.dot(rows, weight, preferred_element_type=jnp.float32).astype(jnp.bfloat16)
        return scatter_sum(products, axis)
    me = lax.axis_index(axis)
    order = jnp.array([bit_reversed(j, stages) for j in range(count)], jnp.int32)
    blocks = jnp.bitwise_xor(me, order)
    half = count // 2
    sent = project_blocks(rows, weight, blocks[half:])
    kept = project_blocks(rows, weight, blocks[:half])
    got = lax.ppermute(sent, axis, perm=[(i, i ^ 1) for i in range(count)])
    held = kept.astype(jnp.float32) + got.astype(jnp.float32)
    for s in range(1, stages):
        half = held.shape[0] // 2
        got = lax.ppermute(
            held[half:].astype(jnp.bfloat16), axis, perm=[(i, i ^ (1 << s)) for i in range(count)]
        )
        held = held[:half] + got.astype(jnp.float32)
    return held[0]


def butterfly_sum(values, axis):
    count, stages = halving_stages(axis)
    if stages is None:
        return lax.psum(values, axis)
    shape = values.shape
    lanes = 128 if values.size % 128 == 0 else values.size
    values = values.reshape(values.size // lanes, lanes)
    for s in range(stages):
        values = values + lax.ppermute(values, axis, perm=[(i, i ^ (1 << s)) for i in range(count)])
    return values.reshape(shape)


def exchange_by_shift(lanes, axis, cap, direction):
    count = lax.axis_size(axis)
    parts = [lanes[:cap]]
    for shift in range(1, count):
        parts.append(
            lax.ppermute(
                lanes[shift * cap:(shift + 1) * cap],
                axis,
                perm=[(i, (i + direction * shift) % count) for i in range(count)],
            )
        )
    return jnp.concatenate(parts, axis=0)


def shards(kv_cache, lengths, source, queries, fresh_kv, out_weight, norm_gain):
    dp_count = lax.axis_size("dp")
    me = lax.axis_index("dp")
    slot_count, row_count, query_width = queries.shape
    kv_width = fresh_kv.shape[2]
    pair_cap = max(1, slot_count // dp_count)
    lane_count = dp_count * pair_cap
    slot_ids = jnp.arange(slot_count, dtype=jnp.int32)
    lane_ids = jnp.arange(lane_count, dtype=jnp.int32)

    old_home = source // slot_count
    old_slot = source % slot_count
    earlier = slot_ids[None, :] < slot_ids[:, None]
    same_home = old_home[:, None] == old_home[None, :]
    rank = jnp.sum(same_home & earlier, axis=1)
    shift = (old_home - me) % dp_count
    out_lane = shift * pair_cap + rank
    tag = jnp.broadcast_to(
        (old_slot + 1).astype(jnp.bfloat16)[:, None, None], (slot_count, row_count, TAG_WIDTH)
    )
    payload = jnp.concatenate([queries, tag], axis=2)
    sending = pack_lanes(payload, out_lane, lane_count)
    arrived = exchange_by_shift(sending, "dp", pair_cap, 1)
    fresh_mix, fresh_sum = attend_fresh(queries, fresh_kv)

    lane_slot = arrived[:, 0, query_width].astype(jnp.int32) - 1
    hits = lane_slot[None, :] == slot_ids[:, None]
    slot_lane = jnp.sum(jnp.where(hits, lane_ids[None, :], 0), axis=1)
    gathered = jnp.take(arrived, slot_lane, axis=0)
    cache_part = attend_cache(gathered, kv_cache, lengths, query_width)

    filled = lane_slot >= 0
    back = jnp.take(cache_part, jnp.maximum(lane_slot, 0), axis=0)
    back = jnp.where(filled[:, None, None], back, jnp.zeros((), back.dtype))
    returned = exchange_by_shift(back, "dp", pair_cap, -1)
    cache_here = jnp.take(returned, out_lane, axis=0)

    heads = query_width // HEAD
    sums = cache_here[:, :, query_width:].astype(jnp.float32)
    cache_sum = sums[:, :, :heads] + sums[:, :, TAG_WIDTH // 2:TAG_WIDTH // 2 + heads]
    total = cache_sum + fresh_sum[:, :, :heads]
    cache_mix = cache_here[:, :, :query_width].astype(jnp.float32).reshape(slot_count, row_count, heads, HEAD)
    joined = cache_mix * cache_sum[..., None] + fresh_mix.reshape(slot_count, row_count, heads, HEAD)
    attended_here = (joined / total[..., None]).astype(jnp.bfloat16).reshape(slot_count, row_count, query_width)

    row_total = slot_count * row_count
    flat_rows = attended_here.reshape(row_total, query_width)
    model_width = out_weight.shape[1]
    own_part = project_and_scatter(flat_rows, out_weight, "tensor")
    square_sum = jnp.sum(own_part * own_part, axis=-1)
    square_sum = butterfly_sum(square_sum, "tensor").reshape(row_total, 1)
    mean_square = square_sum / model_width
    normed = own_part * lax.rsqrt(mean_square + norm_eps) * norm_gain
    return normed.astype(jnp.bfloat16).reshape(slot_count, row_count, own_part.shape[1])


def solution(mesh):
    placed = (
        P(("groups", "dp"), None, "tensor"),
        P(("groups", "dp")),
        P(("groups", "dp")),
        P(("groups", "dp"), None, "tensor"),
        P(("groups", "dp"), None, "tensor"),
        P("tensor", None),
        P("tensor"),
    )
    return jax.shard_map(
        shards,
        mesh=mesh,
        in_specs=placed,
        out_specs=P(("groups", "dp"), None, "tensor"),
        check_vma=False,
    )
```

```python
import functools

import jax
import jax.numpy as jnp
from jax import lax
from jax.experimental import pallas as pl
from jax.experimental.pallas import tpu as pltpu
from jax.sharding import PartitionSpec as P

HEAD = 128
QHEADS = 16
KVHEADS = 8
TAG_WIDTH = 128


score_scale = 144.0 ** (-0.5)
soft_cap = 50.0
norm_eps = 1e-06


def attention_kernel(length_ref, pay_ref, cache_ref, out_ref, *, q_width):
    sessions, cache_length, _ = cache_ref.shape
    row_count = pay_ref.shape[1]
    kv_heads = cache_ref.shape[2] // (2 * HEAD)
    group_size = QHEADS // KVHEADS
    lengths = length_ref[...]
    cache_pos = lax.broadcasted_iota(jnp.int32, (sessions, group_size * row_count, cache_length), 2)
    cache_seen = cache_pos < lengths
    lane = lax.broadcasted_iota(jnp.int32, (sessions, row_count, TAG_WIDTH), 2)
    sums = jnp.zeros((sessions, row_count, TAG_WIDTH), jnp.float32)
    for k in range(kv_heads):
        key_col = 2 * HEAD * k
        grouped = jnp.concatenate(
            [pay_ref[:, :, (group_size * k + g) * HEAD:(group_size * k + g + 1) * HEAD] for g in range(group_size)],
            axis=1,
        )
        cache_keys = cache_ref[:, :, key_col:key_col + HEAD]
        cache_values = cache_ref[:, :, key_col + HEAD:key_col + 2 * HEAD]
        cache_scores = jnp.einsum("bqd,bkd->bqk", grouped, cache_keys, preferred_element_type=jnp.float32) * score_scale
        cache_w = jnp.where(cache_seen, jnp.exp(soft_cap * jnp.tanh(cache_scores / soft_cap)), 0.0)
        total = jnp.sum(cache_w, axis=-1, keepdims=True)
        mixed = jnp.einsum("bqk,bkd->bqd", cache_w.astype(jnp.bfloat16), cache_values, preferred_element_type=jnp.float32)
        mixed = (mixed / total).astype(out_ref.dtype)
        high = total.astype(jnp.bfloat16).astype(jnp.float32)
        low = total - high
        for g in range(group_size):
            head = group_size * k + g
            col = head * HEAD
            out_ref[:, :, col:col + HEAD] = mixed[:, g * row_count:(g + 1) * row_count]
            sums = jnp.where(lane == head, high[:, g * row_count:(g + 1) * row_count], sums)
            sums = jnp.where(lane == TAG_WIDTH // 2 + head, low[:, g * row_count:(g + 1) * row_count], sums)
    out_ref[:, :, q_width:q_width + TAG_WIDTH] = sums.astype(out_ref.dtype)


def attend_cache(payload, cached, lengths, q_width, block=8):
    slot_count, row_count, _ = payload.shape
    cache_length, kv_width = cached.shape[1], cached.shape[2]
    block = min(block, slot_count)
    length_col = lengths.reshape(slot_count, 1, 1)
    return pl.pallas_call(
        functools.partial(attention_kernel, q_width=q_width),
        out_shape=jax.ShapeDtypeStruct((slot_count, row_count, q_width + TAG_WIDTH), jnp.bfloat16),
        grid=(slot_count // block,),
        in_specs=[
            pl.BlockSpec((block, 1, 1), lambda b: (b, 0, 0)),
            pl.BlockSpec((block, row_count, payload.shape[2]), lambda b: (b, 0, 0)),
            pl.BlockSpec((block, cache_length, kv_width), lambda b: (b, 0, 0)),
        ],
        out_specs=pl.BlockSpec((block, row_count, q_width + TAG_WIDTH), lambda b: (b, 0, 0)),
        cost_estimate=pl.CostEstimate(
            flops=4 * slot_count * (q_width // HEAD) * row_count * cache_length * HEAD,
            transcendentals=2 * slot_count * (q_width // HEAD) * row_count * cache_length,
            bytes_accessed=int(cached.size * 2 + payload.size * 2 + slot_count * row_count * (q_width + TAG_WIDTH) * 2),
        ),
    )(length_col, payload, cached)


def fresh_kernel(q_ref, fresh_ref, mix_ref, sum_ref):
    sessions, row_count, _ = q_ref.shape
    kv_heads = fresh_ref.shape[2] // (2 * HEAD)
    group_size = QHEADS // KVHEADS
    fresh_pos = lax.broadcasted_iota(jnp.int32, (sessions, group_size * row_count, row_count), 2)
    query_row = lax.broadcasted_iota(jnp.int32, (sessions, group_size * row_count, row_count), 1) % row_count
    fresh_seen = fresh_pos <= query_row
    lane = lax.broadcasted_iota(jnp.int32, (sessions, row_count, TAG_WIDTH), 2)
    sums = jnp.zeros((sessions, row_count, TAG_WIDTH), jnp.float32)
    for k in range(kv_heads):
        key_col = 2 * HEAD * k
        grouped = jnp.concatenate(
            [q_ref[:, :, (group_size * k + g) * HEAD:(group_size * k + g + 1) * HEAD] for g in range(group_size)],
            axis=1,
        )
        fresh_keys = fresh_ref[:, :, key_col:key_col + HEAD]
        fresh_values = fresh_ref[:, :, key_col + HEAD:key_col + 2 * HEAD]
        fresh_scores = jnp.einsum("bqd,bkd->bqk", grouped, fresh_keys, preferred_element_type=jnp.float32) * score_scale
        fresh_w = jnp.where(fresh_seen, jnp.exp(soft_cap * jnp.tanh(fresh_scores / soft_cap)), 0.0)
        total = jnp.sum(fresh_w, axis=-1, keepdims=True)
        mixed = jnp.einsum("bqk,bkd->bqd", fresh_w.astype(jnp.bfloat16), fresh_values, preferred_element_type=jnp.float32)
        for g in range(group_size):
            head = group_size * k + g
            col = head * HEAD
            mix_ref[:, :, col:col + HEAD] = mixed[:, g * row_count:(g + 1) * row_count]
            sums = jnp.where(lane == head, total[:, g * row_count:(g + 1) * row_count], sums)
    sum_ref[...] = sums


def attend_fresh(queries, fresh_kv, block=8):
    slot_count, row_count, q_width = queries.shape
    kv_width = fresh_kv.shape[2]
    block = min(block, slot_count)
    return pl.pallas_call(
        fresh_kernel,
        out_shape=(
            jax.ShapeDtypeStruct((slot_count, row_count, q_width), jnp.float32),
            jax.ShapeDtypeStruct((slot_count, row_count, TAG_WIDTH), jnp.float32),
        ),
        grid=(slot_count // block,),
        in_specs=[
            pl.BlockSpec((block, row_count, q_width), lambda b: (b, 0, 0)),
            pl.BlockSpec((block, row_count, kv_width), lambda b: (b, 0, 0)),
        ],
        out_specs=(
            pl.BlockSpec((block, row_count, q_width), lambda b: (b, 0, 0)),
            pl.BlockSpec((block, row_count, TAG_WIDTH), lambda b: (b, 0, 0)),
        ),
        cost_estimate=pl.CostEstimate(
            flops=4 * slot_count * (q_width // HEAD) * row_count * row_count * HEAD,
            transcendentals=2 * slot_count * (q_width // HEAD) * row_count * row_count,
            bytes_accessed=int((queries.size + fresh_kv.size) * 2 + slot_count * row_count * (q_width + TAG_WIDTH) * 4),
        ),
    )(queries, fresh_kv)


def pack_lanes(payload, slot_lanes, lane_count):
    lane_ids = jnp.arange(lane_count, dtype=jnp.int32)
    slot_ids = jnp.arange(payload.shape[0], dtype=jnp.int32)
    lane_hits = slot_lanes[None, :] == lane_ids[:, None]
    filled = jnp.any(lane_hits, axis=1)
    chosen = jnp.sum(jnp.where(lane_hits, slot_ids[None, :], 0), axis=1)
    picked = jnp.take(payload, chosen, axis=0)
    return jnp.where(filled[:, None, None], picked, jnp.zeros((), payload.dtype))


def halving_stages(axis):
    count = lax.axis_size(axis)
    stages = count.bit_length() - 1
    return count, stages if (1 << stages) == count else None


def scatter_sum(partial, axis):
    count, stages = halving_stages(axis)
    rows, width = partial.shape
    if stages is None:
        return lax.psum_scatter(partial, axis, scatter_dimension=1, tiled=True).astype(jnp.float32)
    me = lax.axis_index(axis)
    held = partial.reshape((rows,) + (2,) * stages + (width // count,))
    for s in range(stages):
        bit = (me >> s) & 1
        dim = stages - s
        keep = lax.dynamic_index_in_dim(held, bit, axis=dim, keepdims=False)
        send = lax.dynamic_index_in_dim(held, 1 - bit, axis=dim, keepdims=False)
        got = lax.ppermute(
            send.astype(jnp.bfloat16), axis, perm=[(i, i ^ (1 << s)) for i in range(count)]
        )
        held = keep.astype(jnp.float32) + got.astype(jnp.float32)
    return held


def projection_kernel(block_ref, rows_ref, weight_ref, out_ref):
    out_ref[0] = jnp.dot(rows_ref[...], weight_ref[...], preferred_element_type=jnp.float32).astype(out_ref.dtype)


def project_blocks(rows, weight, blocks):
    row_total, inner = rows.shape
    width = weight.shape[1] // lax.axis_size("tensor")
    count = blocks.shape[0]
    return pl.pallas_call(
        projection_kernel,
        out_shape=jax.ShapeDtypeStruct((count, row_total, width), jnp.bfloat16),
        grid_spec=pltpu.PrefetchScalarGridSpec(
            num_scalar_prefetch=1,
            grid=(count,),
            in_specs=[
                pl.BlockSpec((row_total, inner), lambda j, blk: (0, 0)),
                pl.BlockSpec((inner, width), lambda j, blk: (0, blk[j])),
            ],
            out_specs=pl.BlockSpec((1, row_total, width), lambda j, blk: (j, 0, 0)),
        ),
        cost_estimate=pl.CostEstimate(
            flops=2 * count * row_total * inner * width,
            transcendentals=0,
            bytes_accessed=int(rows.size * 2 + count * (inner * width + row_total * width) * 2),
        ),
    )(blocks, rows, weight)


def bit_reversed(value, bits):
    out = 0
    for b in range(bits):
        out |= ((value >> b) & 1) << (bits - 1 - b)
    return out


def project_and_scatter(rows, weight, axis):
    count = lax.axis_size(axis)
    stages = count.bit_length() - 1
    if (1 << stages) != count or (weight.shape[1] // count) % 128:
        products = jnp.dot(rows, weight, preferred_element_type=jnp.float32).astype(jnp.bfloat16)
        return scatter_sum(products, axis)
    me = lax.axis_index(axis)
    order = jnp.array([bit_reversed(j, stages) for j in range(count)], jnp.int32)
    blocks = jnp.bitwise_xor(me, order)
    half = count // 2
    sent = project_blocks(rows, weight, blocks[half:])
    kept = project_blocks(rows, weight, blocks[:half])
    got = lax.ppermute(sent, axis, perm=[(i, i ^ 1) for i in range(count)])
    held = kept.astype(jnp.float32) + got.astype(jnp.float32)
    for s in range(1, stages):
        half = held.shape[0] // 2
        sent = held[half:].astype(jnp.bfloat16)
        rows_half = sent.shape[1] // 2
        perm = [(i, i ^ (1 << s)) for i in range(count)]
        got = jnp.concatenate(
            [lax.ppermute(sent[:, :rows_half], axis, perm=perm), lax.ppermute(sent[:, rows_half:], axis, perm=perm)],
            axis=1,
        )
        held = held[:half] + got.astype(jnp.float32)
    return held[0]


def butterfly_sum(values, axis):
    count, stages = halving_stages(axis)
    if stages is None:
        return lax.psum(values, axis)
    shape = values.shape
    lanes = 128 if values.size % 128 == 0 else values.size
    values = values.reshape(values.size // lanes, lanes)
    for s in range(stages):
        values = values + lax.ppermute(values, axis, perm=[(i, i ^ (1 << s)) for i in range(count)])
    return values.reshape(shape)


def exchange_by_shift(lanes, axis, cap, direction):
    count = lax.axis_size(axis)
    parts = [lanes[:cap]]
    for shift in range(1, count):
        parts.append(
            lax.ppermute(
                lanes[shift * cap:(shift + 1) * cap],
                axis,
                perm=[(i, (i + direction * shift) % count) for i in range(count)],
            )
        )
    return jnp.concatenate(parts, axis=0)


def shards(kv_cache, lengths, source, queries, fresh_kv, out_weight, norm_gain):
    dp_count = lax.axis_size("dp")
    me = lax.axis_index("dp")
    slot_count, row_count, query_width = queries.shape
    kv_width = fresh_kv.shape[2]
    pair_cap = max(1, slot_count // dp_count)
    lane_count = dp_count * pair_cap
    slot_ids = jnp.arange(slot_count, dtype=jnp.int32)
    lane_ids = jnp.arange(lane_count, dtype=jnp.int32)

    old_home = source // slot_count
    old_slot = source % slot_count
    earlier = slot_ids[None, :] < slot_ids[:, None]
    same_home = old_home[:, None] == old_home[None, :]
    rank = jnp.sum(same_home & earlier, axis=1)
    shift = (old_home - me) % dp_count
    out_lane = shift * pair_cap + rank
    tag = jnp.broadcast_to(
        (old_slot + 1).astype(jnp.bfloat16)[:, None, None], (slot_count, row_count, TAG_WIDTH)
    )
    payload = jnp.concatenate([queries, tag], axis=2)
    sending = pack_lanes(payload, out_lane, lane_count)
    arrived = exchange_by_shift(sending, "dp", pair_cap, 1)
    fresh_mix, fresh_sum = attend_fresh(queries, fresh_kv)

    lane_slot = arrived[:, 0, query_width].astype(jnp.int32) - 1
    hits = lane_slot[None, :] == slot_ids[:, None]
    slot_lane = jnp.sum(jnp.where(hits, lane_ids[None, :], 0), axis=1)
    gathered = jnp.take(arrived, slot_lane, axis=0)
    cache_part = attend_cache(gathered, kv_cache, lengths, query_width)

    filled = lane_slot >= 0
    back = jnp.take(cache_part, jnp.maximum(lane_slot, 0), axis=0)
    back = jnp.where(filled[:, None, None], back, jnp.zeros((), back.dtype))
    returned = exchange_by_shift(back, "dp", pair_cap, -1)
    cache_here = jnp.take(returned, out_lane, axis=0)

    heads = query_width // HEAD
    sums = cache_here[:, :, query_width:].astype(jnp.float32)
    cache_sum = sums[:, :, :heads] + sums[:, :, TAG_WIDTH // 2:TAG_WIDTH // 2 + heads]
    total = cache_sum + fresh_sum[:, :, :heads]
    cache_mix = cache_here[:, :, :query_width].astype(jnp.float32).reshape(slot_count, row_count, heads, HEAD)
    joined = cache_mix * cache_sum[..., None] + fresh_mix.reshape(slot_count, row_count, heads, HEAD)
    attended_here = (joined / total[..., None]).astype(jnp.bfloat16).reshape(slot_count, row_count, query_width)

    row_total = slot_count * row_count
    flat_rows = attended_here.reshape(row_total, query_width)
    model_width = out_weight.shape[1]
    own_part = project_and_scatter(flat_rows, out_weight, "tensor")
    square_sum = jnp.sum(own_part * own_part, axis=-1)
    square_sum = butterfly_sum(square_sum, "tensor").reshape(row_total, 1)
    mean_square = square_sum / model_width
    normed = own_part * lax.rsqrt(mean_square + norm_eps) * norm_gain
    return normed.astype(jnp.bfloat16).reshape(slot_count, row_count, own_part.shape[1])


def solution(mesh):
    placed = (
        P(("groups", "dp"), None, "tensor"),
        P(("groups", "dp")),
        P(("groups", "dp")),
        P(("groups", "dp"), None, "tensor"),
        P(("groups", "dp"), None, "tensor"),
        P("tensor", None),
        P("tensor"),
    )
    return jax.shard_map(
        shards,
        mesh=mesh,
        in_specs=placed,
        out_specs=P(("groups", "dp"), None, "tensor"),
        check_vma=False,
    )
```

```python
import functools

import jax
import jax.numpy as jnp
from jax import lax
from jax.experimental import pallas as pl
from jax.experimental.pallas import tpu as pltpu
from jax.sharding import PartitionSpec as P

HEAD = 128
QHEADS = 16
KVHEADS = 8
TAG_WIDTH = 128


score_scale = 144.0 ** (-0.5)
soft_cap = 50.0
norm_eps = 1e-06


def attention_kernel(length_ref, pay_ref, cache_ref, out_ref, *, q_width):
    sessions, cache_length, _ = cache_ref.shape
    row_count = pay_ref.shape[1]
    kv_heads = cache_ref.shape[2] // (2 * HEAD)
    group_size = QHEADS // KVHEADS
    lengths = length_ref[...]
    cache_pos = lax.broadcasted_iota(jnp.int32, (sessions, group_size * row_count, cache_length), 2)
    cache_seen = cache_pos < lengths
    lane = lax.broadcasted_iota(jnp.int32, (sessions, row_count, TAG_WIDTH), 2)
    sums = jnp.zeros((sessions, row_count, TAG_WIDTH), jnp.float32)
    for k in range(kv_heads):
        key_col = 2 * HEAD * k
        grouped = jnp.concatenate(
            [pay_ref[:, :, (group_size * k + g) * HEAD:(group_size * k + g + 1) * HEAD] for g in range(group_size)],
            axis=1,
        )
        cache_keys = cache_ref[:, :, key_col:key_col + HEAD]
        cache_values = cache_ref[:, :, key_col + HEAD:key_col + 2 * HEAD]
        cache_scores = jnp.einsum("bqd,bkd->bqk", grouped, cache_keys, preferred_element_type=jnp.float32) * score_scale
        cache_w = jnp.where(cache_seen, jnp.exp(soft_cap * jnp.tanh(cache_scores / soft_cap)), 0.0)
        total = jnp.sum(cache_w, axis=-1, keepdims=True)
        mixed = jnp.einsum("bqk,bkd->bqd", cache_w.astype(jnp.bfloat16), cache_values, preferred_element_type=jnp.float32)
        mixed = (mixed / total).astype(out_ref.dtype)
        high = total.astype(jnp.bfloat16).astype(jnp.float32)
        low = total - high
        for g in range(group_size):
            head = group_size * k + g
            col = head * HEAD
            out_ref[:, :, col:col + HEAD] = mixed[:, g * row_count:(g + 1) * row_count]
            sums = jnp.where(lane == head, high[:, g * row_count:(g + 1) * row_count], sums)
            sums = jnp.where(lane == TAG_WIDTH // 2 + head, low[:, g * row_count:(g + 1) * row_count], sums)
    out_ref[:, :, q_width:q_width + TAG_WIDTH] = sums.astype(out_ref.dtype)


def attend_cache(payload, cached, lengths, q_width, block=8):
    slot_count, row_count, _ = payload.shape
    cache_length, kv_width = cached.shape[1], cached.shape[2]
    block = min(block, slot_count)
    length_col = lengths.reshape(slot_count, 1, 1)
    return pl.pallas_call(
        functools.partial(attention_kernel, q_width=q_width),
        out_shape=jax.ShapeDtypeStruct((slot_count, row_count, q_width + TAG_WIDTH), jnp.bfloat16),
        grid=(slot_count // block,),
        in_specs=[
            pl.BlockSpec((block, 1, 1), lambda b: (b, 0, 0)),
            pl.BlockSpec((block, row_count, payload.shape[2]), lambda b: (b, 0, 0)),
            pl.BlockSpec((block, cache_length, kv_width), lambda b: (b, 0, 0)),
        ],
        out_specs=pl.BlockSpec((block, row_count, q_width + TAG_WIDTH), lambda b: (b, 0, 0)),
        cost_estimate=pl.CostEstimate(
            flops=4 * slot_count * (q_width // HEAD) * row_count * cache_length * HEAD,
            transcendentals=2 * slot_count * (q_width // HEAD) * row_count * cache_length,
            bytes_accessed=int(cached.size * 2 + payload.size * 2 + slot_count * row_count * (q_width + TAG_WIDTH) * 2),
        ),
    )(length_col, payload, cached)


def fresh_kernel(q_ref, fresh_ref, mix_ref, sum_ref):
    sessions, row_count, _ = q_ref.shape
    kv_heads = fresh_ref.shape[2] // (2 * HEAD)
    group_size = QHEADS // KVHEADS
    fresh_pos = lax.broadcasted_iota(jnp.int32, (sessions, group_size * row_count, row_count), 2)
    query_row = lax.broadcasted_iota(jnp.int32, (sessions, group_size * row_count, row_count), 1) % row_count
    fresh_seen = fresh_pos <= query_row
    lane = lax.broadcasted_iota(jnp.int32, (sessions, row_count, TAG_WIDTH), 2)
    sums = jnp.zeros((sessions, row_count, TAG_WIDTH), jnp.float32)
    for k in range(kv_heads):
        key_col = 2 * HEAD * k
        grouped = jnp.concatenate(
            [q_ref[:, :, (group_size * k + g) * HEAD:(group_size * k + g + 1) * HEAD] for g in range(group_size)],
            axis=1,
        )
        fresh_keys = fresh_ref[:, :, key_col:key_col + HEAD]
        fresh_values = fresh_ref[:, :, key_col + HEAD:key_col + 2 * HEAD]
        fresh_scores = jnp.einsum("bqd,bkd->bqk", grouped, fresh_keys, preferred_element_type=jnp.float32) * score_scale
        fresh_w = jnp.where(fresh_seen, jnp.exp(soft_cap * jnp.tanh(fresh_scores / soft_cap)), 0.0)
        total = jnp.sum(fresh_w, axis=-1, keepdims=True)
        mixed = jnp.einsum("bqk,bkd->bqd", fresh_w.astype(jnp.bfloat16), fresh_values, preferred_element_type=jnp.float32)
        for g in range(group_size):
            head = group_size * k + g
            col = head * HEAD
            mix_ref[:, :, col:col + HEAD] = mixed[:, g * row_count:(g + 1) * row_count]
            sums = jnp.where(lane == head, total[:, g * row_count:(g + 1) * row_count], sums)
    sum_ref[...] = sums


def attend_fresh(queries, fresh_kv, block=8):
    slot_count, row_count, q_width = queries.shape
    kv_width = fresh_kv.shape[2]
    block = min(block, slot_count)
    return pl.pallas_call(
        fresh_kernel,
        out_shape=(
            jax.ShapeDtypeStruct((slot_count, row_count, q_width), jnp.float32),
            jax.ShapeDtypeStruct((slot_count, row_count, TAG_WIDTH), jnp.float32),
        ),
        grid=(slot_count // block,),
        in_specs=[
            pl.BlockSpec((block, row_count, q_width), lambda b: (b, 0, 0)),
            pl.BlockSpec((block, row_count, kv_width), lambda b: (b, 0, 0)),
        ],
        out_specs=(
            pl.BlockSpec((block, row_count, q_width), lambda b: (b, 0, 0)),
            pl.BlockSpec((block, row_count, TAG_WIDTH), lambda b: (b, 0, 0)),
        ),
        cost_estimate=pl.CostEstimate(
            flops=4 * slot_count * (q_width // HEAD) * row_count * row_count * HEAD,
            transcendentals=2 * slot_count * (q_width // HEAD) * row_count * row_count,
            bytes_accessed=int((queries.size + fresh_kv.size) * 2 + slot_count * row_count * (q_width + TAG_WIDTH) * 4),
        ),
    )(queries, fresh_kv)


def pack_lanes(payload, slot_lanes, lane_count):
    lane_ids = jnp.arange(lane_count, dtype=jnp.int32)
    slot_ids = jnp.arange(payload.shape[0], dtype=jnp.int32)
    lane_hits = slot_lanes[None, :] == lane_ids[:, None]
    filled = jnp.any(lane_hits, axis=1)
    chosen = jnp.sum(jnp.where(lane_hits, slot_ids[None, :], 0), axis=1)
    picked = jnp.take(payload, chosen, axis=0)
    return jnp.where(filled[:, None, None], picked, jnp.zeros((), payload.dtype))


def halving_stages(axis):
    count = lax.axis_size(axis)
    stages = count.bit_length() - 1
    return count, stages if (1 << stages) == count else None


def scatter_sum(partial, axis):
    count, stages = halving_stages(axis)
    rows, width = partial.shape
    if stages is None:
        return lax.psum_scatter(partial, axis, scatter_dimension=1, tiled=True).astype(jnp.float32)
    me = lax.axis_index(axis)
    held = partial.reshape((rows,) + (2,) * stages + (width // count,))
    for s in range(stages):
        bit = (me >> s) & 1
        dim = stages - s
        keep = lax.dynamic_index_in_dim(held, bit, axis=dim, keepdims=False)
        send = lax.dynamic_index_in_dim(held, 1 - bit, axis=dim, keepdims=False)
        got = lax.ppermute(
            send.astype(jnp.bfloat16), axis, perm=[(i, i ^ (1 << s)) for i in range(count)]
        )
        held = keep.astype(jnp.float32) + got.astype(jnp.float32)
    return held


def projection_kernel(block_ref, rows_ref, weight_ref, out_ref):
    out_ref[0] = jnp.dot(rows_ref[...], weight_ref[...], preferred_element_type=jnp.float32).astype(out_ref.dtype)


def project_blocks(rows, weight, blocks):
    row_total, inner = rows.shape
    width = weight.shape[1] // lax.axis_size("tensor")
    count = blocks.shape[0]
    return pl.pallas_call(
        projection_kernel,
        out_shape=jax.ShapeDtypeStruct((count, row_total, width), jnp.bfloat16),
        grid_spec=pltpu.PrefetchScalarGridSpec(
            num_scalar_prefetch=1,
            grid=(count,),
            in_specs=[
                pl.BlockSpec((row_total, inner), lambda j, blk: (0, 0)),
                pl.BlockSpec((inner, width), lambda j, blk: (0, blk[j])),
            ],
            out_specs=pl.BlockSpec((1, row_total, width), lambda j, blk: (j, 0, 0)),
        ),
        cost_estimate=pl.CostEstimate(
            flops=2 * count * row_total * inner * width,
            transcendentals=0,
            bytes_accessed=int(rows.size * 2 + count * (inner * width + row_total * width) * 2),
        ),
    )(blocks, rows, weight)


def bit_reversed(value, bits):
    out = 0
    for b in range(bits):
        out |= ((value >> b) & 1) << (bits - 1 - b)
    return out


def project_and_scatter(rows, weight, axis):
    count = lax.axis_size(axis)
    stages = count.bit_length() - 1
    if (1 << stages) != count or (weight.shape[1] // count) % 128:
        products = jnp.dot(rows, weight, preferred_element_type=jnp.float32).astype(jnp.bfloat16)
        return scatter_sum(products, axis)
    me = lax.axis_index(axis)
    order = jnp.array([bit_reversed(j, stages) for j in range(count)], jnp.int32)
    blocks = jnp.bitwise_xor(me, order)
    half = count // 2
    sent = project_blocks(rows, weight, blocks[half:])
    kept = project_blocks(rows, weight, blocks[:half])
    got = lax.ppermute(sent, axis, perm=[(i, i ^ 1) for i in range(count)])
    held = kept.astype(jnp.float32) + got.astype(jnp.float32)
    for s in range(1, stages):
        half = held.shape[0] // 2
        got = lax.ppermute(
            held[half:].astype(jnp.bfloat16), axis, perm=[(i, i ^ (1 << s)) for i in range(count)]
        )
        held = held[:half] + got.astype(jnp.float32)
    return held[0]


def butterfly_sum(values, axis):
    count, stages = halving_stages(axis)
    if stages is None:
        return lax.psum(values, axis)
    shape = values.shape
    lanes = 128 if values.size % 128 == 0 else values.size
    values = values.reshape(values.size // lanes, lanes)
    for s in range(stages):
        values = values + lax.ppermute(values, axis, perm=[(i, i ^ (1 << s)) for i in range(count)])
    return values.reshape(shape)


def exchange_by_shift(lanes, axis, cap, direction):
    count = lax.axis_size(axis)
    parts = [lanes[:cap]]
    for shift in range(1, count):
        parts.append(
            lax.ppermute(
                lanes[shift * cap:(shift + 1) * cap],
                axis,
                perm=[(i, (i + direction * shift) % count) for i in range(count)],
            )
        )
    return jnp.concatenate(parts, axis=0)


def gather_weights(weight, axis):
    count = lax.axis_size(axis)
    width = weight.shape[1] // count
    me = lax.axis_index(axis)
    if count != 4 or width % 128:
        blocks = weight.reshape(weight.shape[0], count, width).transpose(1, 0, 2)
        return lax.all_to_all(blocks, axis, 0, 0, tiled=True), None

    def cols(peer):
        return lax.dynamic_slice_in_dim(weight, peer * width, width, axis=1)

    across = lax.ppermute(
        jnp.stack([cols(me ^ 2), cols(me ^ 3)]), axis, perm=[(i, i ^ 2) for i in range(count)]
    )
    beside = lax.ppermute(
        jnp.stack([cols(me ^ 1), across[1]]), axis, perm=[(i, i ^ 1) for i in range(count)]
    )
    return jnp.stack([cols(me), across[0], beside[0], beside[1]]), True


def gather_rows(attended, axis, manual):
    count = lax.axis_size(axis)
    if manual is None:
        return lax.all_gather(attended, axis, axis=0, tiled=False)
    across = lax.ppermute(attended, axis, perm=[(i, i ^ 2) for i in range(count)])
    beside = lax.ppermute(jnp.stack([attended, across]), axis, perm=[(i, i ^ 1) for i in range(count)])
    return jnp.stack([attended, across, beside[0], beside[1]])


def shards(kv_cache, lengths, source, queries, fresh_kv, out_weight, norm_gain):
    dp_count = lax.axis_size("dp")
    me = lax.axis_index("dp")
    slot_count, row_count, query_width = queries.shape
    kv_width = fresh_kv.shape[2]
    pair_cap = max(1, slot_count // dp_count)
    lane_count = dp_count * pair_cap
    slot_ids = jnp.arange(slot_count, dtype=jnp.int32)
    lane_ids = jnp.arange(lane_count, dtype=jnp.int32)

    old_home = source // slot_count
    old_slot = source % slot_count
    earlier = slot_ids[None, :] < slot_ids[:, None]
    same_home = old_home[:, None] == old_home[None, :]
    rank = jnp.sum(same_home & earlier, axis=1)
    shift = (old_home - me) % dp_count
    out_lane = shift * pair_cap + rank
    tag = jnp.broadcast_to(
        (old_slot + 1).astype(jnp.bfloat16)[:, None, None], (slot_count, row_count, TAG_WIDTH)
    )
    payload = jnp.concatenate([queries, tag], axis=2)
    peer_weights, manual = gather_weights(out_weight, "tensor")
    sending = pack_lanes(payload, out_lane, lane_count)
    arrived = exchange_by_shift(sending, "dp", pair_cap, 1)
    fresh_mix, fresh_sum = attend_fresh(queries, fresh_kv)

    lane_slot = arrived[:, 0, query_width].astype(jnp.int32) - 1
    hits = lane_slot[None, :] == slot_ids[:, None]
    slot_lane = jnp.sum(jnp.where(hits, lane_ids[None, :], 0), axis=1)
    gathered = jnp.take(arrived, slot_lane, axis=0)
    cache_part = attend_cache(gathered, kv_cache, lengths, query_width)

    filled = lane_slot >= 0
    back = jnp.take(cache_part, jnp.maximum(lane_slot, 0), axis=0)
    back = jnp.where(filled[:, None, None], back, jnp.zeros((), back.dtype))
    returned = exchange_by_shift(back, "dp", pair_cap, -1)
    cache_here = jnp.take(returned, out_lane, axis=0)

    heads = query_width // HEAD
    sums = cache_here[:, :, query_width:].astype(jnp.float32)
    cache_sum = sums[:, :, :heads] + sums[:, :, TAG_WIDTH // 2:TAG_WIDTH // 2 + heads]
    total = cache_sum + fresh_sum[:, :, :heads]
    cache_mix = cache_here[:, :, :query_width].astype(jnp.float32).reshape(slot_count, row_count, heads, HEAD)
    joined = cache_mix * cache_sum[..., None] + fresh_mix.reshape(slot_count, row_count, heads, HEAD)
    attended_here = (joined / total[..., None]).astype(jnp.bfloat16).reshape(slot_count, row_count, query_width)

    row_total = slot_count * row_count
    flat_rows = attended_here.reshape(row_total, query_width)
    model_width = out_weight.shape[1]
    every_rows = gather_rows(flat_rows, "tensor", manual)
    peers = every_rows.shape[0]
    own_part = jnp.dot(flat_rows, peer_weights[0], preferred_element_type=jnp.float32)
    rest_rows = jnp.concatenate([every_rows[i] for i in range(1, peers)], axis=1)
    rest_weights = jnp.concatenate([peer_weights[i] for i in range(1, peers)], axis=0)
    own_part = own_part + jnp.dot(rest_rows, rest_weights, preferred_element_type=jnp.float32)
    square_sum = jnp.sum(own_part * own_part, axis=-1)
    square_sum = butterfly_sum(square_sum, "tensor").reshape(row_total, 1)
    mean_square = square_sum / model_width
    normed = own_part * lax.rsqrt(mean_square + norm_eps) * norm_gain
    return normed.astype(jnp.bfloat16).reshape(slot_count, row_count, own_part.shape[1])


def solution(mesh):
    placed = (
        P(("groups", "dp"), None, "tensor"),
        P(("groups", "dp")),
        P(("groups", "dp")),
        P(("groups", "dp"), None, "tensor"),
        P(("groups", "dp"), None, "tensor"),
        P("tensor", None),
        P("tensor"),
    )
    return jax.shard_map(
        shards,
        mesh=mesh,
        in_specs=placed,
        out_specs=P(("groups", "dp"), None, "tensor"),
        check_vma=False,
    )
```

```python
import functools

import jax
import jax.numpy as jnp
from jax import lax
from jax.experimental import pallas as pl
from jax.experimental.pallas import tpu as pltpu
from jax.sharding import PartitionSpec as P

HEAD = 128
QHEADS = 16
KVHEADS = 8
TAG_WIDTH = 128


score_scale = 144.0 ** (-0.5)
soft_cap = 50.0
norm_eps = 1e-06


def attention_kernel(length_ref, pay_ref, cache_ref, out_ref, *, q_width):
    sessions, cache_length, _ = cache_ref.shape
    row_count = pay_ref.shape[1]
    kv_heads = cache_ref.shape[2] // (2 * HEAD)
    group_size = QHEADS // KVHEADS
    lengths = length_ref[...]
    cache_pos = lax.broadcasted_iota(jnp.int32, (sessions, group_size * row_count, cache_length), 2)
    cache_seen = cache_pos < lengths
    lane = lax.broadcasted_iota(jnp.int32, (sessions, row_count, TAG_WIDTH), 2)
    sums = jnp.zeros((sessions, row_count, TAG_WIDTH), jnp.float32)
    for k in range(kv_heads):
        key_col = 2 * HEAD * k
        grouped = jnp.concatenate(
            [pay_ref[:, :, (group_size * k + g) * HEAD:(group_size * k + g + 1) * HEAD] for g in range(group_size)],
            axis=1,
        )
        cache_keys = cache_ref[:, :, key_col:key_col + HEAD]
        cache_values = cache_ref[:, :, key_col + HEAD:key_col + 2 * HEAD]
        cache_scores = jnp.einsum("bqd,bkd->bqk", grouped, cache_keys, preferred_element_type=jnp.float32) * score_scale
        cache_w = jnp.where(cache_seen, jnp.exp(soft_cap * jnp.tanh(cache_scores / soft_cap)), 0.0)
        total = jnp.sum(cache_w, axis=-1, keepdims=True)
        mixed = jnp.einsum("bqk,bkd->bqd", cache_w.astype(jnp.bfloat16), cache_values, preferred_element_type=jnp.float32)
        mixed = (mixed / total).astype(out_ref.dtype)
        high = total.astype(jnp.bfloat16).astype(jnp.float32)
        low = total - high
        for g in range(group_size):
            head = group_size * k + g
            col = head * HEAD
            out_ref[:, :, col:col + HEAD] = mixed[:, g * row_count:(g + 1) * row_count]
            sums = jnp.where(lane == head, high[:, g * row_count:(g + 1) * row_count], sums)
            sums = jnp.where(lane == TAG_WIDTH // 2 + head, low[:, g * row_count:(g + 1) * row_count], sums)
    out_ref[:, :, q_width:q_width + TAG_WIDTH] = sums.astype(out_ref.dtype)


def attend_cache(payload, cached, lengths, q_width, block=8):
    slot_count, row_count, _ = payload.shape
    cache_length, kv_width = cached.shape[1], cached.shape[2]
    block = min(block, slot_count)
    length_col = lengths.reshape(slot_count, 1, 1)
    return pl.pallas_call(
        functools.partial(attention_kernel, q_width=q_width),
        out_shape=jax.ShapeDtypeStruct((slot_count, row_count, q_width + TAG_WIDTH), jnp.bfloat16),
        grid=(slot_count // block,),
        in_specs=[
            pl.BlockSpec((block, 1, 1), lambda b: (b, 0, 0)),
            pl.BlockSpec((block, row_count, payload.shape[2]), lambda b: (b, 0, 0)),
            pl.BlockSpec((block, cache_length, kv_width), lambda b: (b, 0, 0)),
        ],
        out_specs=pl.BlockSpec((block, row_count, q_width + TAG_WIDTH), lambda b: (b, 0, 0)),
        cost_estimate=pl.CostEstimate(
            flops=4 * slot_count * (q_width // HEAD) * row_count * cache_length * HEAD,
            transcendentals=2 * slot_count * (q_width // HEAD) * row_count * cache_length,
            bytes_accessed=int(cached.size * 2 + payload.size * 2 + slot_count * row_count * (q_width + TAG_WIDTH) * 2),
        ),
    )(length_col, payload, cached)


def fresh_kernel(q_ref, fresh_ref, mix_ref, sum_ref):
    sessions, row_count, _ = q_ref.shape
    kv_heads = fresh_ref.shape[2] // (2 * HEAD)
    group_size = QHEADS // KVHEADS
    fresh_pos = lax.broadcasted_iota(jnp.int32, (sessions, group_size * row_count, row_count), 2)
    query_row = lax.broadcasted_iota(jnp.int32, (sessions, group_size * row_count, row_count), 1) % row_count
    fresh_seen = fresh_pos <= query_row
    lane = lax.broadcasted_iota(jnp.int32, (sessions, row_count, TAG_WIDTH), 2)
    sums = jnp.zeros((sessions, row_count, TAG_WIDTH), jnp.float32)
    for k in range(kv_heads):
        key_col = 2 * HEAD * k
        grouped = jnp.concatenate(
            [q_ref[:, :, (group_size * k + g) * HEAD:(group_size * k + g + 1) * HEAD] for g in range(group_size)],
            axis=1,
        )
        fresh_keys = fresh_ref[:, :, key_col:key_col + HEAD]
        fresh_values = fresh_ref[:, :, key_col + HEAD:key_col + 2 * HEAD]
        fresh_scores = jnp.einsum("bqd,bkd->bqk", grouped, fresh_keys, preferred_element_type=jnp.float32) * score_scale
        fresh_w = jnp.where(fresh_seen, jnp.exp(soft_cap * jnp.tanh(fresh_scores / soft_cap)), 0.0)
        total = jnp.sum(fresh_w, axis=-1, keepdims=True)
        mixed = jnp.einsum("bqk,bkd->bqd", fresh_w.astype(jnp.bfloat16), fresh_values, preferred_element_type=jnp.float32)
        for g in range(group_size):
            head = group_size * k + g
            col = head * HEAD
            mix_ref[:, :, col:col + HEAD] = mixed[:, g * row_count:(g + 1) * row_count]
            sums = jnp.where(lane == head, total[:, g * row_count:(g + 1) * row_count], sums)
    sum_ref[...] = sums


def attend_fresh(queries, fresh_kv, block=8):
    slot_count, row_count, q_width = queries.shape
    kv_width = fresh_kv.shape[2]
    block = min(block, slot_count)
    return pl.pallas_call(
        fresh_kernel,
        out_shape=(
            jax.ShapeDtypeStruct((slot_count, row_count, q_width), jnp.float32),
            jax.ShapeDtypeStruct((slot_count, row_count, TAG_WIDTH), jnp.float32),
        ),
        grid=(slot_count // block,),
        in_specs=[
            pl.BlockSpec((block, row_count, q_width), lambda b: (b, 0, 0)),
            pl.BlockSpec((block, row_count, kv_width), lambda b: (b, 0, 0)),
        ],
        out_specs=(
            pl.BlockSpec((block, row_count, q_width), lambda b: (b, 0, 0)),
            pl.BlockSpec((block, row_count, TAG_WIDTH), lambda b: (b, 0, 0)),
        ),
        cost_estimate=pl.CostEstimate(
            flops=4 * slot_count * (q_width // HEAD) * row_count * row_count * HEAD,
            transcendentals=2 * slot_count * (q_width // HEAD) * row_count * row_count,
            bytes_accessed=int((queries.size + fresh_kv.size) * 2 + slot_count * row_count * (q_width + TAG_WIDTH) * 4),
        ),
    )(queries, fresh_kv)


def pack_lanes(payload, slot_lanes, lane_count):
    lane_ids = jnp.arange(lane_count, dtype=jnp.int32)
    slot_ids = jnp.arange(payload.shape[0], dtype=jnp.int32)
    lane_hits = slot_lanes[None, :] == lane_ids[:, None]
    filled = jnp.any(lane_hits, axis=1)
    chosen = jnp.sum(jnp.where(lane_hits, slot_ids[None, :], 0), axis=1)
    picked = jnp.take(payload, chosen, axis=0)
    return jnp.where(filled[:, None, None], picked, jnp.zeros((), payload.dtype))


def halving_stages(axis):
    count = lax.axis_size(axis)
    stages = count.bit_length() - 1
    return count, stages if (1 << stages) == count else None


def scatter_sum(partial, axis):
    count, stages = halving_stages(axis)
    rows, width = partial.shape
    if stages is None:
        return lax.psum_scatter(partial, axis, scatter_dimension=1, tiled=True).astype(jnp.float32)
    me = lax.axis_index(axis)
    held = partial.reshape((rows,) + (2,) * stages + (width // count,))
    for s in range(stages):
        bit = (me >> s) & 1
        dim = stages - s
        keep = lax.dynamic_index_in_dim(held, bit, axis=dim, keepdims=False)
        send = lax.dynamic_index_in_dim(held, 1 - bit, axis=dim, keepdims=False)
        got = lax.ppermute(
            send.astype(jnp.bfloat16), axis, perm=[(i, i ^ (1 << s)) for i in range(count)]
        )
        held = keep.astype(jnp.float32) + got.astype(jnp.float32)
    return held


def projection_kernel(block_ref, rows_ref, weight_ref, out_ref):
    out_ref[0] = jnp.dot(rows_ref[...], weight_ref[...], preferred_element_type=jnp.float32).astype(out_ref.dtype)


def project_blocks(rows, weight, blocks):
    row_total, inner = rows.shape
    width = weight.shape[1] // lax.axis_size("tensor")
    count = blocks.shape[0]
    return pl.pallas_call(
        projection_kernel,
        out_shape=jax.ShapeDtypeStruct((count, row_total, width), jnp.bfloat16),
        grid_spec=pltpu.PrefetchScalarGridSpec(
            num_scalar_prefetch=1,
            grid=(count,),
            in_specs=[
                pl.BlockSpec((row_total, inner), lambda j, blk: (0, 0)),
                pl.BlockSpec((inner, width), lambda j, blk: (0, blk[j])),
            ],
            out_specs=pl.BlockSpec((1, row_total, width), lambda j, blk: (j, 0, 0)),
        ),
        cost_estimate=pl.CostEstimate(
            flops=2 * count * row_total * inner * width,
            transcendentals=0,
            bytes_accessed=int(rows.size * 2 + count * (inner * width + row_total * width) * 2),
        ),
    )(blocks, rows, weight)


def bit_reversed(value, bits):
    out = 0
    for b in range(bits):
        out |= ((value >> b) & 1) << (bits - 1 - b)
    return out


def project_and_scatter(rows, weight, axis):
    count = lax.axis_size(axis)
    stages = count.bit_length() - 1
    if (1 << stages) != count or (weight.shape[1] // count) % 128:
        products = jnp.dot(rows, weight, preferred_element_type=jnp.float32).astype(jnp.bfloat16)
        return scatter_sum(products, axis)
    me = lax.axis_index(axis)
    order = jnp.array([bit_reversed(j, stages) for j in range(count)], jnp.int32)
    blocks = jnp.bitwise_xor(me, order)
    half = count // 2
    sent = project_blocks(rows, weight, blocks[half:])
    kept = project_blocks(rows, weight, blocks[:half])
    got = lax.ppermute(sent, axis, perm=[(i, i ^ 1) for i in range(count)])
    held = kept.astype(jnp.float32) + got.astype(jnp.float32)
    for s in range(1, stages):
        half = held.shape[0] // 2
        got = lax.ppermute(
            held[half:].astype(jnp.bfloat16), axis, perm=[(i, i ^ (1 << s)) for i in range(count)]
        )
        held = held[:half] + got.astype(jnp.float32)
    return held[0]


def butterfly_sum(values, axis):
    count, stages = halving_stages(axis)
    if stages is None:
        return lax.psum(values, axis)
    shape = values.shape
    lanes = 128 if values.size % 128 == 0 else values.size
    values = values.reshape(values.size // lanes, lanes)
    for s in range(stages):
        values = values + lax.ppermute(values, axis, perm=[(i, i ^ (1 << s)) for i in range(count)])
    return values.reshape(shape)


def exchange_by_shift(lanes, axis, cap, direction):
    count = lax.axis_size(axis)
    parts = [lanes[:cap]]
    for shift in range(1, count):
        parts.append(
            lax.ppermute(
                lanes[shift * cap:(shift + 1) * cap],
                axis,
                perm=[(i, (i + direction * shift) % count) for i in range(count)],
            )
        )
    return jnp.concatenate(parts, axis=0)


def gather_weights(weight, axis):
    count = lax.axis_size(axis)
    width = weight.shape[1] // count
    me = lax.axis_index(axis)
    if count != 4 or width % 128:
        blocks = weight.reshape(weight.shape[0], count, width).transpose(1, 0, 2)
        return lax.all_to_all(blocks, axis, 0, 0, tiled=True), None

    def cols(peer):
        return lax.dynamic_slice_in_dim(weight, peer * width, width, axis=1)

    replicas = lax.axis_size("groups")
    if replicas == 2 and weight.shape[0] % 32 == 0:
        group = lax.axis_index("groups")
        half = weight.shape[0] // 2
        mine = lax.dynamic_slice_in_dim(jnp.stack([cols(me ^ 2), cols(me ^ 3)]), group * half, half, axis=1)
        got = lax.ppermute(mine, axis, perm=[(i, i ^ 2) for i in range(count)])
        other = lax.ppermute(got, "groups", perm=[(0, 1), (1, 0)])
        across = jnp.where(group == 0, jnp.concatenate([got, other], axis=1), jnp.concatenate([other, got], axis=1))
    else:
        across = lax.ppermute(
            jnp.stack([cols(me ^ 2), cols(me ^ 3)]), axis, perm=[(i, i ^ 2) for i in range(count)]
        )
    beside = lax.ppermute(
        jnp.stack([cols(me ^ 1), across[1]]), axis, perm=[(i, i ^ 1) for i in range(count)]
    )
    return jnp.stack([cols(me), across[0], beside[0], beside[1]]), True


def gather_rows(attended, axis, manual):
    count = lax.axis_size(axis)
    if manual is None:
        return lax.all_gather(attended, axis, axis=0, tiled=False)
    across = lax.ppermute(attended, axis, perm=[(i, i ^ 2) for i in range(count)])
    beside = lax.ppermute(jnp.stack([attended, across]), axis, perm=[(i, i ^ 1) for i in range(count)])
    return jnp.stack([attended, across, beside[0], beside[1]])


def shards(kv_cache, lengths, source, queries, fresh_kv, out_weight, norm_gain):
    dp_count = lax.axis_size("dp")
    me = lax.axis_index("dp")
    slot_count, row_count, query_width = queries.shape
    kv_width = fresh_kv.shape[2]
    pair_cap = max(1, slot_count // dp_count)
    lane_count = dp_count * pair_cap
    slot_ids = jnp.arange(slot_count, dtype=jnp.int32)
    lane_ids = jnp.arange(lane_count, dtype=jnp.int32)

    old_home = source // slot_count
    old_slot = source % slot_count
    earlier = slot_ids[None, :] < slot_ids[:, None]
    same_home = old_home[:, None] == old_home[None, :]
    rank = jnp.sum(same_home & earlier, axis=1)
    shift = (old_home - me) % dp_count
    out_lane = shift * pair_cap + rank
    tag = jnp.broadcast_to(
        (old_slot + 1).astype(jnp.bfloat16)[:, None, None], (slot_count, row_count, TAG_WIDTH)
    )
    payload = jnp.concatenate([queries, tag], axis=2)
    peer_weights, manual = gather_weights(out_weight, "tensor")
    sending = pack_lanes(payload, out_lane, lane_count)
    arrived = exchange_by_shift(sending, "dp", pair_cap, 1)
    fresh_mix, fresh_sum = attend_fresh(queries, fresh_kv)

    lane_slot = arrived[:, 0, query_width].astype(jnp.int32) - 1
    hits = lane_slot[None, :] == slot_ids[:, None]
    slot_lane = jnp.sum(jnp.where(hits, lane_ids[None, :], 0), axis=1)
    gathered = jnp.take(arrived, slot_lane, axis=0)
    cache_part = attend_cache(gathered, kv_cache, lengths, query_width)

    filled = lane_slot >= 0
    back = jnp.take(cache_part, jnp.maximum(lane_slot, 0), axis=0)
    back = jnp.where(filled[:, None, None], back, jnp.zeros((), back.dtype))
    returned = exchange_by_shift(back, "dp", pair_cap, -1)
    cache_here = jnp.take(returned, out_lane, axis=0)

    heads = query_width // HEAD
    sums = cache_here[:, :, query_width:].astype(jnp.float32)
    cache_sum = sums[:, :, :heads] + sums[:, :, TAG_WIDTH // 2:TAG_WIDTH // 2 + heads]
    total = cache_sum + fresh_sum[:, :, :heads]
    cache_mix = cache_here[:, :, :query_width].astype(jnp.float32).reshape(slot_count, row_count, heads, HEAD)
    joined = cache_mix * cache_sum[..., None] + fresh_mix.reshape(slot_count, row_count, heads, HEAD)
    attended_here = (joined / total[..., None]).astype(jnp.bfloat16).reshape(slot_count, row_count, query_width)

    row_total = slot_count * row_count
    flat_rows = attended_here.reshape(row_total, query_width)
    model_width = out_weight.shape[1]
    every_rows = gather_rows(flat_rows, "tensor", manual)
    peers = every_rows.shape[0]
    own_part = jnp.dot(flat_rows, peer_weights[0], preferred_element_type=jnp.float32)
    rest_rows = jnp.concatenate([every_rows[i] for i in range(1, peers)], axis=1)
    rest_weights = jnp.concatenate([peer_weights[i] for i in range(1, peers)], axis=0)
    own_part = own_part + jnp.dot(rest_rows, rest_weights, preferred_element_type=jnp.float32)
    square_sum = jnp.sum(own_part * own_part, axis=-1)
    square_sum = butterfly_sum(square_sum, "tensor").reshape(row_total, 1)
    mean_square = square_sum / model_width
    normed = own_part * lax.rsqrt(mean_square + norm_eps) * norm_gain
    return normed.astype(jnp.bfloat16).reshape(slot_count, row_count, own_part.shape[1])


def solution(mesh):
    placed = (
        P(("groups", "dp"), None, "tensor"),
        P(("groups", "dp")),
        P(("groups", "dp")),
        P(("groups", "dp"), None, "tensor"),
        P(("groups", "dp"), None, "tensor"),
        P("tensor", None),
        P("tensor"),
    )
    return jax.shard_map(
        shards,
        mesh=mesh,
        in_specs=placed,
        out_specs=P(("groups", "dp"), None, "tensor"),
        check_vma=False,
    )
```

```python
import functools

import jax
import jax.numpy as jnp
from jax import lax
from jax.experimental import pallas as pl
from jax.experimental.pallas import tpu as pltpu
from jax.sharding import PartitionSpec as P

HEAD = 128
QHEADS = 16
KVHEADS = 8
TAG_WIDTH = 128


score_scale = 144.0 ** (-0.5)
soft_cap = 50.0
norm_eps = 1e-06


def attention_kernel(length_ref, pay_ref, cache_ref, out_ref, *, q_width):
    sessions, cache_length, _ = cache_ref.shape
    row_count = pay_ref.shape[1]
    kv_heads = cache_ref.shape[2] // (2 * HEAD)
    group_size = QHEADS // KVHEADS
    lengths = length_ref[...]
    cache_pos = lax.broadcasted_iota(jnp.int32, (sessions, group_size * row_count, cache_length), 2)
    cache_seen = cache_pos < lengths
    lane = lax.broadcasted_iota(jnp.int32, (sessions, row_count, TAG_WIDTH), 2)
    sums = jnp.zeros((sessions, row_count, TAG_WIDTH), jnp.float32)
    for k in range(kv_heads):
        key_col = 2 * HEAD * k
        grouped = jnp.concatenate(
            [pay_ref[:, :, (group_size * k + g) * HEAD:(group_size * k + g + 1) * HEAD] for g in range(group_size)],
            axis=1,
        )
        cache_keys = cache_ref[:, :, key_col:key_col + HEAD]
        cache_values = cache_ref[:, :, key_col + HEAD:key_col + 2 * HEAD]
        cache_scores = jnp.einsum("bqd,bkd->bqk", grouped, cache_keys, preferred_element_type=jnp.float32) * score_scale
        cache_w = jnp.where(cache_seen, jnp.exp(soft_cap * jnp.tanh(cache_scores / soft_cap)), 0.0)
        total = jnp.sum(cache_w, axis=-1, keepdims=True)
        mixed = jnp.einsum("bqk,bkd->bqd", cache_w.astype(jnp.bfloat16), cache_values, preferred_element_type=jnp.float32)
        mixed = (mixed / total).astype(out_ref.dtype)
        high = total.astype(jnp.bfloat16).astype(jnp.float32)
        low = total - high
        for g in range(group_size):
            head = group_size * k + g
            col = head * HEAD
            out_ref[:, :, col:col + HEAD] = mixed[:, g * row_count:(g + 1) * row_count]
            sums = jnp.where(lane == head, high[:, g * row_count:(g + 1) * row_count], sums)
            sums = jnp.where(lane == TAG_WIDTH // 2 + head, low[:, g * row_count:(g + 1) * row_count], sums)
    out_ref[:, :, q_width:q_width + TAG_WIDTH] = sums.astype(out_ref.dtype)


def attend_cache(payload, cached, lengths, q_width, block=8):
    slot_count, row_count, _ = payload.shape
    cache_length, kv_width = cached.shape[1], cached.shape[2]
    block = min(block, slot_count)
    length_col = lengths.reshape(slot_count, 1, 1)
    return pl.pallas_call(
        functools.partial(attention_kernel, q_width=q_width),
        out_shape=jax.ShapeDtypeStruct((slot_count, row_count, q_width + TAG_WIDTH), jnp.bfloat16),
        grid=(slot_count // block,),
        in_specs=[
            pl.BlockSpec((block, 1, 1), lambda b: (b, 0, 0)),
            pl.BlockSpec((block, row_count, payload.shape[2]), lambda b: (b, 0, 0)),
            pl.BlockSpec((block, cache_length, kv_width), lambda b: (b, 0, 0)),
        ],
        out_specs=pl.BlockSpec((block, row_count, q_width + TAG_WIDTH), lambda b: (b, 0, 0)),
        cost_estimate=pl.CostEstimate(
            flops=4 * slot_count * (q_width // HEAD) * row_count * cache_length * HEAD,
            transcendentals=2 * slot_count * (q_width // HEAD) * row_count * cache_length,
            bytes_accessed=int(cached.size * 2 + payload.size * 2 + slot_count * row_count * (q_width + TAG_WIDTH) * 2),
        ),
    )(length_col, payload, cached)


def fresh_kernel(q_ref, fresh_ref, mix_ref, sum_ref):
    sessions, row_count, _ = q_ref.shape
    kv_heads = fresh_ref.shape[2] // (2 * HEAD)
    group_size = QHEADS // KVHEADS
    fresh_pos = lax.broadcasted_iota(jnp.int32, (sessions, group_size * row_count, row_count), 2)
    query_row = lax.broadcasted_iota(jnp.int32, (sessions, group_size * row_count, row_count), 1) % row_count
    fresh_seen = fresh_pos <= query_row
    lane = lax.broadcasted_iota(jnp.int32, (sessions, row_count, TAG_WIDTH), 2)
    sums = jnp.zeros((sessions, row_count, TAG_WIDTH), jnp.float32)
    for k in range(kv_heads):
        key_col = 2 * HEAD * k
        grouped = jnp.concatenate(
            [q_ref[:, :, (group_size * k + g) * HEAD:(group_size * k + g + 1) * HEAD] for g in range(group_size)],
            axis=1,
        )
        fresh_keys = fresh_ref[:, :, key_col:key_col + HEAD]
        fresh_values = fresh_ref[:, :, key_col + HEAD:key_col + 2 * HEAD]
        fresh_scores = jnp.einsum("bqd,bkd->bqk", grouped, fresh_keys, preferred_element_type=jnp.float32) * score_scale
        fresh_w = jnp.where(fresh_seen, jnp.exp(soft_cap * jnp.tanh(fresh_scores / soft_cap)), 0.0)
        total = jnp.sum(fresh_w, axis=-1, keepdims=True)
        mixed = jnp.einsum("bqk,bkd->bqd", fresh_w.astype(jnp.bfloat16), fresh_values, preferred_element_type=jnp.float32)
        for g in range(group_size):
            head = group_size * k + g
            col = head * HEAD
            mix_ref[:, :, col:col + HEAD] = mixed[:, g * row_count:(g + 1) * row_count]
            sums = jnp.where(lane == head, total[:, g * row_count:(g + 1) * row_count], sums)
    sum_ref[...] = sums


def attend_fresh(queries, fresh_kv, block=8):
    slot_count, row_count, q_width = queries.shape
    kv_width = fresh_kv.shape[2]
    block = min(block, slot_count)
    return pl.pallas_call(
        fresh_kernel,
        out_shape=(
            jax.ShapeDtypeStruct((slot_count, row_count, q_width), jnp.float32),
            jax.ShapeDtypeStruct((slot_count, row_count, TAG_WIDTH), jnp.float32),
        ),
        grid=(slot_count // block,),
        in_specs=[
            pl.BlockSpec((block, row_count, q_width), lambda b: (b, 0, 0)),
            pl.BlockSpec((block, row_count, kv_width), lambda b: (b, 0, 0)),
        ],
        out_specs=(
            pl.BlockSpec((block, row_count, q_width), lambda b: (b, 0, 0)),
            pl.BlockSpec((block, row_count, TAG_WIDTH), lambda b: (b, 0, 0)),
        ),
        cost_estimate=pl.CostEstimate(
            flops=4 * slot_count * (q_width // HEAD) * row_count * row_count * HEAD,
            transcendentals=2 * slot_count * (q_width // HEAD) * row_count * row_count,
            bytes_accessed=int((queries.size + fresh_kv.size) * 2 + slot_count * row_count * (q_width + TAG_WIDTH) * 4),
        ),
    )(queries, fresh_kv)


def pack_lanes(payload, slot_lanes, lane_count):
    lane_ids = jnp.arange(lane_count, dtype=jnp.int32)
    slot_ids = jnp.arange(payload.shape[0], dtype=jnp.int32)
    lane_hits = slot_lanes[None, :] == lane_ids[:, None]
    filled = jnp.any(lane_hits, axis=1)
    chosen = jnp.sum(jnp.where(lane_hits, slot_ids[None, :], 0), axis=1)
    picked = jnp.take(payload, chosen, axis=0)
    return jnp.where(filled[:, None, None], picked, jnp.zeros((), payload.dtype))


def halving_stages(axis):
    count = lax.axis_size(axis)
    stages = count.bit_length() - 1
    return count, stages if (1 << stages) == count else None


def scatter_sum(partial, axis):
    count, stages = halving_stages(axis)
    rows, width = partial.shape
    if stages is None:
        return lax.psum_scatter(partial, axis, scatter_dimension=1, tiled=True).astype(jnp.float32)
    me = lax.axis_index(axis)
    held = partial.reshape((rows,) + (2,) * stages + (width // count,))
    for s in range(stages):
        bit = (me >> s) & 1
        dim = stages - s
        keep = lax.dynamic_index_in_dim(held, bit, axis=dim, keepdims=False)
        send = lax.dynamic_index_in_dim(held, 1 - bit, axis=dim, keepdims=False)
        got = lax.ppermute(
            send.astype(jnp.bfloat16), axis, perm=[(i, i ^ (1 << s)) for i in range(count)]
        )
        held = keep.astype(jnp.float32) + got.astype(jnp.float32)
    return held


def projection_kernel(block_ref, rows_ref, weight_ref, out_ref):
    out_ref[0] = jnp.dot(rows_ref[...], weight_ref[...], preferred_element_type=jnp.float32).astype(out_ref.dtype)


def project_blocks(rows, weight, blocks):
    row_total, inner = rows.shape
    width = weight.shape[1] // lax.axis_size("tensor")
    count = blocks.shape[0]
    return pl.pallas_call(
        projection_kernel,
        out_shape=jax.ShapeDtypeStruct((count, row_total, width), jnp.bfloat16),
        grid_spec=pltpu.PrefetchScalarGridSpec(
            num_scalar_prefetch=1,
            grid=(count,),
            in_specs=[
                pl.BlockSpec((row_total, inner), lambda j, blk: (0, 0)),
                pl.BlockSpec((inner, width), lambda j, blk: (0, blk[j])),
            ],
            out_specs=pl.BlockSpec((1, row_total, width), lambda j, blk: (j, 0, 0)),
        ),
        cost_estimate=pl.CostEstimate(
            flops=2 * count * row_total * inner * width,
            transcendentals=0,
            bytes_accessed=int(rows.size * 2 + count * (inner * width + row_total * width) * 2),
        ),
    )(blocks, rows, weight)


def bit_reversed(value, bits):
    out = 0
    for b in range(bits):
        out |= ((value >> b) & 1) << (bits - 1 - b)
    return out


def project_and_scatter(rows, weight, axis):
    count = lax.axis_size(axis)
    stages = count.bit_length() - 1
    if (1 << stages) != count or (weight.shape[1] // count) % 128:
        products = jnp.dot(rows, weight, preferred_element_type=jnp.float32).astype(jnp.bfloat16)
        return scatter_sum(products, axis)
    me = lax.axis_index(axis)
    order = jnp.array([bit_reversed(j, stages) for j in range(count)], jnp.int32)
    blocks = jnp.bitwise_xor(me, order)
    half = count // 2
    sent = project_blocks(rows, weight, blocks[half:])
    kept = project_blocks(rows, weight, blocks[:half])
    got = lax.ppermute(sent, axis, perm=[(i, i ^ 1) for i in range(count)])
    held = kept.astype(jnp.float32) + got.astype(jnp.float32)
    for s in range(1, stages):
        half = held.shape[0] // 2
        got = lax.ppermute(
            held[half:].astype(jnp.bfloat16), axis, perm=[(i, i ^ (1 << s)) for i in range(count)]
        )
        held = held[:half] + got.astype(jnp.float32)
    return held[0]


def butterfly_sum(values, axis):
    count, stages = halving_stages(axis)
    if stages is None:
        return lax.psum(values, axis)
    shape = values.shape
    lanes = 128 if values.size % 128 == 0 else values.size
    values = values.reshape(values.size // lanes, lanes)
    for s in range(stages):
        values = values + lax.ppermute(values, axis, perm=[(i, i ^ (1 << s)) for i in range(count)])
    return values.reshape(shape)


def exchange_by_shift(lanes, axis, cap, direction):
    count = lax.axis_size(axis)
    parts = [lanes[:cap]]
    for shift in range(1, count):
        parts.append(
            lax.ppermute(
                lanes[shift * cap:(shift + 1) * cap],
                axis,
                perm=[(i, (i + direction * shift) % count) for i in range(count)],
            )
        )
    return jnp.concatenate(parts, axis=0)


def gather_weights(weight, axis):
    count = lax.axis_size(axis)
    width = weight.shape[1] // count
    me = lax.axis_index(axis)
    if count != 4 or width % 128:
        blocks = weight.reshape(weight.shape[0], count, width).transpose(1, 0, 2)
        return lax.all_to_all(blocks, axis, 0, 0, tiled=True), None

    def cols(peer):
        return lax.dynamic_slice_in_dim(weight, peer * width, width, axis=1)

    outgoing = jnp.stack([cols(me ^ 2), cols(me ^ 3)])
    across = lax.ppermute(outgoing, axis, perm=[(i, i ^ 2) for i in range(count)])
    beside = lax.ppermute(
        jnp.stack([cols(me ^ 1), across[1]]), axis, perm=[(i, i ^ 1) for i in range(count)]
    )
    return jnp.stack([cols(me), across[0], beside[0], beside[1]]), outgoing


def gather_rows(attended, axis, manual):
    count = lax.axis_size(axis)
    if manual is None:
        return lax.all_gather(attended, axis, axis=0, tiled=False)
    across = lax.ppermute(attended, axis, perm=[(i, i ^ 2) for i in range(count)])
    beside = lax.ppermute(jnp.stack([attended, across]), axis, perm=[(i, i ^ 1) for i in range(count)])
    return jnp.stack([attended, across, beside[0], beside[1]])


def shards(kv_cache, lengths, source, queries, fresh_kv, out_weight, norm_gain):
    dp_count = lax.axis_size("dp")
    me = lax.axis_index("dp")
    slot_count, row_count, query_width = queries.shape
    kv_width = fresh_kv.shape[2]
    pair_cap = max(1, slot_count // dp_count)
    lane_count = dp_count * pair_cap
    slot_ids = jnp.arange(slot_count, dtype=jnp.int32)
    lane_ids = jnp.arange(lane_count, dtype=jnp.int32)

    old_home = source // slot_count
    old_slot = source % slot_count
    earlier = slot_ids[None, :] < slot_ids[:, None]
    same_home = old_home[:, None] == old_home[None, :]
    rank = jnp.sum(same_home & earlier, axis=1)
    shift = (old_home - me) % dp_count
    out_lane = shift * pair_cap + rank
    tag = jnp.broadcast_to(
        (old_slot + 1).astype(jnp.bfloat16)[:, None, None], (slot_count, row_count, TAG_WIDTH)
    )
    payload = jnp.concatenate([queries, tag], axis=2)
    peer_weights, manual = gather_weights(out_weight, "tensor")
    if manual is not None:
        payload = lax.optimization_barrier((payload, manual))[0]
    sending = pack_lanes(payload, out_lane, lane_count)
    arrived = exchange_by_shift(sending, "dp", pair_cap, 1)
    fresh_mix, fresh_sum = attend_fresh(queries, fresh_kv)

    lane_slot = arrived[:, 0, query_width].astype(jnp.int32) - 1
    hits = lane_slot[None, :] == slot_ids[:, None]
    slot_lane = jnp.sum(jnp.where(hits, lane_ids[None, :], 0), axis=1)
    gathered = jnp.take(arrived, slot_lane, axis=0)
    cache_part = attend_cache(gathered, kv_cache, lengths, query_width)

    filled = lane_slot >= 0
    back = jnp.take(cache_part, jnp.maximum(lane_slot, 0), axis=0)
    back = jnp.where(filled[:, None, None], back, jnp.zeros((), back.dtype))
    returned = exchange_by_shift(back, "dp", pair_cap, -1)
    cache_here = jnp.take(returned, out_lane, axis=0)

    heads = query_width // HEAD
    sums = cache_here[:, :, query_width:].astype(jnp.float32)
    cache_sum = sums[:, :, :heads] + sums[:, :, TAG_WIDTH // 2:TAG_WIDTH // 2 + heads]
    total = cache_sum + fresh_sum[:, :, :heads]
    cache_mix = cache_here[:, :, :query_width].astype(jnp.float32).reshape(slot_count, row_count, heads, HEAD)
    joined = cache_mix * cache_sum[..., None] + fresh_mix.reshape(slot_count, row_count, heads, HEAD)
    attended_here = (joined / total[..., None]).astype(jnp.bfloat16).reshape(slot_count, row_count, query_width)

    row_total = slot_count * row_count
    flat_rows = attended_here.reshape(row_total, query_width)
    model_width = out_weight.shape[1]
    every_rows = gather_rows(flat_rows, "tensor", manual)
    peers = every_rows.shape[0]
    own_part = jnp.dot(flat_rows, peer_weights[0], preferred_element_type=jnp.float32)
    rest_rows = jnp.concatenate([every_rows[i] for i in range(1, peers)], axis=1)
    rest_weights = jnp.concatenate([peer_weights[i] for i in range(1, peers)], axis=0)
    own_part = own_part + jnp.dot(rest_rows, rest_weights, preferred_element_type=jnp.float32)
    square_sum = jnp.sum(own_part * own_part, axis=-1)
    square_sum = butterfly_sum(square_sum, "tensor").reshape(row_total, 1)
    mean_square = square_sum / model_width
    normed = own_part * lax.rsqrt(mean_square + norm_eps) * norm_gain
    return normed.astype(jnp.bfloat16).reshape(slot_count, row_count, own_part.shape[1])


def solution(mesh):
    placed = (
        P(("groups", "dp"), None, "tensor"),
        P(("groups", "dp")),
        P(("groups", "dp")),
        P(("groups", "dp"), None, "tensor"),
        P(("groups", "dp"), None, "tensor"),
        P("tensor", None),
        P("tensor"),
    )
    return jax.shard_map(
        shards,
        mesh=mesh,
        in_specs=placed,
        out_specs=P(("groups", "dp"), None, "tensor"),
        check_vma=False,
    )
```

```python
import functools

import jax
import jax.numpy as jnp
from jax import lax
from jax.experimental import pallas as pl
from jax.experimental.pallas import tpu as pltpu
from jax.sharding import PartitionSpec as P

HEAD = 128
QHEADS = 16
KVHEADS = 8
TAG_WIDTH = 128


score_scale = 144.0 ** (-0.5)
soft_cap = 50.0
norm_eps = 1e-06


def attention_kernel(lane_ref, length_ref, pay_ref, cache_ref, out_ref, *, q_width):
    step = pl.program_id(0)
    sessions, cache_length, _ = cache_ref.shape
    row_count = pay_ref.shape[1]
    kv_heads = cache_ref.shape[2] // (2 * HEAD)
    group_size = QHEADS // KVHEADS
    lanes = [lane_ref[step * sessions + i] for i in range(sessions)]
    queries = jnp.stack([pay_ref[lane] for lane in lanes])
    lengths = length_ref[...]
    cache_pos = lax.broadcasted_iota(jnp.int32, (sessions, group_size * row_count, cache_length), 2)
    cache_seen = cache_pos < lengths
    lane_ids = lax.broadcasted_iota(jnp.int32, (sessions, row_count, TAG_WIDTH), 2)
    sums = jnp.zeros((sessions, row_count, TAG_WIDTH), jnp.float32)
    mixes = []
    for k in range(kv_heads):
        key_col = 2 * HEAD * k
        grouped = jnp.concatenate(
            [queries[:, :, (group_size * k + g) * HEAD:(group_size * k + g + 1) * HEAD] for g in range(group_size)],
            axis=1,
        )
        cache_keys = cache_ref[:, :, key_col:key_col + HEAD]
        cache_values = cache_ref[:, :, key_col + HEAD:key_col + 2 * HEAD]
        cache_scores = jnp.einsum("bqd,bkd->bqk", grouped, cache_keys, preferred_element_type=jnp.float32) * score_scale
        cache_w = jnp.where(cache_seen, jnp.exp(soft_cap * jnp.tanh(cache_scores / soft_cap)), 0.0)
        total = jnp.sum(cache_w, axis=-1, keepdims=True)
        mixed = jnp.einsum("bqk,bkd->bqd", cache_w.astype(jnp.bfloat16), cache_values, preferred_element_type=jnp.float32)
        mixed = (mixed / total).astype(out_ref.dtype)
        high = total.astype(jnp.bfloat16).astype(jnp.float32)
        low = total - high
        for g in range(group_size):
            head = group_size * k + g
            mixes.append(mixed[:, g * row_count:(g + 1) * row_count])
            sums = jnp.where(lane_ids == head, high[:, g * row_count:(g + 1) * row_count], sums)
            sums = jnp.where(lane_ids == TAG_WIDTH // 2 + head, low[:, g * row_count:(g + 1) * row_count], sums)
    result = jnp.concatenate(mixes + [sums.astype(out_ref.dtype)], axis=2)
    for i, lane in enumerate(lanes):
        out_ref[lane] = result[i]


def attend_cache(arrived, cached, lengths, slot_lane, q_width, block=8):
    lane_count, row_count, pay_width = arrived.shape
    slot_count, cache_length, kv_width = cached.shape
    block = min(block, slot_count)
    length_col = lengths.reshape(slot_count, 1, 1)
    return pl.pallas_call(
        functools.partial(attention_kernel, q_width=q_width),
        out_shape=jax.ShapeDtypeStruct((lane_count, row_count, q_width + TAG_WIDTH), jnp.bfloat16),
        grid_spec=pltpu.PrefetchScalarGridSpec(
            num_scalar_prefetch=1,
            grid=(slot_count // block,),
            in_specs=[
                pl.BlockSpec((block, 1, 1), lambda b, lanes: (b, 0, 0)),
                pl.BlockSpec((lane_count, row_count, pay_width), lambda b, lanes: (0, 0, 0)),
                pl.BlockSpec((block, cache_length, kv_width), lambda b, lanes: (b, 0, 0)),
            ],
            out_specs=pl.BlockSpec((lane_count, row_count, q_width + TAG_WIDTH), lambda b, lanes: (0, 0, 0)),
        ),
        cost_estimate=pl.CostEstimate(
            flops=4 * slot_count * (q_width // HEAD) * row_count * cache_length * HEAD,
            transcendentals=2 * slot_count * (q_width // HEAD) * row_count * cache_length,
            bytes_accessed=int(cached.size * 2 + arrived.size * 2 + lane_count * row_count * (q_width + TAG_WIDTH) * 2),
        ),
    )(slot_lane, length_col, arrived, cached)


def fresh_kernel(q_ref, fresh_ref, mix_ref, sum_ref):
    sessions, row_count, _ = q_ref.shape
    kv_heads = fresh_ref.shape[2] // (2 * HEAD)
    group_size = QHEADS // KVHEADS
    fresh_pos = lax.broadcasted_iota(jnp.int32, (sessions, group_size * row_count, row_count), 2)
    query_row = lax.broadcasted_iota(jnp.int32, (sessions, group_size * row_count, row_count), 1) % row_count
    fresh_seen = fresh_pos <= query_row
    lane = lax.broadcasted_iota(jnp.int32, (sessions, row_count, TAG_WIDTH), 2)
    sums = jnp.zeros((sessions, row_count, TAG_WIDTH), jnp.float32)
    for k in range(kv_heads):
        key_col = 2 * HEAD * k
        grouped = jnp.concatenate(
            [q_ref[:, :, (group_size * k + g) * HEAD:(group_size * k + g + 1) * HEAD] for g in range(group_size)],
            axis=1,
        )
        fresh_keys = fresh_ref[:, :, key_col:key_col + HEAD]
        fresh_values = fresh_ref[:, :, key_col + HEAD:key_col + 2 * HEAD]
        fresh_scores = jnp.einsum("bqd,bkd->bqk", grouped, fresh_keys, preferred_element_type=jnp.float32) * score_scale
        fresh_w = jnp.where(fresh_seen, jnp.exp(soft_cap * jnp.tanh(fresh_scores / soft_cap)), 0.0)
        total = jnp.sum(fresh_w, axis=-1, keepdims=True)
        mixed = jnp.einsum("bqk,bkd->bqd", fresh_w.astype(jnp.bfloat16), fresh_values, preferred_element_type=jnp.float32)
        for g in range(group_size):
            head = group_size * k + g
            col = head * HEAD
            mix_ref[:, :, col:col + HEAD] = mixed[:, g * row_count:(g + 1) * row_count]
            sums = jnp.where(lane == head, total[:, g * row_count:(g + 1) * row_count], sums)
    sum_ref[...] = sums


def attend_fresh(queries, fresh_kv, block=8):
    slot_count, row_count, q_width = queries.shape
    kv_width = fresh_kv.shape[2]
    block = min(block, slot_count)
    return pl.pallas_call(
        fresh_kernel,
        out_shape=(
            jax.ShapeDtypeStruct((slot_count, row_count, q_width), jnp.float32),
            jax.ShapeDtypeStruct((slot_count, row_count, TAG_WIDTH), jnp.float32),
        ),
        grid=(slot_count // block,),
        in_specs=[
            pl.BlockSpec((block, row_count, q_width), lambda b: (b, 0, 0)),
            pl.BlockSpec((block, row_count, kv_width), lambda b: (b, 0, 0)),
        ],
        out_specs=(
            pl.BlockSpec((block, row_count, q_width), lambda b: (b, 0, 0)),
            pl.BlockSpec((block, row_count, TAG_WIDTH), lambda b: (b, 0, 0)),
        ),
        cost_estimate=pl.CostEstimate(
            flops=4 * slot_count * (q_width // HEAD) * row_count * row_count * HEAD,
            transcendentals=2 * slot_count * (q_width // HEAD) * row_count * row_count,
            bytes_accessed=int((queries.size + fresh_kv.size) * 2 + slot_count * row_count * (q_width + TAG_WIDTH) * 4),
        ),
    )(queries, fresh_kv)


def pack_lanes(payload, slot_lanes, lane_count):
    lane_ids = jnp.arange(lane_count, dtype=jnp.int32)
    slot_ids = jnp.arange(payload.shape[0], dtype=jnp.int32)
    lane_hits = slot_lanes[None, :] == lane_ids[:, None]
    filled = jnp.any(lane_hits, axis=1)
    chosen = jnp.sum(jnp.where(lane_hits, slot_ids[None, :], 0), axis=1)
    picked = jnp.take(payload, chosen, axis=0)
    return jnp.where(filled[:, None, None], picked, jnp.zeros((), payload.dtype))


def halving_stages(axis):
    count = lax.axis_size(axis)
    stages = count.bit_length() - 1
    return count, stages if (1 << stages) == count else None


def scatter_sum(partial, axis):
    count, stages = halving_stages(axis)
    rows, width = partial.shape
    if stages is None:
        return lax.psum_scatter(partial, axis, scatter_dimension=1, tiled=True).astype(jnp.float32)
    me = lax.axis_index(axis)
    held = partial.reshape((rows,) + (2,) * stages + (width // count,))
    for s in range(stages):
        bit = (me >> s) & 1
        dim = stages - s
        keep = lax.dynamic_index_in_dim(held, bit, axis=dim, keepdims=False)
        send = lax.dynamic_index_in_dim(held, 1 - bit, axis=dim, keepdims=False)
        got = lax.ppermute(
            send.astype(jnp.bfloat16), axis, perm=[(i, i ^ (1 << s)) for i in range(count)]
        )
        held = keep.astype(jnp.float32) + got.astype(jnp.float32)
    return held


def projection_kernel(block_ref, rows_ref, weight_ref, out_ref):
    out_ref[0] = jnp.dot(rows_ref[...], weight_ref[...], preferred_element_type=jnp.float32).astype(out_ref.dtype)


def project_blocks(rows, weight, blocks):
    row_total, inner = rows.shape
    width = weight.shape[1] // lax.axis_size("tensor")
    count = blocks.shape[0]
    return pl.pallas_call(
        projection_kernel,
        out_shape=jax.ShapeDtypeStruct((count, row_total, width), jnp.bfloat16),
        grid_spec=pltpu.PrefetchScalarGridSpec(
            num_scalar_prefetch=1,
            grid=(count,),
            in_specs=[
                pl.BlockSpec((row_total, inner), lambda j, blk: (0, 0)),
                pl.BlockSpec((inner, width), lambda j, blk: (0, blk[j])),
            ],
            out_specs=pl.BlockSpec((1, row_total, width), lambda j, blk: (j, 0, 0)),
        ),
        cost_estimate=pl.CostEstimate(
            flops=2 * count * row_total * inner * width,
            transcendentals=0,
            bytes_accessed=int(rows.size * 2 + count * (inner * width + row_total * width) * 2),
        ),
    )(blocks, rows, weight)


def bit_reversed(value, bits):
    out = 0
    for b in range(bits):
        out |= ((value >> b) & 1) << (bits - 1 - b)
    return out


def project_and_scatter(rows, weight, axis):
    count = lax.axis_size(axis)
    stages = count.bit_length() - 1
    if (1 << stages) != count or (weight.shape[1] // count) % 128:
        products = jnp.dot(rows, weight, preferred_element_type=jnp.float32).astype(jnp.bfloat16)
        return scatter_sum(products, axis)
    me = lax.axis_index(axis)
    order = jnp.array([bit_reversed(j, stages) for j in range(count)], jnp.int32)
    blocks = jnp.bitwise_xor(me, order)
    half = count // 2
    sent = project_blocks(rows, weight, blocks[half:])
    kept = project_blocks(rows, weight, blocks[:half])
    got = lax.ppermute(sent, axis, perm=[(i, i ^ 1) for i in range(count)])
    held = kept.astype(jnp.float32) + got.astype(jnp.float32)
    for s in range(1, stages):
        half = held.shape[0] // 2
        got = lax.ppermute(
            held[half:].astype(jnp.bfloat16), axis, perm=[(i, i ^ (1 << s)) for i in range(count)]
        )
        held = held[:half] + got.astype(jnp.float32)
    return held[0]


def butterfly_sum(values, axis):
    count, stages = halving_stages(axis)
    if stages is None:
        return lax.psum(values, axis)
    shape = values.shape
    lanes = 128 if values.size % 128 == 0 else values.size
    values = values.reshape(values.size // lanes, lanes)
    for s in range(stages):
        values = values + lax.ppermute(values, axis, perm=[(i, i ^ (1 << s)) for i in range(count)])
    return values.reshape(shape)


def exchange_by_shift(lanes, axis, cap, direction):
    count = lax.axis_size(axis)
    parts = [lanes[:cap]]
    for shift in range(1, count):
        parts.append(
            lax.ppermute(
                lanes[shift * cap:(shift + 1) * cap],
                axis,
                perm=[(i, (i + direction * shift) % count) for i in range(count)],
            )
        )
    return jnp.concatenate(parts, axis=0)


def shards(kv_cache, lengths, source, queries, fresh_kv, out_weight, norm_gain):
    dp_count = lax.axis_size("dp")
    me = lax.axis_index("dp")
    slot_count, row_count, query_width = queries.shape
    kv_width = fresh_kv.shape[2]
    pair_cap = max(1, slot_count // dp_count)
    lane_count = dp_count * pair_cap
    slot_ids = jnp.arange(slot_count, dtype=jnp.int32)
    lane_ids = jnp.arange(lane_count, dtype=jnp.int32)

    old_home = source // slot_count
    old_slot = source % slot_count
    earlier = slot_ids[None, :] < slot_ids[:, None]
    same_home = old_home[:, None] == old_home[None, :]
    rank = jnp.sum(same_home & earlier, axis=1)
    shift = (old_home - me) % dp_count
    out_lane = shift * pair_cap + rank
    tag = jnp.broadcast_to(
        (old_slot + 1).astype(jnp.bfloat16)[:, None, None], (slot_count, row_count, TAG_WIDTH)
    )
    payload = jnp.concatenate([queries, tag], axis=2)
    sending = pack_lanes(payload, out_lane, lane_count)
    arrived = exchange_by_shift(sending, "dp", pair_cap, 1)
    fresh_mix, fresh_sum = attend_fresh(queries, fresh_kv)

    lane_slot = arrived[:, 0, query_width].astype(jnp.int32) - 1
    hits = lane_slot[None, :] == slot_ids[:, None]
    slot_lane = jnp.clip(jnp.sum(jnp.where(hits, lane_ids[None, :], 0), axis=1), 0, lane_count - 1)
    back = attend_cache(arrived, kv_cache, lengths, slot_lane, query_width)
    returned = exchange_by_shift(back, "dp", pair_cap, -1)
    cache_here = jnp.take(returned, out_lane, axis=0)

    heads = query_width // HEAD
    sums = cache_here[:, :, query_width:].astype(jnp.float32)
    cache_sum = sums[:, :, :heads] + sums[:, :, TAG_WIDTH // 2:TAG_WIDTH // 2 + heads]
    total = cache_sum + fresh_sum[:, :, :heads]
    cache_mix = cache_here[:, :, :query_width].astype(jnp.float32).reshape(slot_count, row_count, heads, HEAD)
    joined = cache_mix * cache_sum[..., None] + fresh_mix.reshape(slot_count, row_count, heads, HEAD)
    attended_here = (joined / total[..., None]).astype(jnp.bfloat16).reshape(slot_count, row_count, query_width)

    row_total = slot_count * row_count
    flat_rows = attended_here.reshape(row_total, query_width)
    model_width = out_weight.shape[1]
    own_part = project_and_scatter(flat_rows, out_weight, "tensor")
    square_sum = jnp.sum(own_part * own_part, axis=-1)
    square_sum = butterfly_sum(square_sum, "tensor").reshape(row_total, 1)
    mean_square = square_sum / model_width
    normed = own_part * lax.rsqrt(mean_square + norm_eps) * norm_gain
    return normed.astype(jnp.bfloat16).reshape(slot_count, row_count, own_part.shape[1])


def solution(mesh):
    placed = (
        P(("groups", "dp"), None, "tensor"),
        P(("groups", "dp")),
        P(("groups", "dp")),
        P(("groups", "dp"), None, "tensor"),
        P(("groups", "dp"), None, "tensor"),
        P("tensor", None),
        P("tensor"),
    )
    return jax.shard_map(
        shards,
        mesh=mesh,
        in_specs=placed,
        out_specs=P(("groups", "dp"), None, "tensor"),
        check_vma=False,
    )
```

```python
import functools

import jax
import jax.numpy as jnp
from jax import lax
from jax.experimental import pallas as pl
from jax.experimental.pallas import tpu as pltpu
from jax.sharding import PartitionSpec as P

HEAD = 128
QHEADS = 16
KVHEADS = 8
TAG_WIDTH = 128


score_scale = 144.0 ** (-0.5)
soft_cap = 50.0
norm_eps = 1e-06


def attention_kernel(lane_ref, length_ref, pay_ref, cache_ref, out_ref, *, q_width):
    step = pl.program_id(0)
    sessions, cache_length, _ = cache_ref.shape
    row_count = pay_ref.shape[1]
    kv_heads = cache_ref.shape[2] // (2 * HEAD)
    group_size = QHEADS // KVHEADS
    lanes = [lane_ref[step * sessions + i] for i in range(sessions)]
    queries = jnp.stack([pay_ref[lane] for lane in lanes])
    lengths = length_ref[...]
    cache_pos = lax.broadcasted_iota(jnp.int32, (sessions, group_size * row_count, cache_length), 2)
    cache_seen = cache_pos < lengths
    lane_ids = lax.broadcasted_iota(jnp.int32, (sessions, row_count, TAG_WIDTH), 2)
    sums = jnp.zeros((sessions, row_count, TAG_WIDTH), jnp.float32)
    mixes = []
    for k in range(kv_heads):
        key_col = 2 * HEAD * k
        grouped = jnp.concatenate(
            [queries[:, :, (group_size * k + g) * HEAD:(group_size * k + g + 1) * HEAD] for g in range(group_size)],
            axis=1,
        )
        cache_keys = cache_ref[:, :, key_col:key_col + HEAD]
        cache_values = cache_ref[:, :, key_col + HEAD:key_col + 2 * HEAD]
        cache_scores = jnp.einsum("bqd,bkd->bqk", grouped, cache_keys, preferred_element_type=jnp.float32) * score_scale
        cache_w = jnp.where(cache_seen, jnp.exp(soft_cap * jnp.tanh(cache_scores / soft_cap)), 0.0)
        total = jnp.sum(cache_w, axis=-1, keepdims=True)
        mixed = jnp.einsum("bqk,bkd->bqd", cache_w.astype(jnp.bfloat16), cache_values, preferred_element_type=jnp.float32)
        mixed = (mixed / total).astype(out_ref.dtype)
        high = total.astype(jnp.bfloat16).astype(jnp.float32)
        low = total - high
        for g in range(group_size):
            head = group_size * k + g
            mixes.append(mixed[:, g * row_count:(g + 1) * row_count])
            sums = jnp.where(lane_ids == head, high[:, g * row_count:(g + 1) * row_count], sums)
            sums = jnp.where(lane_ids == TAG_WIDTH // 2 + head, low[:, g * row_count:(g + 1) * row_count], sums)
    result = jnp.concatenate(mixes + [sums.astype(out_ref.dtype)], axis=2)
    for i, lane in enumerate(lanes):
        out_ref[lane] = result[i]


def attend_cache(arrived, cached, lengths, slot_lane, q_width, block=8):
    lane_count, row_count, pay_width = arrived.shape
    slot_count, cache_length, kv_width = cached.shape
    block = min(block, slot_count)
    length_col = lengths.reshape(slot_count, 1, 1)
    return pl.pallas_call(
        functools.partial(attention_kernel, q_width=q_width),
        out_shape=jax.ShapeDtypeStruct((lane_count, row_count, q_width + TAG_WIDTH), jnp.bfloat16),
        grid_spec=pltpu.PrefetchScalarGridSpec(
            num_scalar_prefetch=1,
            grid=(slot_count // block,),
            in_specs=[
                pl.BlockSpec((block, 1, 1), lambda b, lanes: (b, 0, 0)),
                pl.BlockSpec((lane_count, row_count, pay_width), lambda b, lanes: (0, 0, 0)),
                pl.BlockSpec((block, cache_length, kv_width), lambda b, lanes: (b, 0, 0)),
            ],
            out_specs=pl.BlockSpec((lane_count, row_count, q_width + TAG_WIDTH), lambda b, lanes: (0, 0, 0)),
        ),
        cost_estimate=pl.CostEstimate(
            flops=4 * slot_count * (q_width // HEAD) * row_count * cache_length * HEAD,
            transcendentals=2 * slot_count * (q_width // HEAD) * row_count * cache_length,
            bytes_accessed=int(cached.size * 2 + arrived.size * 2 + lane_count * row_count * (q_width + TAG_WIDTH) * 2),
        ),
    )(slot_lane, length_col, arrived, cached)


def fresh_kernel(q_ref, fresh_ref, mix_ref, sum_ref):
    sessions, row_count, _ = q_ref.shape
    kv_heads = fresh_ref.shape[2] // (2 * HEAD)
    group_size = QHEADS // KVHEADS
    fresh_pos = lax.broadcasted_iota(jnp.int32, (sessions, group_size * row_count, row_count), 2)
    query_row = lax.broadcasted_iota(jnp.int32, (sessions, group_size * row_count, row_count), 1) % row_count
    fresh_seen = fresh_pos <= query_row
    lane = lax.broadcasted_iota(jnp.int32, (sessions, row_count, TAG_WIDTH), 2)
    sums = jnp.zeros((sessions, row_count, TAG_WIDTH), jnp.float32)
    for k in range(kv_heads):
        key_col = 2 * HEAD * k
        grouped = jnp.concatenate(
            [q_ref[:, :, (group_size * k + g) * HEAD:(group_size * k + g + 1) * HEAD] for g in range(group_size)],
            axis=1,
        )
        fresh_keys = fresh_ref[:, :, key_col:key_col + HEAD]
        fresh_values = fresh_ref[:, :, key_col + HEAD:key_col + 2 * HEAD]
        fresh_scores = jnp.einsum("bqd,bkd->bqk", grouped, fresh_keys, preferred_element_type=jnp.float32) * score_scale
        fresh_w = jnp.where(fresh_seen, jnp.exp(soft_cap * jnp.tanh(fresh_scores / soft_cap)), 0.0)
        total = jnp.sum(fresh_w, axis=-1, keepdims=True)
        mixed = jnp.einsum("bqk,bkd->bqd", fresh_w.astype(jnp.bfloat16), fresh_values, preferred_element_type=jnp.float32)
        for g in range(group_size):
            head = group_size * k + g
            col = head * HEAD
            mix_ref[:, :, col:col + HEAD] = mixed[:, g * row_count:(g + 1) * row_count]
            sums = jnp.where(lane == head, total[:, g * row_count:(g + 1) * row_count], sums)
    sum_ref[...] = sums


def attend_fresh(queries, fresh_kv, block=8):
    slot_count, row_count, q_width = queries.shape
    kv_width = fresh_kv.shape[2]
    block = min(block, slot_count)
    return pl.pallas_call(
        fresh_kernel,
        out_shape=(
            jax.ShapeDtypeStruct((slot_count, row_count, q_width), jnp.float32),
            jax.ShapeDtypeStruct((slot_count, row_count, TAG_WIDTH), jnp.float32),
        ),
        grid=(slot_count // block,),
        in_specs=[
            pl.BlockSpec((block, row_count, q_width), lambda b: (b, 0, 0)),
            pl.BlockSpec((block, row_count, kv_width), lambda b: (b, 0, 0)),
        ],
        out_specs=(
            pl.BlockSpec((block, row_count, q_width), lambda b: (b, 0, 0)),
            pl.BlockSpec((block, row_count, TAG_WIDTH), lambda b: (b, 0, 0)),
        ),
        cost_estimate=pl.CostEstimate(
            flops=4 * slot_count * (q_width // HEAD) * row_count * row_count * HEAD,
            transcendentals=2 * slot_count * (q_width // HEAD) * row_count * row_count,
            bytes_accessed=int((queries.size + fresh_kv.size) * 2 + slot_count * row_count * (q_width + TAG_WIDTH) * 4),
        ),
    )(queries, fresh_kv)


def pack_lanes(payload, slot_lanes, lane_count):
    lane_ids = jnp.arange(lane_count, dtype=jnp.int32)
    slot_ids = jnp.arange(payload.shape[0], dtype=jnp.int32)
    lane_hits = slot_lanes[None, :] == lane_ids[:, None]
    filled = jnp.any(lane_hits, axis=1)
    chosen = jnp.sum(jnp.where(lane_hits, slot_ids[None, :], 0), axis=1)
    picked = jnp.take(payload, chosen, axis=0)
    return jnp.where(filled[:, None, None], picked, jnp.zeros((), payload.dtype))


def halving_stages(axis):
    count = lax.axis_size(axis)
    stages = count.bit_length() - 1
    return count, stages if (1 << stages) == count else None


def scatter_sum(partial, axis):
    count, stages = halving_stages(axis)
    rows, width = partial.shape
    if stages is None:
        return lax.psum_scatter(partial, axis, scatter_dimension=1, tiled=True).astype(jnp.float32)
    me = lax.axis_index(axis)
    held = partial.reshape((rows,) + (2,) * stages + (width // count,))
    for s in range(stages):
        bit = (me >> s) & 1
        dim = stages - s
        keep = lax.dynamic_index_in_dim(held, bit, axis=dim, keepdims=False)
        send = lax.dynamic_index_in_dim(held, 1 - bit, axis=dim, keepdims=False)
        got = lax.ppermute(
            send.astype(jnp.bfloat16), axis, perm=[(i, i ^ (1 << s)) for i in range(count)]
        )
        held = keep.astype(jnp.float32) + got.astype(jnp.float32)
    return held


def projection_kernel(block_ref, rows_ref, weight_ref, out_ref):
    out_ref[0] = jnp.dot(rows_ref[...], weight_ref[...], preferred_element_type=jnp.float32).astype(out_ref.dtype)


def project_blocks(rows, weight, blocks):
    row_total, inner = rows.shape
    width = weight.shape[1] // lax.axis_size("tensor")
    count = blocks.shape[0]
    return pl.pallas_call(
        projection_kernel,
        out_shape=jax.ShapeDtypeStruct((count, row_total, width), jnp.bfloat16),
        grid_spec=pltpu.PrefetchScalarGridSpec(
            num_scalar_prefetch=1,
            grid=(count,),
            in_specs=[
                pl.BlockSpec((row_total, inner), lambda j, blk: (0, 0)),
                pl.BlockSpec((inner, width), lambda j, blk: (0, blk[j])),
            ],
            out_specs=pl.BlockSpec((1, row_total, width), lambda j, blk: (j, 0, 0)),
        ),
        cost_estimate=pl.CostEstimate(
            flops=2 * count * row_total * inner * width,
            transcendentals=0,
            bytes_accessed=int(rows.size * 2 + count * (inner * width + row_total * width) * 2),
        ),
    )(blocks, rows, weight)


def bit_reversed(value, bits):
    out = 0
    for b in range(bits):
        out |= ((value >> b) & 1) << (bits - 1 - b)
    return out


def project_and_scatter(rows, weight, axis):
    count = lax.axis_size(axis)
    stages = count.bit_length() - 1
    if (1 << stages) != count or (weight.shape[1] // count) % 128:
        products = jnp.dot(rows, weight, preferred_element_type=jnp.float32).astype(jnp.bfloat16)
        return scatter_sum(products, axis)
    me = lax.axis_index(axis)
    order = jnp.array([bit_reversed(j, stages) for j in range(count)], jnp.int32)
    blocks = jnp.bitwise_xor(me, order)
    half = count // 2
    sent = project_blocks(rows, weight, blocks[half:])
    kept = project_blocks(rows, weight, blocks[:half])
    got = lax.ppermute(sent, axis, perm=[(i, i ^ 1) for i in range(count)])
    held = kept.astype(jnp.float32) + got.astype(jnp.float32)
    for s in range(1, stages):
        half = held.shape[0] // 2
        got = lax.ppermute(
            held[half:].astype(jnp.bfloat16), axis, perm=[(i, i ^ (1 << s)) for i in range(count)]
        )
        held = held[:half] + got.astype(jnp.float32)
    return held[0]


def butterfly_sum(values, axis):
    count, stages = halving_stages(axis)
    if stages is None:
        return lax.psum(values, axis)
    shape = values.shape
    lanes = 128 if values.size % 128 == 0 else values.size
    values = values.reshape(values.size // lanes, lanes)
    for s in range(stages):
        values = values + lax.ppermute(values, axis, perm=[(i, i ^ (1 << s)) for i in range(count)])
    return values.reshape(shape)


def exchange_by_shift(lanes, axis, cap, direction):
    count = lax.axis_size(axis)
    parts = [lanes[:cap]]
    for shift in range(1, count):
        parts.append(
            lax.ppermute(
                lanes[shift * cap:(shift + 1) * cap],
                axis,
                perm=[(i, (i + direction * shift) % count) for i in range(count)],
            )
        )
    return jnp.concatenate(parts, axis=0)


def gather_weights(weight, axis):
    count = lax.axis_size(axis)
    width = weight.shape[1] // count
    me = lax.axis_index(axis)
    if count != 4 or width % 128:
        blocks = weight.reshape(weight.shape[0], count, width).transpose(1, 0, 2)
        return lax.all_to_all(blocks, axis, 0, 0, tiled=True), None

    def cols(peer):
        return lax.dynamic_slice_in_dim(weight, peer * width, width, axis=1)

    replicas = lax.axis_size("groups")
    if replicas == 2 and weight.shape[0] % 32 == 0:
        group = lax.axis_index("groups")
        half = weight.shape[0] // 2
        mine = lax.dynamic_slice_in_dim(jnp.stack([cols(me ^ 2), cols(me ^ 3)]), group * half, half, axis=1)
        piece = half // 2
        got_parts = [
            lax.ppermute(mine[:, p * piece:(p + 1) * piece], axis, perm=[(i, i ^ 2) for i in range(count)])
            for p in range(2)
        ]
        other_parts = [lax.ppermute(part, "groups", perm=[(0, 1), (1, 0)]) for part in got_parts]
        got = jnp.concatenate(got_parts, axis=1)
        other = jnp.concatenate(other_parts, axis=1)
        across = jnp.where(group == 0, jnp.concatenate([got, other], axis=1), jnp.concatenate([other, got], axis=1))
    else:
        across = lax.ppermute(
            jnp.stack([cols(me ^ 2), cols(me ^ 3)]), axis, perm=[(i, i ^ 2) for i in range(count)]
        )
    beside = lax.ppermute(
        jnp.stack([cols(me ^ 1), across[1]]), axis, perm=[(i, i ^ 1) for i in range(count)]
    )
    return jnp.stack([cols(me), across[0], beside[0], beside[1]]), True


def gather_rows(attended, axis, manual):
    count = lax.axis_size(axis)
    if manual is None:
        return lax.all_gather(attended, axis, axis=0, tiled=False)
    across = lax.ppermute(attended, axis, perm=[(i, i ^ 2) for i in range(count)])
    beside = lax.ppermute(jnp.stack([attended, across]), axis, perm=[(i, i ^ 1) for i in range(count)])
    return jnp.stack([attended, across, beside[0], beside[1]])


def shards(kv_cache, lengths, source, queries, fresh_kv, out_weight, norm_gain):
    dp_count = lax.axis_size("dp")
    me = lax.axis_index("dp")
    slot_count, row_count, query_width = queries.shape
    kv_width = fresh_kv.shape[2]
    pair_cap = max(1, slot_count // dp_count)
    lane_count = dp_count * pair_cap
    slot_ids = jnp.arange(slot_count, dtype=jnp.int32)
    lane_ids = jnp.arange(lane_count, dtype=jnp.int32)

    old_home = source // slot_count
    old_slot = source % slot_count
    earlier = slot_ids[None, :] < slot_ids[:, None]
    same_home = old_home[:, None] == old_home[None, :]
    rank = jnp.sum(same_home & earlier, axis=1)
    shift = (old_home - me) % dp_count
    out_lane = shift * pair_cap + rank
    tag = jnp.broadcast_to(
        (old_slot + 1).astype(jnp.bfloat16)[:, None, None], (slot_count, row_count, TAG_WIDTH)
    )
    payload = jnp.concatenate([queries, tag], axis=2)
    peer_weights, manual = gather_weights(out_weight, "tensor")
    sending = pack_lanes(payload, out_lane, lane_count)
    arrived = exchange_by_shift(sending, "dp", pair_cap, 1)
    fresh_mix, fresh_sum = attend_fresh(queries, fresh_kv)

    lane_slot = arrived[:, 0, query_width].astype(jnp.int32) - 1
    hits = lane_slot[None, :] == slot_ids[:, None]
    slot_lane = jnp.clip(jnp.sum(jnp.where(hits, lane_ids[None, :], 0), axis=1), 0, lane_count - 1)
    back = attend_cache(arrived, kv_cache, lengths, slot_lane, query_width)
    returned = exchange_by_shift(back, "dp", pair_cap, -1)
    cache_here = jnp.take(returned, out_lane, axis=0)

    heads = query_width // HEAD
    sums = cache_here[:, :, query_width:].astype(jnp.float32)
    cache_sum = sums[:, :, :heads] + sums[:, :, TAG_WIDTH // 2:TAG_WIDTH // 2 + heads]
    total = cache_sum + fresh_sum[:, :, :heads]
    cache_mix = cache_here[:, :, :query_width].astype(jnp.float32).reshape(slot_count, row_count, heads, HEAD)
    joined = cache_mix * cache_sum[..., None] + fresh_mix.reshape(slot_count, row_count, heads, HEAD)
    attended_here = (joined / total[..., None]).astype(jnp.bfloat16).reshape(slot_count, row_count, query_width)

    row_total = slot_count * row_count
    flat_rows = attended_here.reshape(row_total, query_width)
    model_width = out_weight.shape[1]
    every_rows = gather_rows(flat_rows, "tensor", manual)
    peers = every_rows.shape[0]
    own_part = jnp.dot(flat_rows, peer_weights[0], preferred_element_type=jnp.float32)
    rest_rows = jnp.concatenate([every_rows[i] for i in range(1, peers)], axis=1)
    rest_weights = jnp.concatenate([peer_weights[i] for i in range(1, peers)], axis=0)
    own_part = own_part + jnp.dot(rest_rows, rest_weights, preferred_element_type=jnp.float32)
    square_sum = jnp.sum(own_part * own_part, axis=-1)
    square_sum = butterfly_sum(square_sum, "tensor").reshape(row_total, 1)
    mean_square = square_sum / model_width
    normed = own_part * lax.rsqrt(mean_square + norm_eps) * norm_gain
    return normed.astype(jnp.bfloat16).reshape(slot_count, row_count, own_part.shape[1])


def solution(mesh):
    placed = (
        P(("groups", "dp"), None, "tensor"),
        P(("groups", "dp")),
        P(("groups", "dp")),
        P(("groups", "dp"), None, "tensor"),
        P(("groups", "dp"), None, "tensor"),
        P("tensor", None),
        P("tensor"),
    )
    return jax.shard_map(
        shards,
        mesh=mesh,
        in_specs=placed,
        out_specs=P(("groups", "dp"), None, "tensor"),
        check_vma=False,
    )
```

```python
import functools

import jax
import jax.numpy as jnp
from jax import lax
from jax.experimental import pallas as pl
from jax.experimental.pallas import tpu as pltpu
from jax.sharding import PartitionSpec as P

HEAD = 128
QHEADS = 16
KVHEADS = 8
TAG_WIDTH = 128


score_scale = 144.0 ** (-0.5)
soft_cap = 50.0
norm_eps = 1e-06


def attention_kernel(lane_ref, length_ref, pay_ref, cache_ref, out_ref, *, q_width):
    step = pl.program_id(0)
    sessions, cache_length, _ = cache_ref.shape
    row_count = pay_ref.shape[1]
    kv_heads = cache_ref.shape[2] // (2 * HEAD)
    group_size = QHEADS // KVHEADS
    lanes = [lane_ref[step * sessions + i] for i in range(sessions)]
    queries = jnp.stack([pay_ref[lane] for lane in lanes])
    lengths = length_ref[...]
    cache_pos = lax.broadcasted_iota(jnp.int32, (sessions, group_size * row_count, cache_length), 2)
    cache_seen = cache_pos < lengths
    lane_ids = lax.broadcasted_iota(jnp.int32, (sessions, row_count, TAG_WIDTH), 2)
    sums = jnp.zeros((sessions, row_count, TAG_WIDTH), jnp.float32)
    mixes = []
    for k in range(kv_heads):
        key_col = 2 * HEAD * k
        grouped = jnp.concatenate(
            [queries[:, :, (group_size * k + g) * HEAD:(group_size * k + g + 1) * HEAD] for g in range(group_size)],
            axis=1,
        )
        cache_keys = cache_ref[:, :, key_col:key_col + HEAD]
        cache_values = cache_ref[:, :, key_col + HEAD:key_col + 2 * HEAD]
        cache_scores = jnp.einsum("bqd,bkd->bqk", grouped, cache_keys, preferred_element_type=jnp.float32) * score_scale
        cache_w = jnp.where(cache_seen, jnp.exp(soft_cap * jnp.tanh(cache_scores / soft_cap)), 0.0)
        total = jnp.sum(cache_w, axis=-1, keepdims=True)
        mixed = jnp.einsum("bqk,bkd->bqd", cache_w.astype(jnp.bfloat16), cache_values, preferred_element_type=jnp.float32)
        mixed = (mixed / total).astype(out_ref.dtype)
        high = total.astype(jnp.bfloat16).astype(jnp.float32)
        low = total - high
        for g in range(group_size):
            head = group_size * k + g
            mixes.append(mixed[:, g * row_count:(g + 1) * row_count])
            sums = jnp.where(lane_ids == head, high[:, g * row_count:(g + 1) * row_count], sums)
            sums = jnp.where(lane_ids == TAG_WIDTH // 2 + head, low[:, g * row_count:(g + 1) * row_count], sums)
    result = jnp.concatenate(mixes + [sums.astype(out_ref.dtype)], axis=2)
    for i, lane in enumerate(lanes):
        out_ref[lane] = result[i]


def attend_cache(arrived, cached, lengths, slot_lane, q_width, block=8):
    lane_count, row_count, pay_width = arrived.shape
    slot_count, cache_length, kv_width = cached.shape
    block = min(block, slot_count)
    length_col = lengths.reshape(slot_count, 1, 1)
    return pl.pallas_call(
        functools.partial(attention_kernel, q_width=q_width),
        out_shape=jax.ShapeDtypeStruct((lane_count, row_count, q_width + TAG_WIDTH), jnp.bfloat16),
        grid_spec=pltpu.PrefetchScalarGridSpec(
            num_scalar_prefetch=1,
            grid=(slot_count // block,),
            in_specs=[
                pl.BlockSpec((block, 1, 1), lambda b, lanes: (b, 0, 0)),
                pl.BlockSpec((lane_count, row_count, pay_width), lambda b, lanes: (0, 0, 0)),
                pl.BlockSpec((block, cache_length, kv_width), lambda b, lanes: (b, 0, 0)),
            ],
            out_specs=pl.BlockSpec((lane_count, row_count, q_width + TAG_WIDTH), lambda b, lanes: (0, 0, 0)),
        ),
        cost_estimate=pl.CostEstimate(
            flops=4 * slot_count * (q_width // HEAD) * row_count * cache_length * HEAD,
            transcendentals=2 * slot_count * (q_width // HEAD) * row_count * cache_length,
            bytes_accessed=int(cached.size * 2 + arrived.size * 2 + lane_count * row_count * (q_width + TAG_WIDTH) * 2),
        ),
    )(slot_lane, length_col, arrived, cached)


def fresh_kernel(q_ref, fresh_ref, mix_ref, sum_ref):
    sessions, row_count, _ = q_ref.shape
    kv_heads = fresh_ref.shape[2] // (2 * HEAD)
    group_size = QHEADS // KVHEADS
    fresh_pos = lax.broadcasted_iota(jnp.int32, (sessions, group_size * row_count, row_count), 2)
    query_row = lax.broadcasted_iota(jnp.int32, (sessions, group_size * row_count, row_count), 1) % row_count
    fresh_seen = fresh_pos <= query_row
    lane = lax.broadcasted_iota(jnp.int32, (sessions, row_count, TAG_WIDTH), 2)
    sums = jnp.zeros((sessions, row_count, TAG_WIDTH), jnp.float32)
    for k in range(kv_heads):
        key_col = 2 * HEAD * k
        grouped = jnp.concatenate(
            [q_ref[:, :, (group_size * k + g) * HEAD:(group_size * k + g + 1) * HEAD] for g in range(group_size)],
            axis=1,
        )
        fresh_keys = fresh_ref[:, :, key_col:key_col + HEAD]
        fresh_values = fresh_ref[:, :, key_col + HEAD:key_col + 2 * HEAD]
        fresh_scores = jnp.einsum("bqd,bkd->bqk", grouped, fresh_keys, preferred_element_type=jnp.float32) * score_scale
        fresh_w = jnp.where(fresh_seen, jnp.exp(soft_cap * jnp.tanh(fresh_scores / soft_cap)), 0.0)
        total = jnp.sum(fresh_w, axis=-1, keepdims=True)
        mixed = jnp.einsum("bqk,bkd->bqd", fresh_w.astype(jnp.bfloat16), fresh_values, preferred_element_type=jnp.float32)
        for g in range(group_size):
            head = group_size * k + g
            col = head * HEAD
            mix_ref[:, :, col:col + HEAD] = mixed[:, g * row_count:(g + 1) * row_count]
            sums = jnp.where(lane == head, total[:, g * row_count:(g + 1) * row_count], sums)
    sum_ref[...] = sums


def attend_fresh(queries, fresh_kv, block=8):
    slot_count, row_count, q_width = queries.shape
    kv_width = fresh_kv.shape[2]
    block = min(block, slot_count)
    return pl.pallas_call(
        fresh_kernel,
        out_shape=(
            jax.ShapeDtypeStruct((slot_count, row_count, q_width), jnp.float32),
            jax.ShapeDtypeStruct((slot_count, row_count, TAG_WIDTH), jnp.float32),
        ),
        grid=(slot_count // block,),
        in_specs=[
            pl.BlockSpec((block, row_count, q_width), lambda b: (b, 0, 0)),
            pl.BlockSpec((block, row_count, kv_width), lambda b: (b, 0, 0)),
        ],
        out_specs=(
            pl.BlockSpec((block, row_count, q_width), lambda b: (b, 0, 0)),
            pl.BlockSpec((block, row_count, TAG_WIDTH), lambda b: (b, 0, 0)),
        ),
        cost_estimate=pl.CostEstimate(
            flops=4 * slot_count * (q_width // HEAD) * row_count * row_count * HEAD,
            transcendentals=2 * slot_count * (q_width // HEAD) * row_count * row_count,
            bytes_accessed=int((queries.size + fresh_kv.size) * 2 + slot_count * row_count * (q_width + TAG_WIDTH) * 4),
        ),
    )(queries, fresh_kv)


def halving_stages(axis):
    count = lax.axis_size(axis)
    stages = count.bit_length() - 1
    return count, stages if (1 << stages) == count else None


def scatter_sum(partial, axis):
    count, stages = halving_stages(axis)
    rows, width = partial.shape
    if stages is None:
        return lax.psum_scatter(partial, axis, scatter_dimension=1, tiled=True).astype(jnp.float32)
    me = lax.axis_index(axis)
    held = partial.reshape((rows,) + (2,) * stages + (width // count,))
    for s in range(stages):
        bit = (me >> s) & 1
        dim = stages - s
        keep = lax.dynamic_index_in_dim(held, bit, axis=dim, keepdims=False)
        send = lax.dynamic_index_in_dim(held, 1 - bit, axis=dim, keepdims=False)
        got = lax.ppermute(
            send.astype(jnp.bfloat16), axis, perm=[(i, i ^ (1 << s)) for i in range(count)]
        )
        held = keep.astype(jnp.float32) + got.astype(jnp.float32)
    return held


def projection_kernel(block_ref, rows_ref, weight_ref, out_ref):
    out_ref[0] = jnp.dot(rows_ref[...], weight_ref[...], preferred_element_type=jnp.float32).astype(out_ref.dtype)


def project_blocks(rows, weight, blocks):
    row_total, inner = rows.shape
    width = weight.shape[1] // lax.axis_size("tensor")
    count = blocks.shape[0]
    return pl.pallas_call(
        projection_kernel,
        out_shape=jax.ShapeDtypeStruct((count, row_total, width), jnp.bfloat16),
        grid_spec=pltpu.PrefetchScalarGridSpec(
            num_scalar_prefetch=1,
            grid=(count,),
            in_specs=[
                pl.BlockSpec((row_total, inner), lambda j, blk: (0, 0)),
                pl.BlockSpec((inner, width), lambda j, blk: (0, blk[j])),
            ],
            out_specs=pl.BlockSpec((1, row_total, width), lambda j, blk: (j, 0, 0)),
        ),
        cost_estimate=pl.CostEstimate(
            flops=2 * count * row_total * inner * width,
            transcendentals=0,
            bytes_accessed=int(rows.size * 2 + count * (inner * width + row_total * width) * 2),
        ),
    )(blocks, rows, weight)


def bit_reversed(value, bits):
    out = 0
    for b in range(bits):
        out |= ((value >> b) & 1) << (bits - 1 - b)
    return out


def project_and_scatter(rows, weight, axis):
    count = lax.axis_size(axis)
    stages = count.bit_length() - 1
    if (1 << stages) != count or (weight.shape[1] // count) % 128:
        products = jnp.dot(rows, weight, preferred_element_type=jnp.float32).astype(jnp.bfloat16)
        return scatter_sum(products, axis)
    me = lax.axis_index(axis)
    order = jnp.array([bit_reversed(j, stages) for j in range(count)], jnp.int32)
    blocks = jnp.bitwise_xor(me, order)
    half = count // 2
    sent = project_blocks(rows, weight, blocks[half:])
    kept = project_blocks(rows, weight, blocks[:half])
    got = lax.ppermute(sent, axis, perm=[(i, i ^ 1) for i in range(count)])
    held = kept.astype(jnp.float32) + got.astype(jnp.float32)
    for s in range(1, stages):
        half = held.shape[0] // 2
        got = lax.ppermute(
            held[half:].astype(jnp.bfloat16), axis, perm=[(i, i ^ (1 << s)) for i in range(count)]
        )
        held = held[:half] + got.astype(jnp.float32)
    return held[0]


def butterfly_sum(values, axis):
    count, stages = halving_stages(axis)
    if stages is None:
        return lax.psum(values, axis)
    shape = values.shape
    lanes = 128 if values.size % 128 == 0 else values.size
    values = values.reshape(values.size // lanes, lanes)
    for s in range(stages):
        values = values + lax.ppermute(values, axis, perm=[(i, i ^ (1 << s)) for i in range(count)])
    return values.reshape(shape)


def exchange_by_shift(lanes, axis, cap, direction):
    count = lax.axis_size(axis)
    parts = [lanes[:cap]]
    for shift in range(1, count):
        parts.append(
            lax.ppermute(
                lanes[shift * cap:(shift + 1) * cap],
                axis,
                perm=[(i, (i + direction * shift) % count) for i in range(count)],
            )
        )
    return jnp.concatenate(parts, axis=0)


def shards(kv_cache, lengths, source, queries, fresh_kv, out_weight, norm_gain):
    dp_count = lax.axis_size("dp")
    me = lax.axis_index("dp")
    slot_count, row_count, query_width = queries.shape
    kv_width = fresh_kv.shape[2]
    pair_cap = max(1, slot_count // dp_count)
    lane_count = dp_count * pair_cap
    slot_ids = jnp.arange(slot_count, dtype=jnp.int32)
    lane_ids = jnp.arange(lane_count, dtype=jnp.int32)

    old_home = source // slot_count
    old_slot = source % slot_count
    earlier = slot_ids[None, :] < slot_ids[:, None]
    same_home = old_home[:, None] == old_home[None, :]
    rank = jnp.sum(same_home & earlier, axis=1)
    shift = (old_home - me) % dp_count
    out_lane = shift * pair_cap + rank
    tag = jnp.broadcast_to(
        (old_slot + 1).astype(jnp.bfloat16)[:, None, None], (slot_count, row_count, TAG_WIDTH)
    )
    lane_hits = out_lane[None, :] == lane_ids[:, None]
    chosen = jnp.sum(jnp.where(lane_hits, slot_ids[None, :], 0), axis=1)
    sending = jnp.concatenate([jnp.take(queries, chosen, axis=0), jnp.take(tag, chosen, axis=0)], axis=2)
    arrived = exchange_by_shift(sending, "dp", pair_cap, 1)
    fresh_mix, fresh_sum = attend_fresh(queries, fresh_kv)

    lane_slot = arrived[:, 0, query_width].astype(jnp.int32) - 1
    hits = lane_slot[None, :] == slot_ids[:, None]
    slot_lane = jnp.clip(jnp.sum(jnp.where(hits, lane_ids[None, :], 0), axis=1), 0, lane_count - 1)
    back = attend_cache(arrived, kv_cache, lengths, slot_lane, query_width)
    returned = exchange_by_shift(back, "dp", pair_cap, -1)
    cache_here = jnp.take(returned, out_lane, axis=0)

    heads = query_width // HEAD
    sums = cache_here[:, :, query_width:].astype(jnp.float32)
    cache_sum = sums[:, :, :heads] + sums[:, :, TAG_WIDTH // 2:TAG_WIDTH // 2 + heads]
    total = cache_sum + fresh_sum[:, :, :heads]
    cache_sum = jnp.repeat(cache_sum, HEAD, axis=2)
    total = jnp.repeat(total, HEAD, axis=2)
    joined = cache_here[:, :, :query_width].astype(jnp.float32) * cache_sum + fresh_mix
    attended_here = (joined / total).astype(jnp.bfloat16)

    row_total = slot_count * row_count
    flat_rows = attended_here.reshape(row_total, query_width)
    model_width = out_weight.shape[1]
    own_part = project_and_scatter(flat_rows, out_weight, "tensor")
    square_sum = jnp.sum(own_part * own_part, axis=-1)
    square_sum = butterfly_sum(square_sum, "tensor").reshape(row_total, 1)
    mean_square = square_sum / model_width
    normed = own_part * lax.rsqrt(mean_square + norm_eps) * norm_gain
    return normed.astype(jnp.bfloat16).reshape(slot_count, row_count, own_part.shape[1])


def solution(mesh):
    placed = (
        P(("groups", "dp"), None, "tensor"),
        P(("groups", "dp")),
        P(("groups", "dp")),
        P(("groups", "dp"), None, "tensor"),
        P(("groups", "dp"), None, "tensor"),
        P("tensor", None),
        P("tensor"),
    )
    return jax.shard_map(
        shards,
        mesh=mesh,
        in_specs=placed,
        out_specs=P(("groups", "dp"), None, "tensor"),
        check_vma=False,
    )
```

```python
import functools

import jax
import jax.numpy as jnp
from jax import lax
from jax.experimental import pallas as pl
from jax.experimental.pallas import tpu as pltpu
from jax.sharding import PartitionSpec as P

HEAD = 128
QHEADS = 16
KVHEADS = 8
TAG_WIDTH = 128


score_scale = 144.0 ** (-0.5)
soft_cap = 50.0
norm_eps = 1e-06


def attention_kernel(lane_ref, length_ref, pay_ref, cache_ref, out_ref, *, q_width):
    step = pl.program_id(0)
    sessions, cache_length, _ = cache_ref.shape
    row_count = pay_ref.shape[1]
    kv_heads = cache_ref.shape[2] // (2 * HEAD)
    group_size = QHEADS // KVHEADS
    lanes = [lane_ref[step * sessions + i] for i in range(sessions)]
    queries = jnp.stack([pay_ref[lane] for lane in lanes])
    lengths = length_ref[...]
    cache_pos = lax.broadcasted_iota(jnp.int32, (sessions, group_size * row_count, cache_length), 2)
    cache_seen = cache_pos < lengths
    lane_ids = lax.broadcasted_iota(jnp.int32, (sessions, row_count, TAG_WIDTH), 2)
    sums = jnp.zeros((sessions, row_count, TAG_WIDTH), jnp.float32)
    mixes = []
    for k in range(kv_heads):
        key_col = 2 * HEAD * k
        grouped = jnp.concatenate(
            [queries[:, :, (group_size * k + g) * HEAD:(group_size * k + g + 1) * HEAD] for g in range(group_size)],
            axis=1,
        )
        cache_keys = cache_ref[:, :, key_col:key_col + HEAD]
        cache_values = cache_ref[:, :, key_col + HEAD:key_col + 2 * HEAD]
        cache_scores = jnp.einsum("bqd,bkd->bqk", grouped, cache_keys, preferred_element_type=jnp.float32) * score_scale
        cache_w = jnp.where(cache_seen, jnp.exp(soft_cap * jnp.tanh(cache_scores / soft_cap)), 0.0)
        total = jnp.sum(cache_w, axis=-1, keepdims=True)
        mixed = jnp.einsum("bqk,bkd->bqd", cache_w.astype(jnp.bfloat16), cache_values, preferred_element_type=jnp.float32)
        mixed = (mixed / total).astype(out_ref.dtype)
        high = total.astype(jnp.bfloat16).astype(jnp.float32)
        low = total - high
        for g in range(group_size):
            head = group_size * k + g
            mixes.append(mixed[:, g * row_count:(g + 1) * row_count])
            sums = jnp.where(lane_ids == head, high[:, g * row_count:(g + 1) * row_count], sums)
            sums = jnp.where(lane_ids == TAG_WIDTH // 2 + head, low[:, g * row_count:(g + 1) * row_count], sums)
    result = jnp.concatenate(mixes + [sums.astype(out_ref.dtype)], axis=2)
    for i, lane in enumerate(lanes):
        out_ref[lane] = result[i]


def attend_cache(arrived, cached, lengths, slot_lane, q_width, block=8):
    lane_count, row_count, pay_width = arrived.shape
    slot_count, cache_length, kv_width = cached.shape
    block = min(block, slot_count)
    length_col = lengths.reshape(slot_count, 1, 1)
    return pl.pallas_call(
        functools.partial(attention_kernel, q_width=q_width),
        out_shape=jax.ShapeDtypeStruct((lane_count, row_count, q_width + TAG_WIDTH), jnp.bfloat16),
        grid_spec=pltpu.PrefetchScalarGridSpec(
            num_scalar_prefetch=1,
            grid=(slot_count // block,),
            in_specs=[
                pl.BlockSpec((block, 1, 1), lambda b, lanes: (b, 0, 0)),
                pl.BlockSpec((lane_count, row_count, pay_width), lambda b, lanes: (0, 0, 0)),
                pl.BlockSpec((block, cache_length, kv_width), lambda b, lanes: (b, 0, 0)),
            ],
            out_specs=pl.BlockSpec((lane_count, row_count, q_width + TAG_WIDTH), lambda b, lanes: (0, 0, 0)),
        ),
        cost_estimate=pl.CostEstimate(
            flops=4 * slot_count * (q_width // HEAD) * row_count * cache_length * HEAD,
            transcendentals=2 * slot_count * (q_width // HEAD) * row_count * cache_length,
            bytes_accessed=int(cached.size * 2 + arrived.size * 2 + lane_count * row_count * (q_width + TAG_WIDTH) * 2),
        ),
    )(slot_lane, length_col, arrived, cached)


def fresh_kernel(q_ref, fresh_ref, mix_ref, sum_ref):
    sessions, row_count, _ = q_ref.shape
    kv_heads = fresh_ref.shape[2] // (2 * HEAD)
    group_size = QHEADS // KVHEADS
    fresh_pos = lax.broadcasted_iota(jnp.int32, (sessions, group_size * row_count, row_count), 2)
    query_row = lax.broadcasted_iota(jnp.int32, (sessions, group_size * row_count, row_count), 1) % row_count
    fresh_seen = fresh_pos <= query_row
    lane = lax.broadcasted_iota(jnp.int32, (sessions, row_count, TAG_WIDTH), 2)
    sums = jnp.zeros((sessions, row_count, TAG_WIDTH), jnp.float32)
    for k in range(kv_heads):
        key_col = 2 * HEAD * k
        grouped = jnp.concatenate(
            [q_ref[:, :, (group_size * k + g) * HEAD:(group_size * k + g + 1) * HEAD] for g in range(group_size)],
            axis=1,
        )
        fresh_keys = fresh_ref[:, :, key_col:key_col + HEAD]
        fresh_values = fresh_ref[:, :, key_col + HEAD:key_col + 2 * HEAD]
        fresh_scores = jnp.einsum("bqd,bkd->bqk", grouped, fresh_keys, preferred_element_type=jnp.float32) * score_scale
        fresh_w = jnp.where(fresh_seen, jnp.exp(soft_cap * jnp.tanh(fresh_scores / soft_cap)), 0.0)
        total = jnp.sum(fresh_w, axis=-1, keepdims=True)
        mixed = jnp.einsum("bqk,bkd->bqd", fresh_w.astype(jnp.bfloat16), fresh_values, preferred_element_type=jnp.float32)
        for g in range(group_size):
            head = group_size * k + g
            col = head * HEAD
            mix_ref[:, :, col:col + HEAD] = mixed[:, g * row_count:(g + 1) * row_count]
            sums = jnp.where(lane == head, total[:, g * row_count:(g + 1) * row_count], sums)
    sum_ref[...] = sums


def attend_fresh(queries, fresh_kv, block=8):
    slot_count, row_count, q_width = queries.shape
    kv_width = fresh_kv.shape[2]
    block = min(block, slot_count)
    return pl.pallas_call(
        fresh_kernel,
        out_shape=(
            jax.ShapeDtypeStruct((slot_count, row_count, q_width), jnp.float32),
            jax.ShapeDtypeStruct((slot_count, row_count, TAG_WIDTH), jnp.float32),
        ),
        grid=(slot_count // block,),
        in_specs=[
            pl.BlockSpec((block, row_count, q_width), lambda b: (b, 0, 0)),
            pl.BlockSpec((block, row_count, kv_width), lambda b: (b, 0, 0)),
        ],
        out_specs=(
            pl.BlockSpec((block, row_count, q_width), lambda b: (b, 0, 0)),
            pl.BlockSpec((block, row_count, TAG_WIDTH), lambda b: (b, 0, 0)),
        ),
        cost_estimate=pl.CostEstimate(
            flops=4 * slot_count * (q_width // HEAD) * row_count * row_count * HEAD,
            transcendentals=2 * slot_count * (q_width // HEAD) * row_count * row_count,
            bytes_accessed=int((queries.size + fresh_kv.size) * 2 + slot_count * row_count * (q_width + TAG_WIDTH) * 4),
        ),
    )(queries, fresh_kv)


def pack_lanes(payload, slot_lanes, lane_count):
    lane_ids = jnp.arange(lane_count, dtype=jnp.int32)
    slot_ids = jnp.arange(payload.shape[0], dtype=jnp.int32)
    lane_hits = slot_lanes[None, :] == lane_ids[:, None]
    filled = jnp.any(lane_hits, axis=1)
    chosen = jnp.sum(jnp.where(lane_hits, slot_ids[None, :], 0), axis=1)
    picked = jnp.take(payload, chosen, axis=0)
    return jnp.where(filled[:, None, None], picked, jnp.zeros((), payload.dtype))


def halving_stages(axis):
    count = lax.axis_size(axis)
    stages = count.bit_length() - 1
    return count, stages if (1 << stages) == count else None


def scatter_sum(partial, axis):
    count, stages = halving_stages(axis)
    rows, width = partial.shape
    if stages is None:
        return lax.psum_scatter(partial, axis, scatter_dimension=1, tiled=True).astype(jnp.float32)
    me = lax.axis_index(axis)
    held = partial.reshape((rows,) + (2,) * stages + (width // count,))
    for s in range(stages):
        bit = (me >> s) & 1
        dim = stages - s
        keep = lax.dynamic_index_in_dim(held, bit, axis=dim, keepdims=False)
        send = lax.dynamic_index_in_dim(held, 1 - bit, axis=dim, keepdims=False)
        got = lax.ppermute(
            send.astype(jnp.bfloat16), axis, perm=[(i, i ^ (1 << s)) for i in range(count)]
        )
        held = keep.astype(jnp.float32) + got.astype(jnp.float32)
    return held


def projection_kernel(block_ref, rows_ref, weight_ref, out_ref):
    out_ref[0] = jnp.dot(rows_ref[...], weight_ref[...], preferred_element_type=jnp.float32).astype(out_ref.dtype)


def project_blocks(rows, weight, blocks):
    row_total, inner = rows.shape
    width = weight.shape[1] // lax.axis_size("tensor")
    count = blocks.shape[0]
    return pl.pallas_call(
        projection_kernel,
        out_shape=jax.ShapeDtypeStruct((count, row_total, width), jnp.bfloat16),
        grid_spec=pltpu.PrefetchScalarGridSpec(
            num_scalar_prefetch=1,
            grid=(count,),
            in_specs=[
                pl.BlockSpec((row_total, inner), lambda j, blk: (0, 0)),
                pl.BlockSpec((inner, width), lambda j, blk: (0, blk[j])),
            ],
            out_specs=pl.BlockSpec((1, row_total, width), lambda j, blk: (j, 0, 0)),
        ),
        cost_estimate=pl.CostEstimate(
            flops=2 * count * row_total * inner * width,
            transcendentals=0,
            bytes_accessed=int(rows.size * 2 + count * (inner * width + row_total * width) * 2),
        ),
    )(blocks, rows, weight)


def bit_reversed(value, bits):
    out = 0
    for b in range(bits):
        out |= ((value >> b) & 1) << (bits - 1 - b)
    return out


def project_and_scatter(rows, weight, axis):
    count = lax.axis_size(axis)
    stages = count.bit_length() - 1
    if (1 << stages) != count or (weight.shape[1] // count) % 128:
        products = jnp.dot(rows, weight, preferred_element_type=jnp.float32).astype(jnp.bfloat16)
        return scatter_sum(products, axis)
    me = lax.axis_index(axis)
    order = jnp.array([bit_reversed(j, stages) for j in range(count)], jnp.int32)
    blocks = jnp.bitwise_xor(me, order)
    half = count // 2
    sent = project_blocks(rows, weight, blocks[half:])
    kept = project_blocks(rows, weight, blocks[:half])
    got = lax.ppermute(sent, axis, perm=[(i, i ^ 1) for i in range(count)])
    for s in range(1, stages):
        half = kept.shape[0] // 2
        sent = (kept[half:].astype(jnp.float32) + got[half:].astype(jnp.float32)).astype(jnp.bfloat16)
        kept, got, sent = lax.optimization_barrier((kept, got, sent))
        held = kept[:half].astype(jnp.float32) + got[:half].astype(jnp.float32)
        arrived = lax.ppermute(sent, axis, perm=[(i, i ^ (1 << s)) for i in range(count)])
        kept, got = held, arrived
    return kept[0].astype(jnp.float32) + got[0].astype(jnp.float32)


def butterfly_sum(values, axis):
    count, stages = halving_stages(axis)
    if stages is None:
        return lax.psum(values, axis)
    shape = values.shape
    lanes = 128 if values.size % 128 == 0 else values.size
    values = values.reshape(values.size // lanes, lanes)
    for s in range(stages):
        values = values + lax.ppermute(values, axis, perm=[(i, i ^ (1 << s)) for i in range(count)])
    return values.reshape(shape)


def exchange_by_shift(lanes, axis, cap, direction):
    count = lax.axis_size(axis)
    parts = [lanes[:cap]]
    for shift in range(1, count):
        parts.append(
            lax.ppermute(
                lanes[shift * cap:(shift + 1) * cap],
                axis,
                perm=[(i, (i + direction * shift) % count) for i in range(count)],
            )
        )
    return jnp.concatenate(parts, axis=0)


def shards(kv_cache, lengths, source, queries, fresh_kv, out_weight, norm_gain):
    dp_count = lax.axis_size("dp")
    me = lax.axis_index("dp")
    slot_count, row_count, query_width = queries.shape
    kv_width = fresh_kv.shape[2]
    pair_cap = max(1, slot_count // dp_count)
    lane_count = dp_count * pair_cap
    slot_ids = jnp.arange(slot_count, dtype=jnp.int32)
    lane_ids = jnp.arange(lane_count, dtype=jnp.int32)

    old_home = source // slot_count
    old_slot = source % slot_count
    earlier = slot_ids[None, :] < slot_ids[:, None]
    same_home = old_home[:, None] == old_home[None, :]
    rank = jnp.sum(same_home & earlier, axis=1)
    shift = (old_home - me) % dp_count
    out_lane = shift * pair_cap + rank
    tag = jnp.broadcast_to(
        (old_slot + 1).astype(jnp.bfloat16)[:, None, None], (slot_count, row_count, TAG_WIDTH)
    )
    payload = jnp.concatenate([queries, tag], axis=2)
    sending = pack_lanes(payload, out_lane, lane_count)
    arrived = exchange_by_shift(sending, "dp", pair_cap, 1)
    fresh_mix, fresh_sum = attend_fresh(queries, fresh_kv)

    lane_slot = arrived[:, 0, query_width].astype(jnp.int32) - 1
    hits = lane_slot[None, :] == slot_ids[:, None]
    slot_lane = jnp.clip(jnp.sum(jnp.where(hits, lane_ids[None, :], 0), axis=1), 0, lane_count - 1)
    back = attend_cache(arrived, kv_cache, lengths, slot_lane, query_width)
    returned = exchange_by_shift(back, "dp", pair_cap, -1)
    cache_here = jnp.take(returned, out_lane, axis=0)

    heads = query_width // HEAD
    sums = cache_here[:, :, query_width:].astype(jnp.float32)
    cache_sum = sums[:, :, :heads] + sums[:, :, TAG_WIDTH // 2:TAG_WIDTH // 2 + heads]
    total = cache_sum + fresh_sum[:, :, :heads]
    cache_mix = cache_here[:, :, :query_width].astype(jnp.float32).reshape(slot_count, row_count, heads, HEAD)
    joined = cache_mix * cache_sum[..., None] + fresh_mix.reshape(slot_count, row_count, heads, HEAD)
    attended_here = (joined / total[..., None]).astype(jnp.bfloat16).reshape(slot_count, row_count, query_width)

    row_total = slot_count * row_count
    flat_rows = attended_here.reshape(row_total, query_width)
    model_width = out_weight.shape[1]
    own_part = project_and_scatter(flat_rows, out_weight, "tensor")
    square_sum = jnp.sum(own_part * own_part, axis=-1)
    square_sum = butterfly_sum(square_sum, "tensor").reshape(row_total, 1)
    mean_square = square_sum / model_width
    normed = own_part * lax.rsqrt(mean_square + norm_eps) * norm_gain
    return normed.astype(jnp.bfloat16).reshape(slot_count, row_count, own_part.shape[1])


def solution(mesh):
    placed = (
        P(("groups", "dp"), None, "tensor"),
        P(("groups", "dp")),
        P(("groups", "dp")),
        P(("groups", "dp"), None, "tensor"),
        P(("groups", "dp"), None, "tensor"),
        P("tensor", None),
        P("tensor"),
    )
    return jax.shard_map(
        shards,
        mesh=mesh,
        in_specs=placed,
        out_specs=P(("groups", "dp"), None, "tensor"),
        check_vma=False,
    )
```

```python
import functools

import jax
import jax.numpy as jnp
from jax import lax
from jax.experimental import pallas as pl
from jax.experimental.pallas import tpu as pltpu
from jax.sharding import PartitionSpec as P

HEAD = 128
QHEADS = 16
KVHEADS = 8
TAG_WIDTH = 128


score_scale = 144.0 ** (-0.5)
soft_cap = 50.0
norm_eps = 1e-06


def attention_kernel(lane_ref, length_ref, pay_ref, cache_ref, out_ref, *, q_width):
    step = pl.program_id(0)
    sessions, cache_length, _ = cache_ref.shape
    row_count = pay_ref.shape[1]
    kv_heads = cache_ref.shape[2] // (2 * HEAD)
    group_size = QHEADS // KVHEADS
    lanes = [lane_ref[step * sessions + i] for i in range(sessions)]
    queries = jnp.stack([pay_ref[lane] for lane in lanes])
    lengths = length_ref[...]
    cache_pos = lax.broadcasted_iota(jnp.int32, (sessions, group_size * row_count, cache_length), 2)
    cache_seen = cache_pos < lengths
    lane_ids = lax.broadcasted_iota(jnp.int32, (sessions, row_count, TAG_WIDTH), 2)
    sums = jnp.zeros((sessions, row_count, TAG_WIDTH), jnp.float32)
    mixes = []
    for k in range(kv_heads):
        key_col = 2 * HEAD * k
        grouped = jnp.concatenate(
            [queries[:, :, (group_size * k + g) * HEAD:(group_size * k + g + 1) * HEAD] for g in range(group_size)],
            axis=1,
        )
        cache_keys = cache_ref[:, :, key_col:key_col + HEAD]
        cache_values = cache_ref[:, :, key_col + HEAD:key_col + 2 * HEAD]
        cache_scores = jnp.einsum("bqd,bkd->bqk", grouped, cache_keys, preferred_element_type=jnp.float32) * score_scale
        cache_w = jnp.where(cache_seen, jnp.exp(soft_cap * jnp.tanh(cache_scores / soft_cap)), 0.0)
        total = jnp.sum(cache_w, axis=-1, keepdims=True)
        mixed = jnp.einsum("bqk,bkd->bqd", cache_w.astype(jnp.bfloat16), cache_values, preferred_element_type=jnp.float32)
        mixed = (mixed / total).astype(out_ref.dtype)
        high = total.astype(jnp.bfloat16).astype(jnp.float32)
        low = total - high
        for g in range(group_size):
            head = group_size * k + g
            mixes.append(mixed[:, g * row_count:(g + 1) * row_count])
            sums = jnp.where(lane_ids == head, high[:, g * row_count:(g + 1) * row_count], sums)
            sums = jnp.where(lane_ids == TAG_WIDTH // 2 + head, low[:, g * row_count:(g + 1) * row_count], sums)
    result = jnp.concatenate(mixes + [sums.astype(out_ref.dtype)], axis=2)
    for i, lane in enumerate(lanes):
        out_ref[lane] = result[i]


def attend_cache(arrived, cached, lengths, slot_lane, q_width, block=8):
    lane_count, row_count, pay_width = arrived.shape
    slot_count, cache_length, kv_width = cached.shape
    block = min(block, slot_count)
    length_col = lengths.reshape(slot_count, 1, 1)
    return pl.pallas_call(
        functools.partial(attention_kernel, q_width=q_width),
        out_shape=jax.ShapeDtypeStruct((lane_count, row_count, q_width + TAG_WIDTH), jnp.bfloat16),
        grid_spec=pltpu.PrefetchScalarGridSpec(
            num_scalar_prefetch=1,
            grid=(slot_count // block,),
            in_specs=[
                pl.BlockSpec((block, 1, 1), lambda b, lanes: (b, 0, 0)),
                pl.BlockSpec((lane_count, row_count, pay_width), lambda b, lanes: (0, 0, 0)),
                pl.BlockSpec((block, cache_length, kv_width), lambda b, lanes: (b, 0, 0)),
            ],
            out_specs=pl.BlockSpec((lane_count, row_count, q_width + TAG_WIDTH), lambda b, lanes: (0, 0, 0)),
        ),
        cost_estimate=pl.CostEstimate(
            flops=4 * slot_count * (q_width // HEAD) * row_count * cache_length * HEAD,
            transcendentals=2 * slot_count * (q_width // HEAD) * row_count * cache_length,
            bytes_accessed=int(cached.size * 2 + arrived.size * 2 + lane_count * row_count * (q_width + TAG_WIDTH) * 2),
        ),
    )(slot_lane, length_col, arrived, cached)


def fresh_kernel(q_ref, fresh_ref, mix_ref, sum_ref):
    sessions, row_count, _ = q_ref.shape
    kv_heads = fresh_ref.shape[2] // (2 * HEAD)
    group_size = QHEADS // KVHEADS
    fresh_pos = lax.broadcasted_iota(jnp.int32, (sessions, group_size * row_count, row_count), 2)
    query_row = lax.broadcasted_iota(jnp.int32, (sessions, group_size * row_count, row_count), 1) % row_count
    fresh_seen = fresh_pos <= query_row
    lane = lax.broadcasted_iota(jnp.int32, (sessions, row_count, TAG_WIDTH), 2)
    sums = jnp.zeros((sessions, row_count, TAG_WIDTH), jnp.float32)
    for k in range(kv_heads):
        key_col = 2 * HEAD * k
        grouped = jnp.concatenate(
            [q_ref[:, :, (group_size * k + g) * HEAD:(group_size * k + g + 1) * HEAD] for g in range(group_size)],
            axis=1,
        )
        fresh_keys = fresh_ref[:, :, key_col:key_col + HEAD]
        fresh_values = fresh_ref[:, :, key_col + HEAD:key_col + 2 * HEAD]
        fresh_scores = jnp.einsum("bqd,bkd->bqk", grouped, fresh_keys, preferred_element_type=jnp.float32) * score_scale
        fresh_w = jnp.where(fresh_seen, jnp.exp(soft_cap * jnp.tanh(fresh_scores / soft_cap)), 0.0)
        total = jnp.sum(fresh_w, axis=-1, keepdims=True)
        mixed = jnp.einsum("bqk,bkd->bqd", fresh_w.astype(jnp.bfloat16), fresh_values, preferred_element_type=jnp.float32)
        for g in range(group_size):
            head = group_size * k + g
            col = head * HEAD
            mix_ref[:, :, col:col + HEAD] = mixed[:, g * row_count:(g + 1) * row_count]
            sums = jnp.where(lane == head, total[:, g * row_count:(g + 1) * row_count], sums)
    sum_ref[...] = sums


def attend_fresh(queries, fresh_kv, block=8):
    slot_count, row_count, q_width = queries.shape
    kv_width = fresh_kv.shape[2]
    block = min(block, slot_count)
    return pl.pallas_call(
        fresh_kernel,
        out_shape=(
            jax.ShapeDtypeStruct((slot_count, row_count, q_width), jnp.float32),
            jax.ShapeDtypeStruct((slot_count, row_count, TAG_WIDTH), jnp.float32),
        ),
        grid=(slot_count // block,),
        in_specs=[
            pl.BlockSpec((block, row_count, q_width), lambda b: (b, 0, 0)),
            pl.BlockSpec((block, row_count, kv_width), lambda b: (b, 0, 0)),
        ],
        out_specs=(
            pl.BlockSpec((block, row_count, q_width), lambda b: (b, 0, 0)),
            pl.BlockSpec((block, row_count, TAG_WIDTH), lambda b: (b, 0, 0)),
        ),
        cost_estimate=pl.CostEstimate(
            flops=4 * slot_count * (q_width // HEAD) * row_count * row_count * HEAD,
            transcendentals=2 * slot_count * (q_width // HEAD) * row_count * row_count,
            bytes_accessed=int((queries.size + fresh_kv.size) * 2 + slot_count * row_count * (q_width + TAG_WIDTH) * 4),
        ),
    )(queries, fresh_kv)


def halving_stages(axis):
    count = lax.axis_size(axis)
    stages = count.bit_length() - 1
    return count, stages if (1 << stages) == count else None


def scatter_sum(partial, axis):
    count, stages = halving_stages(axis)
    rows, width = partial.shape
    if stages is None:
        return lax.psum_scatter(partial, axis, scatter_dimension=1, tiled=True).astype(jnp.float32)
    me = lax.axis_index(axis)
    held = partial.reshape((rows,) + (2,) * stages + (width // count,))
    for s in range(stages):
        bit = (me >> s) & 1
        dim = stages - s
        keep = lax.dynamic_index_in_dim(held, bit, axis=dim, keepdims=False)
        send = lax.dynamic_index_in_dim(held, 1 - bit, axis=dim, keepdims=False)
        got = lax.ppermute(
            send.astype(jnp.bfloat16), axis, perm=[(i, i ^ (1 << s)) for i in range(count)]
        )
        held = keep.astype(jnp.float32) + got.astype(jnp.float32)
    return held


def projection_kernel(block_ref, rows_ref, weight_ref, out_ref):
    out_ref[0] = jnp.dot(rows_ref[...], weight_ref[...], preferred_element_type=jnp.float32).astype(out_ref.dtype)


def project_blocks(rows, weight, blocks):
    row_total, inner = rows.shape
    width = weight.shape[1] // lax.axis_size("tensor")
    count = blocks.shape[0]
    return pl.pallas_call(
        projection_kernel,
        out_shape=jax.ShapeDtypeStruct((count, row_total, width), jnp.bfloat16),
        grid_spec=pltpu.PrefetchScalarGridSpec(
            num_scalar_prefetch=1,
            grid=(count,),
            in_specs=[
                pl.BlockSpec((row_total, inner), lambda j, blk: (0, 0)),
                pl.BlockSpec((inner, width), lambda j, blk: (0, blk[j])),
            ],
            out_specs=pl.BlockSpec((1, row_total, width), lambda j, blk: (j, 0, 0)),
        ),
        cost_estimate=pl.CostEstimate(
            flops=2 * count * row_total * inner * width,
            transcendentals=0,
            bytes_accessed=int(rows.size * 2 + count * (inner * width + row_total * width) * 2),
        ),
    )(blocks, rows, weight)


def bit_reversed(value, bits):
    out = 0
    for b in range(bits):
        out |= ((value >> b) & 1) << (bits - 1 - b)
    return out


def project_and_scatter(rows, weight, axis):
    count = lax.axis_size(axis)
    stages = count.bit_length() - 1
    if (1 << stages) != count or (weight.shape[1] // count) % 128:
        products = jnp.dot(rows, weight, preferred_element_type=jnp.float32).astype(jnp.bfloat16)
        return scatter_sum(products, axis)
    me = lax.axis_index(axis)
    order = jnp.array([bit_reversed(j, stages) for j in range(count)], jnp.int32)
    blocks = jnp.bitwise_xor(me, order)
    half = count // 2
    sent = project_blocks(rows, weight, blocks[half:])
    kept = project_blocks(rows, weight, blocks[:half])
    got = lax.ppermute(sent, axis, perm=[(i, i ^ 1) for i in range(count)])
    held = kept.astype(jnp.float32) + got.astype(jnp.float32)
    for s in range(1, stages):
        half = held.shape[0] // 2
        got = lax.ppermute(
            held[half:].astype(jnp.bfloat16), axis, perm=[(i, i ^ (1 << s)) for i in range(count)]
        )
        held = held[:half] + got.astype(jnp.float32)
    return held[0]


def butterfly_sum(values, axis):
    count, stages = halving_stages(axis)
    if stages is None:
        return lax.psum(values, axis)
    shape = values.shape
    lanes = 128 if values.size % 128 == 0 else values.size
    values = values.reshape(values.size // lanes, lanes)
    for s in range(stages):
        values = values + lax.ppermute(values, axis, perm=[(i, i ^ (1 << s)) for i in range(count)])
    return values.reshape(shape)


def exchange_by_shift(lanes, axis, cap, direction):
    count = lax.axis_size(axis)
    parts = [lanes[:cap]]
    for shift in range(1, count):
        parts.append(
            lax.ppermute(
                lanes[shift * cap:(shift + 1) * cap],
                axis,
                perm=[(i, (i + direction * shift) % count) for i in range(count)],
            )
        )
    return jnp.concatenate(parts, axis=0)


def shards(kv_cache, lengths, source, queries, fresh_kv, out_weight, norm_gain):
    dp_count = lax.axis_size("dp")
    me = lax.axis_index("dp")
    slot_count, row_count, query_width = queries.shape
    kv_width = fresh_kv.shape[2]
    pair_cap = max(1, slot_count // dp_count)
    lane_count = dp_count * pair_cap
    slot_ids = jnp.arange(slot_count, dtype=jnp.int32)
    lane_ids = jnp.arange(lane_count, dtype=jnp.int32)

    old_home = source // slot_count
    old_slot = source % slot_count
    earlier = slot_ids[None, :] < slot_ids[:, None]
    same_home = old_home[:, None] == old_home[None, :]
    rank = jnp.sum(same_home & earlier, axis=1)
    shift = (old_home - me) % dp_count
    out_lane = shift * pair_cap + rank
    lane_hits = out_lane[None, :] == lane_ids[:, None]
    chosen = jnp.sum(jnp.where(lane_hits, slot_ids[None, :], 0), axis=1)
    arrived = exchange_by_shift(jnp.take(queries, chosen, axis=0), "dp", pair_cap, 1)
    arrived_tag = exchange_by_shift(old_slot[chosen] + 1, "dp", pair_cap, 1)
    fresh_mix, fresh_sum = attend_fresh(queries, fresh_kv)

    lane_slot = arrived_tag - 1
    hits = lane_slot[None, :] == slot_ids[:, None]
    slot_lane = jnp.clip(jnp.sum(jnp.where(hits, lane_ids[None, :], 0), axis=1), 0, lane_count - 1)
    back = attend_cache(arrived, kv_cache, lengths, slot_lane, query_width)
    returned = exchange_by_shift(back, "dp", pair_cap, -1)
    cache_here = jnp.take(returned, out_lane, axis=0)

    heads = query_width // HEAD
    sums = cache_here[:, :, query_width:].astype(jnp.float32)
    cache_sum = sums[:, :, :heads] + sums[:, :, TAG_WIDTH // 2:TAG_WIDTH // 2 + heads]
    total = cache_sum + fresh_sum[:, :, :heads]
    cache_mix = cache_here[:, :, :query_width].astype(jnp.float32).reshape(slot_count, row_count, heads, HEAD)
    joined = cache_mix * cache_sum[..., None] + fresh_mix.reshape(slot_count, row_count, heads, HEAD)
    attended_here = (joined / total[..., None]).astype(jnp.bfloat16).reshape(slot_count, row_count, query_width)

    row_total = slot_count * row_count
    flat_rows = attended_here.reshape(row_total, query_width)
    model_width = out_weight.shape[1]
    own_part = project_and_scatter(flat_rows, out_weight, "tensor")
    square_sum = jnp.sum(own_part * own_part, axis=-1)
    square_sum = butterfly_sum(square_sum, "tensor").reshape(row_total, 1)
    mean_square = square_sum / model_width
    normed = own_part * lax.rsqrt(mean_square + norm_eps) * norm_gain
    return normed.astype(jnp.bfloat16).reshape(slot_count, row_count, own_part.shape[1])


def solution(mesh):
    placed = (
        P(("groups", "dp"), None, "tensor"),
        P(("groups", "dp")),
        P(("groups", "dp")),
        P(("groups", "dp"), None, "tensor"),
        P(("groups", "dp"), None, "tensor"),
        P("tensor", None),
        P("tensor"),
    )
    return jax.shard_map(
        shards,
        mesh=mesh,
        in_specs=placed,
        out_specs=P(("groups", "dp"), None, "tensor"),
        check_vma=False,
    )
```

```python
import functools

import jax
import jax.numpy as jnp
from jax import lax
from jax.experimental import pallas as pl
from jax.experimental.pallas import tpu as pltpu
from jax.sharding import PartitionSpec as P

HEAD = 128
QHEADS = 16
KVHEADS = 8
TAG_WIDTH = 128


score_scale = 144.0 ** (-0.5)
soft_cap = 50.0
norm_eps = 1e-06


def attention_kernel(lane_ref, length_ref, pay_ref, cache_ref, out_ref, *, q_width):
    step = pl.program_id(0)
    sessions, cache_length, _ = cache_ref.shape
    row_count = pay_ref.shape[1]
    kv_heads = cache_ref.shape[2] // (2 * HEAD)
    group_size = QHEADS // KVHEADS
    lanes = [lane_ref[step * sessions + i] for i in range(sessions)]
    queries = jnp.stack([pay_ref[lane] for lane in lanes])
    lengths = length_ref[...]
    cache_pos = lax.broadcasted_iota(jnp.int32, (sessions, group_size * row_count, cache_length), 2)
    cache_seen = cache_pos < lengths
    lane_ids = lax.broadcasted_iota(jnp.int32, (sessions, row_count, TAG_WIDTH), 2)
    sums = jnp.zeros((sessions, row_count, TAG_WIDTH), jnp.float32)
    mixes = []
    for k in range(kv_heads):
        key_col = 2 * HEAD * k
        grouped = jnp.concatenate(
            [queries[:, :, (group_size * k + g) * HEAD:(group_size * k + g + 1) * HEAD] for g in range(group_size)],
            axis=1,
        )
        cache_keys = cache_ref[:, :, key_col:key_col + HEAD]
        cache_values = cache_ref[:, :, key_col + HEAD:key_col + 2 * HEAD]
        cache_scores = jnp.einsum("bqd,bkd->bqk", grouped, cache_keys, preferred_element_type=jnp.float32) * score_scale
        cache_w = jnp.where(cache_seen, jnp.exp(soft_cap * jnp.tanh(cache_scores / soft_cap)), 0.0)
        total = jnp.sum(cache_w, axis=-1, keepdims=True)
        mixed = jnp.einsum("bqk,bkd->bqd", cache_w.astype(jnp.bfloat16), cache_values, preferred_element_type=jnp.float32)
        mixed = (mixed / total).astype(out_ref.dtype)
        high = total.astype(jnp.bfloat16).astype(jnp.float32)
        low = total - high
        for g in range(group_size):
            head = group_size * k + g
            mixes.append(mixed[:, g * row_count:(g + 1) * row_count])
            sums = jnp.where(lane_ids == head, high[:, g * row_count:(g + 1) * row_count], sums)
            sums = jnp.where(lane_ids == TAG_WIDTH // 2 + head, low[:, g * row_count:(g + 1) * row_count], sums)
    result = jnp.concatenate(mixes + [sums.astype(out_ref.dtype)], axis=2)
    for i, lane in enumerate(lanes):
        out_ref[lane] = result[i]


def attend_cache(arrived, cached, lengths, slot_lane, q_width, block=8):
    lane_count, row_count, pay_width = arrived.shape
    slot_count, cache_length, kv_width = cached.shape
    block = min(block, slot_count)
    length_col = lengths.reshape(slot_count, 1, 1)
    return pl.pallas_call(
        functools.partial(attention_kernel, q_width=q_width),
        out_shape=jax.ShapeDtypeStruct((lane_count, row_count, q_width + TAG_WIDTH), jnp.bfloat16),
        grid_spec=pltpu.PrefetchScalarGridSpec(
            num_scalar_prefetch=1,
            grid=(slot_count // block,),
            in_specs=[
                pl.BlockSpec((block, 1, 1), lambda b, lanes: (b, 0, 0)),
                pl.BlockSpec((lane_count, row_count, pay_width), lambda b, lanes: (0, 0, 0)),
                pl.BlockSpec((block, cache_length, kv_width), lambda b, lanes: (b, 0, 0)),
            ],
            out_specs=pl.BlockSpec((lane_count, row_count, q_width + TAG_WIDTH), lambda b, lanes: (0, 0, 0)),
        ),
        cost_estimate=pl.CostEstimate(
            flops=4 * slot_count * (q_width // HEAD) * row_count * cache_length * HEAD,
            transcendentals=2 * slot_count * (q_width // HEAD) * row_count * cache_length,
            bytes_accessed=int(cached.size * 2 + arrived.size * 2 + lane_count * row_count * (q_width + TAG_WIDTH) * 2),
        ),
    )(slot_lane, length_col, arrived, cached)


def fresh_kernel(q_ref, fresh_ref, mix_ref, sum_ref):
    sessions, row_count, _ = q_ref.shape
    kv_heads = fresh_ref.shape[2] // (2 * HEAD)
    group_size = QHEADS // KVHEADS
    fresh_pos = lax.broadcasted_iota(jnp.int32, (sessions, group_size * row_count, row_count), 2)
    query_row = lax.broadcasted_iota(jnp.int32, (sessions, group_size * row_count, row_count), 1) % row_count
    fresh_seen = fresh_pos <= query_row
    lane = lax.broadcasted_iota(jnp.int32, (sessions, row_count, TAG_WIDTH), 2)
    sums = jnp.zeros((sessions, row_count, TAG_WIDTH), jnp.float32)
    for k in range(kv_heads):
        key_col = 2 * HEAD * k
        grouped = jnp.concatenate(
            [q_ref[:, :, (group_size * k + g) * HEAD:(group_size * k + g + 1) * HEAD] for g in range(group_size)],
            axis=1,
        )
        fresh_keys = fresh_ref[:, :, key_col:key_col + HEAD]
        fresh_values = fresh_ref[:, :, key_col + HEAD:key_col + 2 * HEAD]
        fresh_scores = jnp.einsum("bqd,bkd->bqk", grouped, fresh_keys, preferred_element_type=jnp.float32) * score_scale
        fresh_w = jnp.where(fresh_seen, jnp.exp(soft_cap * jnp.tanh(fresh_scores / soft_cap)), 0.0)
        total = jnp.sum(fresh_w, axis=-1, keepdims=True)
        mixed = jnp.einsum("bqk,bkd->bqd", fresh_w.astype(jnp.bfloat16), fresh_values, preferred_element_type=jnp.float32)
        for g in range(group_size):
            head = group_size * k + g
            col = head * HEAD
            mix_ref[:, :, col:col + HEAD] = mixed[:, g * row_count:(g + 1) * row_count]
            sums = jnp.where(lane == head, total[:, g * row_count:(g + 1) * row_count], sums)
    sum_ref[...] = sums


def attend_fresh(queries, fresh_kv, block=8):
    slot_count, row_count, q_width = queries.shape
    kv_width = fresh_kv.shape[2]
    block = min(block, slot_count)
    return pl.pallas_call(
        fresh_kernel,
        out_shape=(
            jax.ShapeDtypeStruct((slot_count, row_count, q_width), jnp.float32),
            jax.ShapeDtypeStruct((slot_count, row_count, TAG_WIDTH), jnp.float32),
        ),
        grid=(slot_count // block,),
        in_specs=[
            pl.BlockSpec((block, row_count, q_width), lambda b: (b, 0, 0)),
            pl.BlockSpec((block, row_count, kv_width), lambda b: (b, 0, 0)),
        ],
        out_specs=(
            pl.BlockSpec((block, row_count, q_width), lambda b: (b, 0, 0)),
            pl.BlockSpec((block, row_count, TAG_WIDTH), lambda b: (b, 0, 0)),
        ),
        cost_estimate=pl.CostEstimate(
            flops=4 * slot_count * (q_width // HEAD) * row_count * row_count * HEAD,
            transcendentals=2 * slot_count * (q_width // HEAD) * row_count * row_count,
            bytes_accessed=int((queries.size + fresh_kv.size) * 2 + slot_count * row_count * (q_width + TAG_WIDTH) * 4),
        ),
    )(queries, fresh_kv)


def pack_lanes(payload, slot_lanes, lane_count):
    lane_ids = jnp.arange(lane_count, dtype=jnp.int32)
    slot_ids = jnp.arange(payload.shape[0], dtype=jnp.int32)
    lane_hits = slot_lanes[None, :] == lane_ids[:, None]
    filled = jnp.any(lane_hits, axis=1)
    chosen = jnp.sum(jnp.where(lane_hits, slot_ids[None, :], 0), axis=1)
    picked = jnp.take(payload, chosen, axis=0)
    return jnp.where(filled[:, None, None], picked, jnp.zeros((), payload.dtype))


def halving_stages(axis):
    count = lax.axis_size(axis)
    stages = count.bit_length() - 1
    return count, stages if (1 << stages) == count else None


def scatter_sum(partial, axis):
    count, stages = halving_stages(axis)
    rows, width = partial.shape
    if stages is None:
        return lax.psum_scatter(partial, axis, scatter_dimension=1, tiled=True).astype(jnp.float32)
    me = lax.axis_index(axis)
    held = partial.reshape((rows,) + (2,) * stages + (width // count,))
    for s in range(stages):
        bit = (me >> s) & 1
        dim = stages - s
        keep = lax.dynamic_index_in_dim(held, bit, axis=dim, keepdims=False)
        send = lax.dynamic_index_in_dim(held, 1 - bit, axis=dim, keepdims=False)
        got = lax.ppermute(
            send.astype(jnp.bfloat16), axis, perm=[(i, i ^ (1 << s)) for i in range(count)]
        )
        held = keep.astype(jnp.float32) + got.astype(jnp.float32)
    return held


def projection_kernel(block_ref, rows_ref, *refs):
    weight_refs, out_ref = refs[:-1], refs[-1]
    rows = rows_ref[...]
    for j, weight_ref in enumerate(weight_refs):
        out_ref[j] = jnp.dot(rows, weight_ref[...], preferred_element_type=jnp.float32).astype(out_ref.dtype)


def project_blocks(rows, weight, blocks):
    row_total, inner = rows.shape
    width = weight.shape[1] // lax.axis_size("tensor")
    count = blocks.shape[0]
    return pl.pallas_call(
        projection_kernel,
        out_shape=jax.ShapeDtypeStruct((count, row_total, width), jnp.bfloat16),
        grid_spec=pltpu.PrefetchScalarGridSpec(
            num_scalar_prefetch=1,
            grid=(1,),
            in_specs=[pl.BlockSpec((row_total, inner), lambda s, blk: (0, 0))]
            + [pl.BlockSpec((inner, width), lambda s, blk, j=j: (0, blk[j])) for j in range(count)],
            out_specs=pl.BlockSpec((count, row_total, width), lambda s, blk: (0, 0, 0)),
        ),
        cost_estimate=pl.CostEstimate(
            flops=2 * count * row_total * inner * width,
            transcendentals=0,
            bytes_accessed=int(rows.size * 2 + count * (inner * width + row_total * width) * 2),
        ),
    )(blocks, rows, *([weight] * count))


def bit_reversed(value, bits):
    out = 0
    for b in range(bits):
        out |= ((value >> b) & 1) << (bits - 1 - b)
    return out


def project_and_scatter(rows, weight, axis):
    count = lax.axis_size(axis)
    stages = count.bit_length() - 1
    if (1 << stages) != count or (weight.shape[1] // count) % 128:
        products = jnp.dot(rows, weight, preferred_element_type=jnp.float32).astype(jnp.bfloat16)
        return scatter_sum(products, axis)
    me = lax.axis_index(axis)
    order = jnp.array([bit_reversed(j, stages) for j in range(count)], jnp.int32)
    blocks = jnp.bitwise_xor(me, order)
    half = count // 2
    sent = project_blocks(rows, weight, blocks[half:])
    kept = project_blocks(rows, weight, blocks[:half])
    got = lax.ppermute(sent, axis, perm=[(i, i ^ 1) for i in range(count)])
    held = kept.astype(jnp.float32) + got.astype(jnp.float32)
    for s in range(1, stages):
        half = held.shape[0] // 2
        got = lax.ppermute(
            held[half:].astype(jnp.bfloat16), axis, perm=[(i, i ^ (1 << s)) for i in range(count)]
        )
        held = held[:half] + got.astype(jnp.float32)
    return held[0]


def butterfly_sum(values, axis):
    count, stages = halving_stages(axis)
    if stages is None:
        return lax.psum(values, axis)
    shape = values.shape
    lanes = 128 if values.size % 128 == 0 else values.size
    values = values.reshape(values.size // lanes, lanes)
    for s in range(stages):
        values = values + lax.ppermute(values, axis, perm=[(i, i ^ (1 << s)) for i in range(count)])
    return values.reshape(shape)


def exchange_by_shift(lanes, axis, cap, direction):
    count = lax.axis_size(axis)
    parts = [lanes[:cap]]
    for shift in range(1, count):
        parts.append(
            lax.ppermute(
                lanes[shift * cap:(shift + 1) * cap],
                axis,
                perm=[(i, (i + direction * shift) % count) for i in range(count)],
            )
        )
    return jnp.concatenate(parts, axis=0)


def shards(kv_cache, lengths, source, queries, fresh_kv, out_weight, norm_gain):
    dp_count = lax.axis_size("dp")
    me = lax.axis_index("dp")
    slot_count, row_count, query_width = queries.shape
    kv_width = fresh_kv.shape[2]
    pair_cap = max(1, slot_count // dp_count)
    lane_count = dp_count * pair_cap
    slot_ids = jnp.arange(slot_count, dtype=jnp.int32)
    lane_ids = jnp.arange(lane_count, dtype=jnp.int32)

    old_home = source // slot_count
    old_slot = source % slot_count
    earlier = slot_ids[None, :] < slot_ids[:, None]
    same_home = old_home[:, None] == old_home[None, :]
    rank = jnp.sum(same_home & earlier, axis=1)
    shift = (old_home - me) % dp_count
    out_lane = shift * pair_cap + rank
    tag = jnp.broadcast_to(
        (old_slot + 1).astype(jnp.bfloat16)[:, None, None], (slot_count, row_count, TAG_WIDTH)
    )
    payload = jnp.concatenate([queries, tag], axis=2)
    sending = pack_lanes(payload, out_lane, lane_count)
    arrived = exchange_by_shift(sending, "dp", pair_cap, 1)
    fresh_mix, fresh_sum = attend_fresh(queries, fresh_kv)

    lane_slot = arrived[:, 0, query_width].astype(jnp.int32) - 1
    hits = lane_slot[None, :] == slot_ids[:, None]
    slot_lane = jnp.clip(jnp.sum(jnp.where(hits, lane_ids[None, :], 0), axis=1), 0, lane_count - 1)
    back = attend_cache(arrived, kv_cache, lengths, slot_lane, query_width)
    returned = exchange_by_shift(back, "dp", pair_cap, -1)
    cache_here = jnp.take(returned, out_lane, axis=0)

    heads = query_width // HEAD
    sums = cache_here[:, :, query_width:].astype(jnp.float32)
    cache_sum = sums[:, :, :heads] + sums[:, :, TAG_WIDTH // 2:TAG_WIDTH // 2 + heads]
    total = cache_sum + fresh_sum[:, :, :heads]
    cache_mix = cache_here[:, :, :query_width].astype(jnp.float32).reshape(slot_count, row_count, heads, HEAD)
    joined = cache_mix * cache_sum[..., None] + fresh_mix.reshape(slot_count, row_count, heads, HEAD)
    attended_here = (joined / total[..., None]).astype(jnp.bfloat16).reshape(slot_count, row_count, query_width)

    row_total = slot_count * row_count
    flat_rows = attended_here.reshape(row_total, query_width)
    model_width = out_weight.shape[1]
    own_part = project_and_scatter(flat_rows, out_weight, "tensor")
    square_sum = jnp.sum(own_part * own_part, axis=-1)
    square_sum = butterfly_sum(square_sum, "tensor").reshape(row_total, 1)
    mean_square = square_sum / model_width
    normed = own_part * lax.rsqrt(mean_square + norm_eps) * norm_gain
    return normed.astype(jnp.bfloat16).reshape(slot_count, row_count, own_part.shape[1])


def solution(mesh):
    placed = (
        P(("groups", "dp"), None, "tensor"),
        P(("groups", "dp")),
        P(("groups", "dp")),
        P(("groups", "dp"), None, "tensor"),
        P(("groups", "dp"), None, "tensor"),
        P("tensor", None),
        P("tensor"),
    )
    return jax.shard_map(
        shards,
        mesh=mesh,
        in_specs=placed,
        out_specs=P(("groups", "dp"), None, "tensor"),
        check_vma=False,
    )
```

```python
import functools

import jax
import jax.numpy as jnp
from jax import lax
from jax.experimental import pallas as pl
from jax.experimental.pallas import tpu as pltpu
from jax.sharding import PartitionSpec as P

HEAD = 128
QHEADS = 16
KVHEADS = 8
TAG_WIDTH = 128


score_scale = 144.0 ** (-0.5)
soft_cap = 50.0
norm_eps = 1e-06


def attention_kernel(lane_ref, length_ref, pay_ref, cache_ref, *out_refs, q_width, cap):
    step = pl.program_id(0)
    sessions, cache_length, _ = cache_ref.shape
    row_count = pay_ref.shape[1]
    kv_heads = cache_ref.shape[2] // (2 * HEAD)
    group_size = QHEADS // KVHEADS
    out_dtype = out_refs[0].dtype
    lanes = [lane_ref[step * sessions + i] for i in range(sessions)]
    queries = jnp.stack([pay_ref[lane] for lane in lanes])
    lengths = length_ref[...]
    cache_pos = lax.broadcasted_iota(jnp.int32, (sessions, group_size * row_count, cache_length), 2)
    cache_seen = cache_pos < lengths
    lane_ids = lax.broadcasted_iota(jnp.int32, (sessions, row_count, TAG_WIDTH), 2)
    sums = jnp.zeros((sessions, row_count, TAG_WIDTH), jnp.float32)
    mixes = []
    for k in range(kv_heads):
        key_col = 2 * HEAD * k
        grouped = jnp.concatenate(
            [queries[:, :, (group_size * k + g) * HEAD:(group_size * k + g + 1) * HEAD] for g in range(group_size)],
            axis=1,
        )
        cache_keys = cache_ref[:, :, key_col:key_col + HEAD]
        cache_values = cache_ref[:, :, key_col + HEAD:key_col + 2 * HEAD]
        cache_scores = jnp.einsum("bqd,bkd->bqk", grouped, cache_keys, preferred_element_type=jnp.float32) * score_scale
        cache_w = jnp.where(cache_seen, jnp.exp(soft_cap * jnp.tanh(cache_scores / soft_cap)), 0.0)
        total = jnp.sum(cache_w, axis=-1, keepdims=True)
        mixed = jnp.einsum("bqk,bkd->bqd", cache_w.astype(jnp.bfloat16), cache_values, preferred_element_type=jnp.float32)
        mixed = (mixed / total).astype(out_dtype)
        high = total.astype(jnp.bfloat16).astype(jnp.float32)
        low = total - high
        for g in range(group_size):
            head = group_size * k + g
            mixes.append(mixed[:, g * row_count:(g + 1) * row_count])
            sums = jnp.where(lane_ids == head, high[:, g * row_count:(g + 1) * row_count], sums)
            sums = jnp.where(lane_ids == TAG_WIDTH // 2 + head, low[:, g * row_count:(g + 1) * row_count], sums)
    result = jnp.concatenate(mixes + [sums.astype(out_dtype)], axis=2)
    for i, lane in enumerate(lanes):
        for shift, out_ref in enumerate(out_refs):

            @pl.when(lane // cap == shift)
            def _():
                out_ref[lane % cap] = result[i]


def attend_cache(arrived, cached, lengths, slot_lane, q_width, cap, block=8):
    lane_count, row_count, pay_width = arrived.shape
    shifts = lane_count // cap
    slot_count, cache_length, kv_width = cached.shape
    block = min(block, slot_count)
    length_col = lengths.reshape(slot_count, 1, 1)
    return pl.pallas_call(
        functools.partial(attention_kernel, q_width=q_width, cap=cap),
        out_shape=[jax.ShapeDtypeStruct((cap, row_count, q_width + TAG_WIDTH), jnp.bfloat16)] * shifts,
        grid_spec=pltpu.PrefetchScalarGridSpec(
            num_scalar_prefetch=1,
            grid=(slot_count // block,),
            in_specs=[
                pl.BlockSpec((block, 1, 1), lambda b, lanes: (b, 0, 0)),
                pl.BlockSpec((lane_count, row_count, pay_width), lambda b, lanes: (0, 0, 0)),
                pl.BlockSpec((block, cache_length, kv_width), lambda b, lanes: (b, 0, 0)),
            ],
            out_specs=[pl.BlockSpec((cap, row_count, q_width + TAG_WIDTH), lambda b, lanes: (0, 0, 0))] * shifts,
        ),
        cost_estimate=pl.CostEstimate(
            flops=4 * slot_count * (q_width // HEAD) * row_count * cache_length * HEAD,
            transcendentals=2 * slot_count * (q_width // HEAD) * row_count * cache_length,
            bytes_accessed=int(cached.size * 2 + arrived.size * 2 + lane_count * row_count * (q_width + TAG_WIDTH) * 2),
        ),
    )(slot_lane, length_col, arrived, cached)


def fresh_kernel(q_ref, fresh_ref, mix_ref, sum_ref):
    sessions, row_count, _ = q_ref.shape
    kv_heads = fresh_ref.shape[2] // (2 * HEAD)
    group_size = QHEADS // KVHEADS
    fresh_pos = lax.broadcasted_iota(jnp.int32, (sessions, group_size * row_count, row_count), 2)
    query_row = lax.broadcasted_iota(jnp.int32, (sessions, group_size * row_count, row_count), 1) % row_count
    fresh_seen = fresh_pos <= query_row
    lane = lax.broadcasted_iota(jnp.int32, (sessions, row_count, TAG_WIDTH), 2)
    sums = jnp.zeros((sessions, row_count, TAG_WIDTH), jnp.float32)
    for k in range(kv_heads):
        key_col = 2 * HEAD * k
        grouped = jnp.concatenate(
            [q_ref[:, :, (group_size * k + g) * HEAD:(group_size * k + g + 1) * HEAD] for g in range(group_size)],
            axis=1,
        )
        fresh_keys = fresh_ref[:, :, key_col:key_col + HEAD]
        fresh_values = fresh_ref[:, :, key_col + HEAD:key_col + 2 * HEAD]
        fresh_scores = jnp.einsum("bqd,bkd->bqk", grouped, fresh_keys, preferred_element_type=jnp.float32) * score_scale
        fresh_w = jnp.where(fresh_seen, jnp.exp(soft_cap * jnp.tanh(fresh_scores / soft_cap)), 0.0)
        total = jnp.sum(fresh_w, axis=-1, keepdims=True)
        mixed = jnp.einsum("bqk,bkd->bqd", fresh_w.astype(jnp.bfloat16), fresh_values, preferred_element_type=jnp.float32)
        for g in range(group_size):
            head = group_size * k + g
            col = head * HEAD
            mix_ref[:, :, col:col + HEAD] = mixed[:, g * row_count:(g + 1) * row_count]
            sums = jnp.where(lane == head, total[:, g * row_count:(g + 1) * row_count], sums)
    sum_ref[...] = sums


def attend_fresh(queries, fresh_kv, block=8):
    slot_count, row_count, q_width = queries.shape
    kv_width = fresh_kv.shape[2]
    block = min(block, slot_count)
    return pl.pallas_call(
        fresh_kernel,
        out_shape=(
            jax.ShapeDtypeStruct((slot_count, row_count, q_width), jnp.float32),
            jax.ShapeDtypeStruct((slot_count, row_count, TAG_WIDTH), jnp.float32),
        ),
        grid=(slot_count // block,),
        in_specs=[
            pl.BlockSpec((block, row_count, q_width), lambda b: (b, 0, 0)),
            pl.BlockSpec((block, row_count, kv_width), lambda b: (b, 0, 0)),
        ],
        out_specs=(
            pl.BlockSpec((block, row_count, q_width), lambda b: (b, 0, 0)),
            pl.BlockSpec((block, row_count, TAG_WIDTH), lambda b: (b, 0, 0)),
        ),
        cost_estimate=pl.CostEstimate(
            flops=4 * slot_count * (q_width // HEAD) * row_count * row_count * HEAD,
            transcendentals=2 * slot_count * (q_width // HEAD) * row_count * row_count,
            bytes_accessed=int((queries.size + fresh_kv.size) * 2 + slot_count * row_count * (q_width + TAG_WIDTH) * 4),
        ),
    )(queries, fresh_kv)


def pack_lanes(payload, slot_lanes, lane_count):
    lane_ids = jnp.arange(lane_count, dtype=jnp.int32)
    slot_ids = jnp.arange(payload.shape[0], dtype=jnp.int32)
    lane_hits = slot_lanes[None, :] == lane_ids[:, None]
    filled = jnp.any(lane_hits, axis=1)
    chosen = jnp.sum(jnp.where(lane_hits, slot_ids[None, :], 0), axis=1)
    picked = jnp.take(payload, chosen, axis=0)
    return jnp.where(filled[:, None, None], picked, jnp.zeros((), payload.dtype))


def halving_stages(axis):
    count = lax.axis_size(axis)
    stages = count.bit_length() - 1
    return count, stages if (1 << stages) == count else None


def scatter_sum(partial, axis):
    count, stages = halving_stages(axis)
    rows, width = partial.shape
    if stages is None:
        return lax.psum_scatter(partial, axis, scatter_dimension=1, tiled=True).astype(jnp.float32)
    me = lax.axis_index(axis)
    held = partial.reshape((rows,) + (2,) * stages + (width // count,))
    for s in range(stages):
        bit = (me >> s) & 1
        dim = stages - s
        keep = lax.dynamic_index_in_dim(held, bit, axis=dim, keepdims=False)
        send = lax.dynamic_index_in_dim(held, 1 - bit, axis=dim, keepdims=False)
        got = lax.ppermute(
            send.astype(jnp.bfloat16), axis, perm=[(i, i ^ (1 << s)) for i in range(count)]
        )
        held = keep.astype(jnp.float32) + got.astype(jnp.float32)
    return held


def projection_kernel(block_ref, rows_ref, weight_ref, out_ref):
    out_ref[0] = jnp.dot(rows_ref[...], weight_ref[...], preferred_element_type=jnp.float32).astype(out_ref.dtype)


def project_blocks(rows, weight, blocks):
    row_total, inner = rows.shape
    width = weight.shape[1] // lax.axis_size("tensor")
    count = blocks.shape[0]
    return pl.pallas_call(
        projection_kernel,
        out_shape=jax.ShapeDtypeStruct((count, row_total, width), jnp.bfloat16),
        grid_spec=pltpu.PrefetchScalarGridSpec(
            num_scalar_prefetch=1,
            grid=(count,),
            in_specs=[
                pl.BlockSpec((row_total, inner), lambda j, blk: (0, 0)),
                pl.BlockSpec((inner, width), lambda j, blk: (0, blk[j])),
            ],
            out_specs=pl.BlockSpec((1, row_total, width), lambda j, blk: (j, 0, 0)),
        ),
        cost_estimate=pl.CostEstimate(
            flops=2 * count * row_total * inner * width,
            transcendentals=0,
            bytes_accessed=int(rows.size * 2 + count * (inner * width + row_total * width) * 2),
        ),
    )(blocks, rows, weight)


def bit_reversed(value, bits):
    out = 0
    for b in range(bits):
        out |= ((value >> b) & 1) << (bits - 1 - b)
    return out


def project_and_scatter(rows, weight, axis):
    count = lax.axis_size(axis)
    stages = count.bit_length() - 1
    if (1 << stages) != count or (weight.shape[1] // count) % 128:
        products = jnp.dot(rows, weight, preferred_element_type=jnp.float32).astype(jnp.bfloat16)
        return scatter_sum(products, axis)
    me = lax.axis_index(axis)
    order = jnp.array([bit_reversed(j, stages) for j in range(count)], jnp.int32)
    blocks = jnp.bitwise_xor(me, order)
    half = count // 2
    sent = project_blocks(rows, weight, blocks[half:])
    kept = project_blocks(rows, weight, blocks[:half])
    got = lax.ppermute(sent, axis, perm=[(i, i ^ 1) for i in range(count)])
    held = kept.astype(jnp.float32) + got.astype(jnp.float32)
    for s in range(1, stages):
        half = held.shape[0] // 2
        got = lax.ppermute(
            held[half:].astype(jnp.bfloat16), axis, perm=[(i, i ^ (1 << s)) for i in range(count)]
        )
        held = held[:half] + got.astype(jnp.float32)
    return held[0]


def butterfly_sum(values, axis):
    count, stages = halving_stages(axis)
    if stages is None:
        return lax.psum(values, axis)
    shape = values.shape
    lanes = 128 if values.size % 128 == 0 else values.size
    values = values.reshape(values.size // lanes, lanes)
    for s in range(stages):
        values = values + lax.ppermute(values, axis, perm=[(i, i ^ (1 << s)) for i in range(count)])
    return values.reshape(shape)


def exchange_by_shift(lanes, axis, cap, direction):
    count = lax.axis_size(axis)
    parts = [lanes[:cap]]
    for shift in range(1, count):
        parts.append(
            lax.ppermute(
                lanes[shift * cap:(shift + 1) * cap],
                axis,
                perm=[(i, (i + direction * shift) % count) for i in range(count)],
            )
        )
    return jnp.concatenate(parts, axis=0)


def exchange_parts(parts, axis, direction):
    count = lax.axis_size(axis)
    got = [parts[0]]
    for shift in range(1, count):
        got.append(lax.ppermute(parts[shift], axis, perm=[(i, (i + direction * shift) % count) for i in range(count)]))
    return jnp.concatenate(got, axis=0)


def shards(kv_cache, lengths, source, queries, fresh_kv, out_weight, norm_gain):
    dp_count = lax.axis_size("dp")
    me = lax.axis_index("dp")
    slot_count, row_count, query_width = queries.shape
    kv_width = fresh_kv.shape[2]
    pair_cap = max(1, slot_count // dp_count)
    lane_count = dp_count * pair_cap
    slot_ids = jnp.arange(slot_count, dtype=jnp.int32)
    lane_ids = jnp.arange(lane_count, dtype=jnp.int32)

    old_home = source // slot_count
    old_slot = source % slot_count
    earlier = slot_ids[None, :] < slot_ids[:, None]
    same_home = old_home[:, None] == old_home[None, :]
    rank = jnp.sum(same_home & earlier, axis=1)
    shift = (old_home - me) % dp_count
    out_lane = shift * pair_cap + rank
    tag = jnp.broadcast_to(
        (old_slot + 1).astype(jnp.bfloat16)[:, None, None], (slot_count, row_count, TAG_WIDTH)
    )
    payload = jnp.concatenate([queries, tag], axis=2)
    sending = pack_lanes(payload, out_lane, lane_count)
    arrived = exchange_by_shift(sending, "dp", pair_cap, 1)
    fresh_mix, fresh_sum = attend_fresh(queries, fresh_kv)

    lane_slot = arrived[:, 0, query_width].astype(jnp.int32) - 1
    hits = lane_slot[None, :] == slot_ids[:, None]
    slot_lane = jnp.clip(jnp.sum(jnp.where(hits, lane_ids[None, :], 0), axis=1), 0, lane_count - 1)
    back = attend_cache(arrived, kv_cache, lengths, slot_lane, query_width, pair_cap)
    returned = exchange_parts(back, "dp", -1)
    cache_here = jnp.take(returned, out_lane, axis=0)

    heads = query_width // HEAD
    sums = cache_here[:, :, query_width:].astype(jnp.float32)
    cache_sum = sums[:, :, :heads] + sums[:, :, TAG_WIDTH // 2:TAG_WIDTH // 2 + heads]
    total = cache_sum + fresh_sum[:, :, :heads]
    cache_mix = cache_here[:, :, :query_width].astype(jnp.float32).reshape(slot_count, row_count, heads, HEAD)
    joined = cache_mix * cache_sum[..., None] + fresh_mix.reshape(slot_count, row_count, heads, HEAD)
    attended_here = (joined / total[..., None]).astype(jnp.bfloat16).reshape(slot_count, row_count, query_width)

    row_total = slot_count * row_count
    flat_rows = attended_here.reshape(row_total, query_width)
    model_width = out_weight.shape[1]
    own_part = project_and_scatter(flat_rows, out_weight, "tensor")
    square_sum = jnp.sum(own_part * own_part, axis=-1)
    square_sum = butterfly_sum(square_sum, "tensor").reshape(row_total, 1)
    mean_square = square_sum / model_width
    normed = own_part * lax.rsqrt(mean_square + norm_eps) * norm_gain
    return normed.astype(jnp.bfloat16).reshape(slot_count, row_count, own_part.shape[1])


def solution(mesh):
    placed = (
        P(("groups", "dp"), None, "tensor"),
        P(("groups", "dp")),
        P(("groups", "dp")),
        P(("groups", "dp"), None, "tensor"),
        P(("groups", "dp"), None, "tensor"),
        P("tensor", None),
        P("tensor"),
    )
    return jax.shard_map(
        shards,
        mesh=mesh,
        in_specs=placed,
        out_specs=P(("groups", "dp"), None, "tensor"),
        check_vma=False,
    )
```

```python
import functools

import jax
import jax.numpy as jnp
from jax import lax
from jax.experimental import pallas as pl
from jax.experimental.pallas import tpu as pltpu
from jax.sharding import PartitionSpec as P

HEAD = 128
QHEADS = 16
KVHEADS = 8
TAG_WIDTH = 128


score_scale = 144.0 ** (-0.5)
soft_cap = 50.0
norm_eps = 1e-06


def attention_kernel(lane_ref, length_ref, pay_ref, cache_ref, out_ref, *, q_width):
    step = pl.program_id(0)
    sessions, cache_length, _ = cache_ref.shape
    row_count = pay_ref.shape[1]
    kv_heads = cache_ref.shape[2] // (2 * HEAD)
    group_size = QHEADS // KVHEADS
    lanes = [lane_ref[step * sessions + i] for i in range(sessions)]
    queries = jnp.stack([pay_ref[lane] for lane in lanes])
    lengths = length_ref[...]
    cache_pos = lax.broadcasted_iota(jnp.int32, (sessions, group_size * row_count, cache_length), 2)
    cache_seen = cache_pos < lengths
    lane_ids = lax.broadcasted_iota(jnp.int32, (sessions, row_count, TAG_WIDTH), 2)
    sums = jnp.zeros((sessions, row_count, TAG_WIDTH), jnp.float32)
    mixes = []
    for k in range(kv_heads):
        key_col = 2 * HEAD * k
        grouped = jnp.concatenate(
            [queries[:, :, (group_size * k + g) * HEAD:(group_size * k + g + 1) * HEAD] for g in range(group_size)],
            axis=1,
        )
        cache_keys = cache_ref[:, :, key_col:key_col + HEAD]
        cache_values = cache_ref[:, :, key_col + HEAD:key_col + 2 * HEAD]
        cache_scores = jnp.einsum("bqd,bkd->bqk", grouped, cache_keys, preferred_element_type=jnp.float32) * score_scale
        cache_w = jnp.where(cache_seen, jnp.exp(soft_cap * jnp.tanh(cache_scores / soft_cap)), 0.0)
        total = jnp.sum(cache_w, axis=-1, keepdims=True)
        mixed = jnp.einsum("bqk,bkd->bqd", cache_w.astype(jnp.bfloat16), cache_values, preferred_element_type=jnp.float32)
        mixed = (mixed / total).astype(out_ref.dtype)
        high = total.astype(jnp.bfloat16).astype(jnp.float32)
        low = total - high
        for g in range(group_size):
            head = group_size * k + g
            mixes.append(mixed[:, g * row_count:(g + 1) * row_count])
            sums = jnp.where(lane_ids == head, high[:, g * row_count:(g + 1) * row_count], sums)
            sums = jnp.where(lane_ids == TAG_WIDTH // 2 + head, low[:, g * row_count:(g + 1) * row_count], sums)
    result = jnp.concatenate(mixes + [sums.astype(out_ref.dtype)], axis=2)
    for i, lane in enumerate(lanes):
        out_ref[lane] = result[i]


def attend_cache(arrived, cached, lengths, slot_lane, q_width, block=16):
    lane_count, row_count, pay_width = arrived.shape
    slot_count, cache_length, kv_width = cached.shape
    block = min(block, slot_count)
    length_col = lengths.reshape(slot_count, 1, 1)
    return pl.pallas_call(
        functools.partial(attention_kernel, q_width=q_width),
        out_shape=jax.ShapeDtypeStruct((lane_count, row_count, q_width + TAG_WIDTH), jnp.bfloat16),
        grid_spec=pltpu.PrefetchScalarGridSpec(
            num_scalar_prefetch=1,
            grid=(slot_count // block,),
            in_specs=[
                pl.BlockSpec((block, 1, 1), lambda b, lanes: (b, 0, 0)),
                pl.BlockSpec((lane_count, row_count, pay_width), lambda b, lanes: (0, 0, 0)),
                pl.BlockSpec((block, cache_length, kv_width), lambda b, lanes: (b, 0, 0)),
            ],
            out_specs=pl.BlockSpec((lane_count, row_count, q_width + TAG_WIDTH), lambda b, lanes: (0, 0, 0)),
        ),
        cost_estimate=pl.CostEstimate(
            flops=4 * slot_count * (q_width // HEAD) * row_count * cache_length * HEAD,
            transcendentals=2 * slot_count * (q_width // HEAD) * row_count * cache_length,
            bytes_accessed=int(cached.size * 2 + arrived.size * 2 + lane_count * row_count * (q_width + TAG_WIDTH) * 2),
        ),
    )(slot_lane, length_col, arrived, cached)


def fresh_kernel(q_ref, fresh_ref, mix_ref, sum_ref):
    sessions, row_count, _ = q_ref.shape
    kv_heads = fresh_ref.shape[2] // (2 * HEAD)
    group_size = QHEADS // KVHEADS
    fresh_pos = lax.broadcasted_iota(jnp.int32, (sessions, group_size * row_count, row_count), 2)
    query_row = lax.broadcasted_iota(jnp.int32, (sessions, group_size * row_count, row_count), 1) % row_count
    fresh_seen = fresh_pos <= query_row
    lane = lax.broadcasted_iota(jnp.int32, (sessions, row_count, TAG_WIDTH), 2)
    sums = jnp.zeros((sessions, row_count, TAG_WIDTH), jnp.float32)
    for k in range(kv_heads):
        key_col = 2 * HEAD * k
        grouped = jnp.concatenate(
            [q_ref[:, :, (group_size * k + g) * HEAD:(group_size * k + g + 1) * HEAD] for g in range(group_size)],
            axis=1,
        )
        fresh_keys = fresh_ref[:, :, key_col:key_col + HEAD]
        fresh_values = fresh_ref[:, :, key_col + HEAD:key_col + 2 * HEAD]
        fresh_scores = jnp.einsum("bqd,bkd->bqk", grouped, fresh_keys, preferred_element_type=jnp.float32) * score_scale
        fresh_w = jnp.where(fresh_seen, jnp.exp(soft_cap * jnp.tanh(fresh_scores / soft_cap)), 0.0)
        total = jnp.sum(fresh_w, axis=-1, keepdims=True)
        mixed = jnp.einsum("bqk,bkd->bqd", fresh_w.astype(jnp.bfloat16), fresh_values, preferred_element_type=jnp.float32)
        for g in range(group_size):
            head = group_size * k + g
            col = head * HEAD
            mix_ref[:, :, col:col + HEAD] = mixed[:, g * row_count:(g + 1) * row_count]
            sums = jnp.where(lane == head, total[:, g * row_count:(g + 1) * row_count], sums)
    sum_ref[...] = sums


def attend_fresh(queries, fresh_kv, block=8):
    slot_count, row_count, q_width = queries.shape
    kv_width = fresh_kv.shape[2]
    block = min(block, slot_count)
    return pl.pallas_call(
        fresh_kernel,
        out_shape=(
            jax.ShapeDtypeStruct((slot_count, row_count, q_width), jnp.float32),
            jax.ShapeDtypeStruct((slot_count, row_count, TAG_WIDTH), jnp.float32),
        ),
        grid=(slot_count // block,),
        in_specs=[
            pl.BlockSpec((block, row_count, q_width), lambda b: (b, 0, 0)),
            pl.BlockSpec((block, row_count, kv_width), lambda b: (b, 0, 0)),
        ],
        out_specs=(
            pl.BlockSpec((block, row_count, q_width), lambda b: (b, 0, 0)),
            pl.BlockSpec((block, row_count, TAG_WIDTH), lambda b: (b, 0, 0)),
        ),
        cost_estimate=pl.CostEstimate(
            flops=4 * slot_count * (q_width // HEAD) * row_count * row_count * HEAD,
            transcendentals=2 * slot_count * (q_width // HEAD) * row_count * row_count,
            bytes_accessed=int((queries.size + fresh_kv.size) * 2 + slot_count * row_count * (q_width + TAG_WIDTH) * 4),
        ),
    )(queries, fresh_kv)


def pack_lanes(payload, slot_lanes, lane_count):
    lane_ids = jnp.arange(lane_count, dtype=jnp.int32)
    slot_ids = jnp.arange(payload.shape[0], dtype=jnp.int32)
    lane_hits = slot_lanes[None, :] == lane_ids[:, None]
    filled = jnp.any(lane_hits, axis=1)
    chosen = jnp.sum(jnp.where(lane_hits, slot_ids[None, :], 0), axis=1)
    picked = jnp.take(payload, chosen, axis=0)
    return jnp.where(filled[:, None, None], picked, jnp.zeros((), payload.dtype))


def halving_stages(axis):
    count = lax.axis_size(axis)
    stages = count.bit_length() - 1
    return count, stages if (1 << stages) == count else None


def scatter_sum(partial, axis):
    count, stages = halving_stages(axis)
    rows, width = partial.shape
    if stages is None:
        return lax.psum_scatter(partial, axis, scatter_dimension=1, tiled=True).astype(jnp.float32)
    me = lax.axis_index(axis)
    held = partial.reshape((rows,) + (2,) * stages + (width // count,))
    for s in range(stages):
        bit = (me >> s) & 1
        dim = stages - s
        keep = lax.dynamic_index_in_dim(held, bit, axis=dim, keepdims=False)
        send = lax.dynamic_index_in_dim(held, 1 - bit, axis=dim, keepdims=False)
        got = lax.ppermute(
            send.astype(jnp.bfloat16), axis, perm=[(i, i ^ (1 << s)) for i in range(count)]
        )
        held = keep.astype(jnp.float32) + got.astype(jnp.float32)
    return held


def projection_kernel(block_ref, rows_ref, weight_ref, out_ref):
    out_ref[0] = jnp.dot(rows_ref[...], weight_ref[...], preferred_element_type=jnp.float32).astype(out_ref.dtype)


def project_blocks(rows, weight, blocks):
    row_total, inner = rows.shape
    width = weight.shape[1] // lax.axis_size("tensor")
    count = blocks.shape[0]
    return pl.pallas_call(
        projection_kernel,
        out_shape=jax.ShapeDtypeStruct((count, row_total, width), jnp.bfloat16),
        grid_spec=pltpu.PrefetchScalarGridSpec(
            num_scalar_prefetch=1,
            grid=(count,),
            in_specs=[
                pl.BlockSpec((row_total, inner), lambda j, blk: (0, 0)),
                pl.BlockSpec((inner, width), lambda j, blk: (0, blk[j])),
            ],
            out_specs=pl.BlockSpec((1, row_total, width), lambda j, blk: (j, 0, 0)),
        ),
        cost_estimate=pl.CostEstimate(
            flops=2 * count * row_total * inner * width,
            transcendentals=0,
            bytes_accessed=int(rows.size * 2 + count * (inner * width + row_total * width) * 2),
        ),
    )(blocks, rows, weight)


def bit_reversed(value, bits):
    out = 0
    for b in range(bits):
        out |= ((value >> b) & 1) << (bits - 1 - b)
    return out


def project_and_scatter(rows, weight, axis):
    count = lax.axis_size(axis)
    stages = count.bit_length() - 1
    if (1 << stages) != count or (weight.shape[1] // count) % 128:
        products = jnp.dot(rows, weight, preferred_element_type=jnp.float32).astype(jnp.bfloat16)
        return scatter_sum(products, axis)
    me = lax.axis_index(axis)
    order = jnp.array([bit_reversed(j, stages) for j in range(count)], jnp.int32)
    blocks = jnp.bitwise_xor(me, order)
    half = count // 2
    sent = project_blocks(rows, weight, blocks[half:])
    kept = project_blocks(rows, weight, blocks[:half])
    got = lax.ppermute(sent, axis, perm=[(i, i ^ 1) for i in range(count)])
    held = kept.astype(jnp.float32) + got.astype(jnp.float32)
    for s in range(1, stages):
        half = held.shape[0] // 2
        got = lax.ppermute(
            held[half:].astype(jnp.bfloat16), axis, perm=[(i, i ^ (1 << s)) for i in range(count)]
        )
        held = held[:half] + got.astype(jnp.float32)
    return held[0]


def butterfly_sum(values, axis):
    count, stages = halving_stages(axis)
    if stages is None:
        return lax.psum(values, axis)
    shape = values.shape
    lanes = 128 if values.size % 128 == 0 else values.size
    values = values.reshape(values.size // lanes, lanes)
    for s in range(stages):
        values = values + lax.ppermute(values, axis, perm=[(i, i ^ (1 << s)) for i in range(count)])
    return values.reshape(shape)


def exchange_by_shift(lanes, axis, cap, direction):
    count = lax.axis_size(axis)
    parts = [lanes[:cap]]
    for shift in range(1, count):
        parts.append(
            lax.ppermute(
                lanes[shift * cap:(shift + 1) * cap],
                axis,
                perm=[(i, (i + direction * shift) % count) for i in range(count)],
            )
        )
    return jnp.concatenate(parts, axis=0)


def shards(kv_cache, lengths, source, queries, fresh_kv, out_weight, norm_gain):
    dp_count = lax.axis_size("dp")
    me = lax.axis_index("dp")
    slot_count, row_count, query_width = queries.shape
    kv_width = fresh_kv.shape[2]
    pair_cap = max(1, slot_count // dp_count)
    lane_count = dp_count * pair_cap
    slot_ids = jnp.arange(slot_count, dtype=jnp.int32)
    lane_ids = jnp.arange(lane_count, dtype=jnp.int32)

    old_home = source // slot_count
    old_slot = source % slot_count
    earlier = slot_ids[None, :] < slot_ids[:, None]
    same_home = old_home[:, None] == old_home[None, :]
    rank = jnp.sum(same_home & earlier, axis=1)
    shift = (old_home - me) % dp_count
    out_lane = shift * pair_cap + rank
    tag = jnp.broadcast_to(
        (old_slot + 1).astype(jnp.bfloat16)[:, None, None], (slot_count, row_count, TAG_WIDTH)
    )
    payload = jnp.concatenate([queries, tag], axis=2)
    sending = pack_lanes(payload, out_lane, lane_count)
    arrived = exchange_by_shift(sending, "dp", pair_cap, 1)
    fresh_mix, fresh_sum = attend_fresh(queries, fresh_kv)

    lane_slot = arrived[:, 0, query_width].astype(jnp.int32) - 1
    hits = lane_slot[None, :] == slot_ids[:, None]
    slot_lane = jnp.clip(jnp.sum(jnp.where(hits, lane_ids[None, :], 0), axis=1), 0, lane_count - 1)
    back = attend_cache(arrived, kv_cache, lengths, slot_lane, query_width)
    returned = exchange_by_shift(back, "dp", pair_cap, -1)
    cache_here = jnp.take(returned, out_lane, axis=0)

    heads = query_width // HEAD
    sums = cache_here[:, :, query_width:].astype(jnp.float32)
    cache_sum = sums[:, :, :heads] + sums[:, :, TAG_WIDTH // 2:TAG_WIDTH // 2 + heads]
    total = cache_sum + fresh_sum[:, :, :heads]
    cache_mix = cache_here[:, :, :query_width].astype(jnp.float32).reshape(slot_count, row_count, heads, HEAD)
    joined = cache_mix * cache_sum[..., None] + fresh_mix.reshape(slot_count, row_count, heads, HEAD)
    attended_here = (joined / total[..., None]).astype(jnp.bfloat16).reshape(slot_count, row_count, query_width)

    row_total = slot_count * row_count
    flat_rows = attended_here.reshape(row_total, query_width)
    model_width = out_weight.shape[1]
    own_part = project_and_scatter(flat_rows, out_weight, "tensor")
    square_sum = jnp.sum(own_part * own_part, axis=-1)
    square_sum = butterfly_sum(square_sum, "tensor").reshape(row_total, 1)
    mean_square = square_sum / model_width
    normed = own_part * lax.rsqrt(mean_square + norm_eps) * norm_gain
    return normed.astype(jnp.bfloat16).reshape(slot_count, row_count, own_part.shape[1])


def solution(mesh):
    placed = (
        P(("groups", "dp"), None, "tensor"),
        P(("groups", "dp")),
        P(("groups", "dp")),
        P(("groups", "dp"), None, "tensor"),
        P(("groups", "dp"), None, "tensor"),
        P("tensor", None),
        P("tensor"),
    )
    return jax.shard_map(
        shards,
        mesh=mesh,
        in_specs=placed,
        out_specs=P(("groups", "dp"), None, "tensor"),
        check_vma=False,
    )
```

```python
import functools

import jax
import jax.numpy as jnp
from jax import lax
from jax.experimental import pallas as pl
from jax.experimental.pallas import tpu as pltpu
from jax.sharding import PartitionSpec as P

HEAD = 128
QHEADS = 16
KVHEADS = 8
TAG_WIDTH = 128


score_scale = 144.0 ** (-0.5)
soft_cap = 50.0
norm_eps = 1e-06


def attention_kernel(lane_ref, length_ref, pay_ref, cache_ref, out_ref, *, q_width):
    step = pl.program_id(0)
    sessions, cache_length, _ = cache_ref.shape
    row_count = pay_ref.shape[1]
    kv_heads = cache_ref.shape[2] // (2 * HEAD)
    group_size = QHEADS // KVHEADS
    lanes = [lane_ref[step * sessions + i] for i in range(sessions)]
    queries = jnp.stack([pay_ref[lane] for lane in lanes])
    lengths = length_ref[...]
    cache_pos = lax.broadcasted_iota(jnp.int32, (sessions, group_size * row_count, cache_length), 2)
    cache_seen = cache_pos < lengths
    lane_ids = lax.broadcasted_iota(jnp.int32, (sessions, row_count, TAG_WIDTH), 2)
    sums = jnp.zeros((sessions, row_count, TAG_WIDTH), jnp.float32)
    mixes = []
    for k in range(kv_heads):
        key_col = 2 * HEAD * k
        grouped = jnp.concatenate(
            [queries[:, :, (group_size * k + g) * HEAD:(group_size * k + g + 1) * HEAD] for g in range(group_size)],
            axis=1,
        )
        cache_keys = cache_ref[:, :, key_col:key_col + HEAD]
        cache_values = cache_ref[:, :, key_col + HEAD:key_col + 2 * HEAD]
        cache_scores = jnp.einsum("bqd,bkd->bqk", grouped, cache_keys, preferred_element_type=jnp.float32) * score_scale
        cache_w = jnp.where(cache_seen, jnp.exp(soft_cap * jnp.tanh(cache_scores / soft_cap)), 0.0)
        total = jnp.sum(cache_w, axis=-1, keepdims=True)
        mixed = jnp.einsum("bqk,bkd->bqd", cache_w.astype(jnp.bfloat16), cache_values, preferred_element_type=jnp.float32)
        mixed = (mixed / total).astype(out_ref.dtype)
        high = total.astype(jnp.bfloat16).astype(jnp.float32)
        low = total - high
        for g in range(group_size):
            head = group_size * k + g
            mixes.append(mixed[:, g * row_count:(g + 1) * row_count])
            sums = jnp.where(lane_ids == head, high[:, g * row_count:(g + 1) * row_count], sums)
            sums = jnp.where(lane_ids == TAG_WIDTH // 2 + head, low[:, g * row_count:(g + 1) * row_count], sums)
    result = jnp.concatenate(mixes + [sums.astype(out_ref.dtype)], axis=2)
    for i, lane in enumerate(lanes):
        out_ref[lane] = result[i]


def attend_cache(arrived, cached, lengths, slot_lane, q_width, block=32):
    lane_count, row_count, pay_width = arrived.shape
    slot_count, cache_length, kv_width = cached.shape
    block = min(block, slot_count)
    length_col = lengths.reshape(slot_count, 1, 1)
    return pl.pallas_call(
        functools.partial(attention_kernel, q_width=q_width),
        out_shape=jax.ShapeDtypeStruct((lane_count, row_count, q_width + TAG_WIDTH), jnp.bfloat16),
        grid_spec=pltpu.PrefetchScalarGridSpec(
            num_scalar_prefetch=1,
            grid=(slot_count // block,),
            in_specs=[
                pl.BlockSpec((block, 1, 1), lambda b, lanes: (b, 0, 0)),
                pl.BlockSpec((lane_count, row_count, pay_width), lambda b, lanes: (0, 0, 0)),
                pl.BlockSpec((block, cache_length, kv_width), lambda b, lanes: (b, 0, 0)),
            ],
            out_specs=pl.BlockSpec((lane_count, row_count, q_width + TAG_WIDTH), lambda b, lanes: (0, 0, 0)),
        ),
        cost_estimate=pl.CostEstimate(
            flops=4 * slot_count * (q_width // HEAD) * row_count * cache_length * HEAD,
            transcendentals=2 * slot_count * (q_width // HEAD) * row_count * cache_length,
            bytes_accessed=int(cached.size * 2 + arrived.size * 2 + lane_count * row_count * (q_width + TAG_WIDTH) * 2),
        ),
    )(slot_lane, length_col, arrived, cached)


def fresh_kernel(q_ref, fresh_ref, mix_ref, sum_ref):
    sessions, row_count, _ = q_ref.shape
    kv_heads = fresh_ref.shape[2] // (2 * HEAD)
    group_size = QHEADS // KVHEADS
    fresh_pos = lax.broadcasted_iota(jnp.int32, (sessions, group_size * row_count, row_count), 2)
    query_row = lax.broadcasted_iota(jnp.int32, (sessions, group_size * row_count, row_count), 1) % row_count
    fresh_seen = fresh_pos <= query_row
    lane = lax.broadcasted_iota(jnp.int32, (sessions, row_count, TAG_WIDTH), 2)
    sums = jnp.zeros((sessions, row_count, TAG_WIDTH), jnp.float32)
    for k in range(kv_heads):
        key_col = 2 * HEAD * k
        grouped = jnp.concatenate(
            [q_ref[:, :, (group_size * k + g) * HEAD:(group_size * k + g + 1) * HEAD] for g in range(group_size)],
            axis=1,
        )
        fresh_keys = fresh_ref[:, :, key_col:key_col + HEAD]
        fresh_values = fresh_ref[:, :, key_col + HEAD:key_col + 2 * HEAD]
        fresh_scores = jnp.einsum("bqd,bkd->bqk", grouped, fresh_keys, preferred_element_type=jnp.float32) * score_scale
        fresh_w = jnp.where(fresh_seen, jnp.exp(soft_cap * jnp.tanh(fresh_scores / soft_cap)), 0.0)
        total = jnp.sum(fresh_w, axis=-1, keepdims=True)
        mixed = jnp.einsum("bqk,bkd->bqd", fresh_w.astype(jnp.bfloat16), fresh_values, preferred_element_type=jnp.float32)
        for g in range(group_size):
            head = group_size * k + g
            col = head * HEAD
            mix_ref[:, :, col:col + HEAD] = mixed[:, g * row_count:(g + 1) * row_count]
            sums = jnp.where(lane == head, total[:, g * row_count:(g + 1) * row_count], sums)
    sum_ref[...] = sums


def attend_fresh(queries, fresh_kv, block=8):
    slot_count, row_count, q_width = queries.shape
    kv_width = fresh_kv.shape[2]
    block = min(block, slot_count)
    return pl.pallas_call(
        fresh_kernel,
        out_shape=(
            jax.ShapeDtypeStruct((slot_count, row_count, q_width), jnp.float32),
            jax.ShapeDtypeStruct((slot_count, row_count, TAG_WIDTH), jnp.float32),
        ),
        grid=(slot_count // block,),
        in_specs=[
            pl.BlockSpec((block, row_count, q_width), lambda b: (b, 0, 0)),
            pl.BlockSpec((block, row_count, kv_width), lambda b: (b, 0, 0)),
        ],
        out_specs=(
            pl.BlockSpec((block, row_count, q_width), lambda b: (b, 0, 0)),
            pl.BlockSpec((block, row_count, TAG_WIDTH), lambda b: (b, 0, 0)),
        ),
        cost_estimate=pl.CostEstimate(
            flops=4 * slot_count * (q_width // HEAD) * row_count * row_count * HEAD,
            transcendentals=2 * slot_count * (q_width // HEAD) * row_count * row_count,
            bytes_accessed=int((queries.size + fresh_kv.size) * 2 + slot_count * row_count * (q_width + TAG_WIDTH) * 4),
        ),
    )(queries, fresh_kv)


def pack_lanes(payload, slot_lanes, lane_count):
    lane_ids = jnp.arange(lane_count, dtype=jnp.int32)
    slot_ids = jnp.arange(payload.shape[0], dtype=jnp.int32)
    lane_hits = slot_lanes[None, :] == lane_ids[:, None]
    filled = jnp.any(lane_hits, axis=1)
    chosen = jnp.sum(jnp.where(lane_hits, slot_ids[None, :], 0), axis=1)
    picked = jnp.take(payload, chosen, axis=0)
    return jnp.where(filled[:, None, None], picked, jnp.zeros((), payload.dtype))


def halving_stages(axis):
    count = lax.axis_size(axis)
    stages = count.bit_length() - 1
    return count, stages if (1 << stages) == count else None


def scatter_sum(partial, axis):
    count, stages = halving_stages(axis)
    rows, width = partial.shape
    if stages is None:
        return lax.psum_scatter(partial, axis, scatter_dimension=1, tiled=True).astype(jnp.float32)
    me = lax.axis_index(axis)
    held = partial.reshape((rows,) + (2,) * stages + (width // count,))
    for s in range(stages):
        bit = (me >> s) & 1
        dim = stages - s
        keep = lax.dynamic_index_in_dim(held, bit, axis=dim, keepdims=False)
        send = lax.dynamic_index_in_dim(held, 1 - bit, axis=dim, keepdims=False)
        got = lax.ppermute(
            send.astype(jnp.bfloat16), axis, perm=[(i, i ^ (1 << s)) for i in range(count)]
        )
        held = keep.astype(jnp.float32) + got.astype(jnp.float32)
    return held


def projection_kernel(block_ref, rows_ref, weight_ref, out_ref):
    out_ref[0] = jnp.dot(rows_ref[...], weight_ref[...], preferred_element_type=jnp.float32).astype(out_ref.dtype)


def project_blocks(rows, weight, blocks):
    row_total, inner = rows.shape
    width = weight.shape[1] // lax.axis_size("tensor")
    count = blocks.shape[0]
    return pl.pallas_call(
        projection_kernel,
        out_shape=jax.ShapeDtypeStruct((count, row_total, width), jnp.bfloat16),
        grid_spec=pltpu.PrefetchScalarGridSpec(
            num_scalar_prefetch=1,
            grid=(count,),
            in_specs=[
                pl.BlockSpec((row_total, inner), lambda j, blk: (0, 0)),
                pl.BlockSpec((inner, width), lambda j, blk: (0, blk[j])),
            ],
            out_specs=pl.BlockSpec((1, row_total, width), lambda j, blk: (j, 0, 0)),
        ),
        cost_estimate=pl.CostEstimate(
            flops=2 * count * row_total * inner * width,
            transcendentals=0,
            bytes_accessed=int(rows.size * 2 + count * (inner * width + row_total * width) * 2),
        ),
    )(blocks, rows, weight)


def bit_reversed(value, bits):
    out = 0
    for b in range(bits):
        out |= ((value >> b) & 1) << (bits - 1 - b)
    return out


def project_and_scatter(rows, weight, axis):
    count = lax.axis_size(axis)
    stages = count.bit_length() - 1
    if (1 << stages) != count or (weight.shape[1] // count) % 128:
        products = jnp.dot(rows, weight, preferred_element_type=jnp.float32).astype(jnp.bfloat16)
        return scatter_sum(products, axis)
    me = lax.axis_index(axis)
    order = jnp.array([bit_reversed(j, stages) for j in range(count)], jnp.int32)
    blocks = jnp.bitwise_xor(me, order)
    half = count // 2
    sent = project_blocks(rows, weight, blocks[half:])
    kept = project_blocks(rows, weight, blocks[:half])
    got = lax.ppermute(sent, axis, perm=[(i, i ^ 1) for i in range(count)])
    held = kept.astype(jnp.float32) + got.astype(jnp.float32)
    for s in range(1, stages):
        half = held.shape[0] // 2
        got = lax.ppermute(
            held[half:].astype(jnp.bfloat16), axis, perm=[(i, i ^ (1 << s)) for i in range(count)]
        )
        held = held[:half] + got.astype(jnp.float32)
    return held[0]


def butterfly_sum(values, axis):
    count, stages = halving_stages(axis)
    if stages is None:
        return lax.psum(values, axis)
    shape = values.shape
    lanes = 128 if values.size % 128 == 0 else values.size
    values = values.reshape(values.size // lanes, lanes)
    for s in range(stages):
        values = values + lax.ppermute(values, axis, perm=[(i, i ^ (1 << s)) for i in range(count)])
    return values.reshape(shape)


def exchange_by_shift(lanes, axis, cap, direction):
    count = lax.axis_size(axis)
    parts = [lanes[:cap]]
    for shift in range(1, count):
        parts.append(
            lax.ppermute(
                lanes[shift * cap:(shift + 1) * cap],
                axis,
                perm=[(i, (i + direction * shift) % count) for i in range(count)],
            )
        )
    return jnp.concatenate(parts, axis=0)


def shards(kv_cache, lengths, source, queries, fresh_kv, out_weight, norm_gain):
    dp_count = lax.axis_size("dp")
    me = lax.axis_index("dp")
    slot_count, row_count, query_width = queries.shape
    kv_width = fresh_kv.shape[2]
    pair_cap = max(1, slot_count // dp_count)
    lane_count = dp_count * pair_cap
    slot_ids = jnp.arange(slot_count, dtype=jnp.int32)
    lane_ids = jnp.arange(lane_count, dtype=jnp.int32)

    old_home = source // slot_count
    old_slot = source % slot_count
    earlier = slot_ids[None, :] < slot_ids[:, None]
    same_home = old_home[:, None] == old_home[None, :]
    rank = jnp.sum(same_home & earlier, axis=1)
    shift = (old_home - me) % dp_count
    out_lane = shift * pair_cap + rank
    tag = jnp.broadcast_to(
        (old_slot + 1).astype(jnp.bfloat16)[:, None, None], (slot_count, row_count, TAG_WIDTH)
    )
    payload = jnp.concatenate([queries, tag], axis=2)
    sending = pack_lanes(payload, out_lane, lane_count)
    arrived = exchange_by_shift(sending, "dp", pair_cap, 1)
    fresh_mix, fresh_sum = attend_fresh(queries, fresh_kv)

    lane_slot = arrived[:, 0, query_width].astype(jnp.int32) - 1
    hits = lane_slot[None, :] == slot_ids[:, None]
    slot_lane = jnp.clip(jnp.sum(jnp.where(hits, lane_ids[None, :], 0), axis=1), 0, lane_count - 1)
    back = attend_cache(arrived, kv_cache, lengths, slot_lane, query_width)
    returned = exchange_by_shift(back, "dp", pair_cap, -1)
    cache_here = jnp.take(returned, out_lane, axis=0)

    heads = query_width // HEAD
    sums = cache_here[:, :, query_width:].astype(jnp.float32)
    cache_sum = sums[:, :, :heads] + sums[:, :, TAG_WIDTH // 2:TAG_WIDTH // 2 + heads]
    total = cache_sum + fresh_sum[:, :, :heads]
    cache_mix = cache_here[:, :, :query_width].astype(jnp.float32).reshape(slot_count, row_count, heads, HEAD)
    joined = cache_mix * cache_sum[..., None] + fresh_mix.reshape(slot_count, row_count, heads, HEAD)
    attended_here = (joined / total[..., None]).astype(jnp.bfloat16).reshape(slot_count, row_count, query_width)

    row_total = slot_count * row_count
    flat_rows = attended_here.reshape(row_total, query_width)
    model_width = out_weight.shape[1]
    own_part = project_and_scatter(flat_rows, out_weight, "tensor")
    square_sum = jnp.sum(own_part * own_part, axis=-1)
    square_sum = butterfly_sum(square_sum, "tensor").reshape(row_total, 1)
    mean_square = square_sum / model_width
    normed = own_part * lax.rsqrt(mean_square + norm_eps) * norm_gain
    return normed.astype(jnp.bfloat16).reshape(slot_count, row_count, own_part.shape[1])


def solution(mesh):
    placed = (
        P(("groups", "dp"), None, "tensor"),
        P(("groups", "dp")),
        P(("groups", "dp")),
        P(("groups", "dp"), None, "tensor"),
        P(("groups", "dp"), None, "tensor"),
        P("tensor", None),
        P("tensor"),
    )
    return jax.shard_map(
        shards,
        mesh=mesh,
        in_specs=placed,
        out_specs=P(("groups", "dp"), None, "tensor"),
        check_vma=False,
    )
```
